128 devices in a mesh: pitch: 8 (over x_lo, y), span: 16 (over z, x_hi, core).
Axes of the slice: x: 4 (x_hi: 2, x_lo: 2; x = x_hi * 2 + x_lo), y: 4, z: 4, core: 2. Of those that a mesh axis runs over, the one named last changes fastest.
Arguments:
- flow_state: float32 [4, 256, 1024, 128], P(None, 'span', 'pitch'), may hold values from -0.36 to 3.4, as said below
- node_offset: float32 [2, 256, 1024, 128], P(None, 'span', 'pitch'), may hold values from -0.1 to 0.1
- blade_mode: float32 [2, 256, 128], P(None, 'span'), may hold values from -0.2 to 0.2
- phase_angles: float32 [2], replicated, may hold values from -3.140625 to 3.140625
- lag_series: float32 [2, 3, 2, 4, 256, 128], P(None, None, None, None, 'span'), may hold values from -0.3 to 0.3, as said below
Outputs:
- new_state: float32 [4, 256, 1024, 128], P(None, 'span', 'pitch')
- moved_offset: float32 [2, 256, 1024, 128], P(None, 'span', 'pitch')
The draws below stay inside these ranges and needn't reach their ends.
Inputs may be any that keep to these rules, and one draw needn't show every extreme that they name: `flow_state`: built from density in 0.8 to 1.2, velocity components within 0.3 and pressure in 0.7 to 1.3. `lag_series`: entries for density lie within 0.01.
All inputs are finite; a program needn't handle non-finite values.
Results may differ from the reference program's by a relative error of at most 0.00002.
Values sent between devices are 32-bit elements; how exact they have to be, the bound alone decides.
No kernel may reach another device: no remote copies, remote signals or barrier semaphores. Data moves between devices by JAX's collectives and lax.ppermute only.
A program may use at most 192 MiB of HBM per device.

```python
import jax
import jax.numpy as jnp
from jax import lax

R = 128
HARM = 3
NA = 256
NP = 1024


def draw_flow_state(key, part):
    key_list = jax.random.split(key, 4)
    grid_shape = (NA, NP, R)
    first_draw = jax.random.uniform(key_list[0], grid_shape, jnp.float32, -1.0, 1.0)
    second_draw = jax.random.uniform(key_list[1], grid_shape, jnp.float32, -1.0, 1.0)
    third_draw = jax.random.uniform(key_list[2], grid_shape, jnp.float32, -1.0, 1.0)
    fourth_draw = jax.random.uniform(key_list[3], grid_shape, jnp.float32, -1.0, 1.0)
    density = 1.0 + 0.2 * first_draw
    vel_x = 0.3 * second_draw
    vel_y = 0.3 * third_draw
    pressure = 1.0 + 0.3 * fourth_draw
    energy = pressure / 0.4 + 0.5 * density * (vel_x * vel_x + vel_y * vel_y)
    return jnp.stack([density, density * vel_x, density * vel_y, energy])


def draw_lag_series(key, part):
    values = jax.random.uniform(key, (2, HARM, 2, 4, NA, R), jnp.float32, -1.0, 1.0)
    var_scale = jnp.array([0.01, 0.3, 0.3, 0.3], jnp.float32)
    return values * var_scale[None, None, None, :, None, None]


def level_of(key, extent, cuts, low, top_value):
    def one(position, parts):
        heights = jax.random.uniform(jax.random.fold_in(jax.random.fold_in(key, 6), position), (parts,), jnp.float32, low / len(cuts), top_value / len(cuts))
        return jnp.repeat(jnp.exp(heights), extent[position] // parts).reshape((-1,) + (1,) * (len(extent) - position - 1))

    gain = one(*cuts[0])
    for cut in cuts[1:]:
        gain = gain * one(*cut)
    return gain


def setup_inputs(seed: int = 0) -> dict:
    key_of = jax.random.split(jax.random.key(seed), 6)
    return {
        "flow_state": draw_flow_state(jax.random.fold_in(key_of[5], 71), 0),
        "node_offset": jnp.clip(jax.random.uniform(key_of[1], (2, NA, NP, R), jnp.float32, -0.1, 0.1) * level_of(key_of[1], (2, NA, NP, R), ((1, 16), (2, 8)), -0.4, 0.0), -0.1, 0.1),
        "blade_mode": jnp.clip(jax.random.uniform(key_of[2], (2, NA, R), jnp.float32, -0.2, 0.2) * level_of(key_of[2], (2, NA, R), ((1, 16),), -0.4, 0.0), -0.2, 0.2),
        "phase_angles": jnp.clip(jax.random.uniform(key_of[3], (2,), jnp.float32, -3.140625, 3.140625), -3.140625, 3.140625),
        "lag_series": draw_lag_series(jax.random.fold_in(key_of[5], 71), 0),
    }


HEAT_RATIO = 1.4
TIME_STEP = 0.25
DAMPING = 0.02
SECTION_WEIGHTS = (0.5, 1.0)

def extend_linear(values, axis_pos):
    length = values.shape[axis_pos]
    first_row = lax.slice_in_dim(values, 0, 1, axis=axis_pos)
    second_row = lax.slice_in_dim(values, 1, 2, axis=axis_pos)
    last_row = lax.slice_in_dim(values, length - 1, length, axis=axis_pos)
    before_row = lax.slice_in_dim(values, length - 2, length - 1, axis=axis_pos)
    step_low = first_row - second_row
    step_high = last_row - before_row
    return jnp.concatenate([first_row + 2.0 * step_low, first_row + step_low, values, last_row + step_high, last_row + 2.0 * step_high], axis=axis_pos)

def radial_damping(values, axis_pos):
    count = values.shape[axis_pos]
    first_row = lax.slice_in_dim(values, 0, 1, axis=axis_pos)
    last_row = lax.slice_in_dim(values, count - 1, count, axis=axis_pos)
    extended = jnp.concatenate([first_row, first_row, values, last_row, last_row], axis=axis_pos)
    return lax.slice_in_dim(extended, 4, 4 + count, axis=axis_pos) - 4.0 * lax.slice_in_dim(extended, 3, 3 + count, axis=axis_pos) + 6.0 * values - 4.0 * lax.slice_in_dim(extended, 1, 1 + count, axis=axis_pos) + lax.slice_in_dim(extended, 0, count, axis=axis_pos)

def unit_normal(earlier, later):
    along_x = later[0] - earlier[0]
    along_y = 1.0 + later[1] - earlier[1]
    length = jnp.sqrt(along_x * along_x + along_y * along_y)
    return jnp.stack([along_x / length, along_y / length])

def wall_amplitude(shape_mode, angle, blade_mask):
    return (shape_mode[0] * jnp.cos(angle) - shape_mode[1] * jnp.sin(angle)) * blade_mask

def lag_shift(series, phase_now, phase_move):
    series_sum = jnp.zeros(series.shape[2:], jnp.float32)
    for number in range(series.shape[0]):
        harmonic = float(number + 1)
        change_cos = jnp.cos(harmonic * (phase_now + phase_move)) - jnp.cos(harmonic * phase_now)
        change_sin = jnp.sin(harmonic * (phase_now + phase_move)) - jnp.sin(harmonic * phase_now)
        series_sum = series_sum + series[number, 0] * change_cos - series[number, 1] * change_sin
    return series_sum

def metric_terms(offset_x, offset_y):
    x_zeta = 1.0 + (offset_x[..., 2:, 1:-1] - offset_x[..., :-2, 1:-1]) * 0.5
    x_xi = (offset_x[..., 1:-1, 2:] - offset_x[..., 1:-1, :-2]) * 0.5
    y_xi = 1.0 + (offset_y[..., 1:-1, 2:] - offset_y[..., 1:-1, :-2]) * 0.5
    y_zeta = (offset_y[..., 2:, 1:-1] - offset_y[..., :-2, 1:-1]) * 0.5
    return (x_zeta, x_xi, y_xi, y_zeta)

def geometry(grid_pad):
    x_zeta, x_xi, y_xi, y_zeta = metric_terms(grid_pad[0], grid_pad[1])
    old_zeta, old_xi, oldy_xi, oldy_zeta = metric_terms(grid_pad[0] - grid_pad[2], grid_pad[1] - grid_pad[3])
    volume_new = (x_zeta * y_xi - x_xi * y_zeta)[..., 1:-1, 1:-1]
    volume_old = (old_zeta * oldy_xi - old_xi * oldy_zeta)[..., 1:-1, 1:-1]
    speed_x = grid_pad[2][..., 1:-1, 1:-1] / TIME_STEP
    speed_y = grid_pad[3][..., 1:-1, 1:-1] / TIME_STEP
    first_pitch = -y_zeta
    second_pitch = x_zeta
    sweep_pitch = first_pitch * speed_x + second_pitch * speed_y
    first_axial = y_xi
    second_axial = -x_xi
    sweep_axial = first_axial * speed_x + second_axial * speed_y
    return ((first_pitch, second_pitch, sweep_pitch, first_axial, second_axial, sweep_axial), volume_old, volume_new)

def directional(strip_cells, first_coef, second_coef, sweep_term):
    density = strip_cells[0]
    vel_x = strip_cells[1] / density
    vel_y = strip_cells[2] / density
    energy = strip_cells[3]
    pressure = (HEAT_RATIO - 1.0) * (energy - 0.5 * density * (vel_x * vel_x + vel_y * vel_y))
    flux_x = jnp.stack([strip_cells[1], strip_cells[1] * vel_x + pressure, strip_cells[1] * vel_y, (energy + pressure) * vel_x])
    flux_y = jnp.stack([strip_cells[2], strip_cells[2] * vel_x, strip_cells[2] * vel_y + pressure, (energy + pressure) * vel_y])
    return first_coef * flux_x + second_coef * flux_y - sweep_term * strip_cells

def planar_residual(padded, geo_terms):
    first_pitch, second_pitch, sweep_pitch, first_axial, second_axial, sweep_axial = geo_terms
    pitch_flux = directional(padded[..., 2:-2, 1:-1], first_pitch[..., 1:-1, :], second_pitch[..., 1:-1, :], sweep_pitch[..., 1:-1, :])
    axial_flux = directional(padded[..., 1:-1, 2:-2], first_axial[..., :, 1:-1], second_axial[..., :, 1:-1], sweep_axial[..., :, 1:-1])
    divergence = (pitch_flux[..., 2:] - pitch_flux[..., :-2]) * 0.5 + (axial_flux[..., 2:, :] - axial_flux[..., :-2, :]) * 0.5
    centre = padded[..., 2:-2, 2:-2]
    fourth = padded[..., 2:-2, 4:] - 4.0 * padded[..., 2:-2, 3:-1] + 6.0 * centre - 4.0 * padded[..., 2:-2, 1:-3] + padded[..., 2:-2, :-4] + (padded[..., 4:, 2:-2] - 4.0 * padded[..., 3:-1, 2:-2] + 6.0 * centre - 4.0 * padded[..., 1:-3, 2:-2] + padded[..., :-4, 2:-2])
    return divergence + DAMPING * fourth

def flow_ghosts(row_zero, row_one, row_last, row_before, wrap_low0, wrap_low1, wrap_high0, wrap_high1, blade_flag, corr_low, corr_high):
    sign_flip = jnp.array([1.0, 1.0, -1.0, 1.0], jnp.float32).reshape((4,) + (1,) * (row_zero.ndim - 1))
    ghost_m2 = jnp.where(blade_flag, row_one * sign_flip, wrap_low0 + corr_low)
    ghost_m1 = jnp.where(blade_flag, row_zero * sign_flip, wrap_low1 + corr_low)
    ghost_p0 = jnp.where(blade_flag, row_last * sign_flip, wrap_high0 + corr_high)
    ghost_p1 = jnp.where(blade_flag, row_before * sign_flip, wrap_high1 + corr_high)
    return (ghost_m2, ghost_m1, ghost_p0, ghost_p1)

def reference(flow_state, node_offset, blade_mode, phase_angles, lag_series):
    axial_index = jnp.arange(NA, dtype=jnp.int32)
    lead_edge = NA // 4
    blade_flag = (axial_index >= lead_edge) & (axial_index < NA - lead_edge)
    blade_mask = blade_flag.astype(jnp.float32)
    blend_row = jnp.arange(NP, dtype=jnp.int32).astype(jnp.float32) / (NP - 1)
    phase_now = phase_angles[0]
    phase_lag = phase_angles[1]

    def surface_geometry(pieces):
        offsets, shape_mode = pieces
        low_wall = wall_amplitude(shape_mode, phase_now, blade_mask) * unit_normal(offsets[..., 0], offsets[..., 1])
        high_wall = wall_amplitude(shape_mode, phase_now + phase_lag, blade_mask) * unit_normal(offsets[..., NP - 2], offsets[..., NP - 1])
        shift_field = (1.0 - blend_row) * low_wall[..., None] + blend_row * high_wall[..., None]
        moved = offsets + shift_field
        grid_field = jnp.concatenate([moved, shift_field], 0)
        grid_pad = extend_linear(extend_linear(grid_field, 1), 2)
        geo_terms, volume_old, volume_new = geometry(grid_pad)
        return (moved, geo_terms, volume_old, volume_new)
    moved_r, geo_r, old_r, new_r = lax.map(surface_geometry, (jnp.moveaxis(node_offset, -1, 0), jnp.moveaxis(blade_mode, -1, 0)))
    corr_low_r = jnp.moveaxis(lag_shift(lag_series[1], phase_now, -phase_lag), -1, 0)
    corr_high_r = jnp.moveaxis(lag_shift(lag_series[0], phase_now, phase_lag), -1, 0)

    def surface_residual(pieces):
        current, geo_terms, corr_low, corr_high = pieces
        ghost_m2, ghost_m1, ghost_p0, ghost_p1 = flow_ghosts(current[..., 0], current[..., 1], current[..., NP - 1], current[..., NP - 2], current[..., NP - 2], current[..., NP - 1], current[..., 0], current[..., 1], blade_flag, corr_low, corr_high)
        padded = jnp.concatenate([ghost_m2[..., None], ghost_m1[..., None], current, ghost_p0[..., None], ghost_p1[..., None]], -1)
        padded = jnp.concatenate([padded[..., 0:1, :], padded[..., 0:1, :], padded, padded[..., -1:, :], padded[..., -1:, :]], -2)
        return planar_residual(padded, geo_terms)
    start_r = jnp.moveaxis(flow_state, -1, 0)
    current_r = start_r
    for weight in SECTION_WEIGHTS:
        planar = lax.map(surface_residual, (current_r, geo_r, corr_low_r, corr_high_r))
        total = planar + DAMPING * radial_damping(current_r, 0)
        current_r = (old_r[:, None] * start_r - weight * TIME_STEP * total) / new_r[:, None]
    return (jnp.moveaxis(current_r, 0, -1), jnp.moveaxis(moved_r, 0, -1))
```

```python
import jax
import jax.numpy as jnp
from jax import lax
from jax.sharding import PartitionSpec as P

HEAT_RATIO = 1.4
TIME_STEP = 0.25
DAMPING = 0.02
SECTION_WEIGHTS = (0.5, 1.0)


def broadcast(value, axis, root):
    mine = lax.axis_index(axis) == root
    return lax.psum(jnp.where(mine, value, jnp.zeros_like(value)), axis)


def padded_2(block, sides, width):
    for axis, dim in sides:
        count = lax.axis_size(axis)
        forward = [(i, i + 1) for i in range(count - 1)]
        forward.append((count - 1, 0))
        backward = [(target, source) for source, target in forward]
        low = lax.ppermute(
            lax.slice_in_dim(block, block.shape[dim] - width, None, axis=dim), axis, forward
        )
        high = lax.ppermute(lax.slice_in_dim(block, 0, width, axis=dim), axis, backward)
        block = jnp.concatenate([low, block, high], axis=dim)
    return block


def fill_ends(padded, axis_pos, depth, at_first, at_last):
    length = padded.shape[axis_pos]
    inner_first = lax.slice_in_dim(padded, depth, depth + 1, axis=axis_pos)
    inner_second = lax.slice_in_dim(padded, depth + 1, depth + 2, axis=axis_pos)
    inner_last = lax.slice_in_dim(padded, length - depth - 1, length - depth, axis=axis_pos)
    inner_before = lax.slice_in_dim(padded, length - depth - 2, length - depth - 1, axis=axis_pos)
    step_low = inner_first - inner_second
    step_high = inner_last - inner_before
    low_side = jnp.concatenate(
        [inner_first + float(count) * step_low for count in range(depth, 0, -1)], axis=axis_pos
    )
    high_side = jnp.concatenate(
        [inner_last + float(count) * step_high for count in range(1, depth + 1)], axis=axis_pos
    )
    low_side = jnp.where(at_first, low_side, lax.slice_in_dim(padded, 0, depth, axis=axis_pos))
    high_side = jnp.where(
        at_last, high_side, lax.slice_in_dim(padded, length - depth, length, axis=axis_pos)
    )
    return jnp.concatenate(
        [low_side, lax.slice_in_dim(padded, depth, length - depth, axis=axis_pos), high_side],
        axis=axis_pos,
    )


def radial_damping(values, axis_pos):
    count = values.shape[axis_pos]
    first_row = lax.slice_in_dim(values, 0, 1, axis=axis_pos)
    last_row = lax.slice_in_dim(values, count - 1, count, axis=axis_pos)
    extended = jnp.concatenate([first_row, first_row, values, last_row, last_row], axis=axis_pos)
    return (
        lax.slice_in_dim(extended, 4, 4 + count, axis=axis_pos)
        - 4.0 * lax.slice_in_dim(extended, 3, 3 + count, axis=axis_pos)
        + 6.0 * values
        - 4.0 * lax.slice_in_dim(extended, 1, 1 + count, axis=axis_pos)
        + lax.slice_in_dim(extended, 0, count, axis=axis_pos)
    )


def unit_normal(earlier, later):
    along_x = later[0] - earlier[0]
    along_y = 1.0 + later[1] - earlier[1]
    length = jnp.sqrt(along_x * along_x + along_y * along_y)
    return jnp.stack([along_x / length, along_y / length])


def wall_amplitude(shape_mode, angle, blade_mask):
    return (shape_mode[0] * jnp.cos(angle) - shape_mode[1] * jnp.sin(angle)) * blade_mask


def lag_shift(series, phase_now, phase_move):
    series_sum = jnp.zeros(series.shape[2:], jnp.float32)
    for number in range(series.shape[0]):
        harmonic = float(number + 1)
        change_cos = jnp.cos(harmonic * (phase_now + phase_move)) - jnp.cos(harmonic * phase_now)
        change_sin = jnp.sin(harmonic * (phase_now + phase_move)) - jnp.sin(harmonic * phase_now)
        series_sum = series_sum + series[number, 0] * change_cos - series[number, 1] * change_sin
    return series_sum


def metric_terms(offset_x, offset_y):
    x_zeta = 1.0 + (offset_x[2:, 1:-1] - offset_x[:-2, 1:-1]) * 0.5
    x_xi = (offset_x[1:-1, 2:] - offset_x[1:-1, :-2]) * 0.5
    y_xi = 1.0 + (offset_y[1:-1, 2:] - offset_y[1:-1, :-2]) * 0.5
    y_zeta = (offset_y[2:, 1:-1] - offset_y[:-2, 1:-1]) * 0.5
    return (x_zeta, x_xi, y_xi, y_zeta)


def geometry(grid_pad):
    x_zeta, x_xi, y_xi, y_zeta = metric_terms(grid_pad[0], grid_pad[1])
    old_zeta, old_xi, oldy_xi, oldy_zeta = metric_terms(
        grid_pad[0] - grid_pad[2], grid_pad[1] - grid_pad[3]
    )
    volume_new = (x_zeta * y_xi - x_xi * y_zeta)[1:-1, 1:-1]
    volume_old = (old_zeta * oldy_xi - old_xi * oldy_zeta)[1:-1, 1:-1]
    speed_x = grid_pad[2][1:-1, 1:-1] / TIME_STEP
    speed_y = grid_pad[3][1:-1, 1:-1] / TIME_STEP
    first_pitch = -y_zeta
    sweep_pitch = first_pitch * speed_x + x_zeta * speed_y
    second_axial = -x_xi
    sweep_axial = y_xi * speed_x + second_axial * speed_y
    return (
        (first_pitch, x_zeta, sweep_pitch, y_xi, second_axial, sweep_axial),
        volume_old,
        volume_new,
    )


def directional(strip_cells, first_coef, second_coef, sweep_term):
    density = strip_cells[0]
    vel_x = strip_cells[1] / density
    vel_y = strip_cells[2] / density
    energy = strip_cells[3]
    pressure = (HEAT_RATIO - 1.0) * (energy - 0.5 * density * (vel_x * vel_x + vel_y * vel_y))
    flux_x = jnp.stack(
        [
            strip_cells[1],
            strip_cells[1] * vel_x + pressure,
            strip_cells[1] * vel_y,
            (energy + pressure) * vel_x,
        ]
    )
    flux_y = jnp.stack(
        [
            strip_cells[2],
            strip_cells[2] * vel_x,
            strip_cells[2] * vel_y + pressure,
            (energy + pressure) * vel_y,
        ]
    )
    return first_coef * flux_x + second_coef * flux_y - sweep_term * strip_cells


def residual(padded, geo_terms):
    first_pitch, second_pitch, sweep_pitch, first_axial, second_axial, sweep_axial = geo_terms
    pitch_flux = directional(
        padded[:, 2:-2, 1:-1], first_pitch[1:-1], second_pitch[1:-1], sweep_pitch[1:-1]
    )
    axial_flux = directional(
        padded[:, 1:-1, 2:-2], first_axial[:, 1:-1], second_axial[:, 1:-1], sweep_axial[:, 1:-1]
    )
    divergence = (pitch_flux[:, :, 2:] - pitch_flux[:, :, :-2]) * 0.5 + (
        axial_flux[:, 2:] - axial_flux[:, :-2]
    ) * 0.5
    centre = padded[:, 2:-2, 2:-2]
    fourth = (
        padded[:, 2:-2, 4:]
        - 4.0 * padded[:, 2:-2, 3:-1]
        + 6.0 * centre
        - 4.0 * padded[:, 2:-2, 1:-3]
        + padded[:, 2:-2, :-4]
        + (
            padded[:, 4:, 2:-2]
            - 4.0 * padded[:, 3:-1, 2:-2]
            + 6.0 * centre
            - 4.0 * padded[:, 1:-3, 2:-2]
            + padded[:, :-4, 2:-2]
        )
    )
    return divergence + DAMPING * fourth + DAMPING * radial_damping(centre, 3)


def flow_ghosts(
    row_zero,
    row_one,
    row_last,
    row_before,
    wrap_low0,
    wrap_low1,
    wrap_high0,
    wrap_high1,
    blade_flag,
    corr_low,
    corr_high,
):
    sign_flip = jnp.array([1.0, 1.0, -1.0, 1.0], jnp.float32).reshape(
        (4,) + (1,) * (row_zero.ndim - 1)
    )
    ghost_m2 = jnp.where(blade_flag, row_one * sign_flip, wrap_low0 + corr_low)
    ghost_m1 = jnp.where(blade_flag, row_zero * sign_flip, wrap_low1 + corr_low)
    ghost_p0 = jnp.where(blade_flag, row_last * sign_flip, wrap_high0 + corr_high)
    ghost_p1 = jnp.where(blade_flag, row_before * sign_flip, wrap_high1 + corr_high)
    return (ghost_m2, ghost_m1, ghost_p0, ghost_p1)


def finish_flow(
    padded, depth, row_flag, corr_low, corr_high, low_end, high_end, first_end, last_end
):
    middle_rows = padded[:, 2:-2]
    width = middle_rows.shape[2]
    ghost_m2, ghost_m1, ghost_p0, ghost_p1 = flow_ghosts(
        middle_rows[:, :, 2],
        middle_rows[:, :, 3],
        middle_rows[:, :, width - 3],
        middle_rows[:, :, width - 4],
        middle_rows[:, :, 0],
        middle_rows[:, :, 1],
        middle_rows[:, :, width - 2],
        middle_rows[:, :, width - 1],
        row_flag[:, None],
        corr_low,
        corr_high,
    )
    low_pair = jnp.where(low_end, jnp.stack([ghost_m2, ghost_m1], 2), middle_rows[:, :, 0:2])
    high_pair = jnp.where(
        high_end, jnp.stack([ghost_p0, ghost_p1], 2), middle_rows[:, :, width - 2 :]
    )
    middle_rows = jnp.concatenate([low_pair, middle_rows[:, :, 2 : width - 2], high_pair], 2)
    whole = jnp.concatenate([padded[:, 0:2], middle_rows, padded[:, -2:]], 1)
    top_copy = jnp.repeat(whole[:, depth : depth + 1], depth, axis=1)
    bottom_copy = jnp.repeat(whole[:, -depth - 1 : -depth], depth, axis=1)
    top_rows = jnp.where(first_end, top_copy, whole[:, :depth])
    bottom_rows = jnp.where(last_end, bottom_copy, whole[:, -depth:])
    return jnp.concatenate([top_rows, whole[:, depth:-depth], bottom_rows], 1)


def per_device(flow_state, node_offset, blade_mode, phase_angles, lag_series):
    n_pitch = lax.axis_size("pitch")
    n_span = lax.axis_size("span")
    pitch_rows = flow_state.shape[2]
    axial_cols = flow_state.shape[1]
    total_pitch = pitch_rows * n_pitch
    total_axial = axial_cols * n_span
    pitch_at = lax.axis_index("pitch")
    span_at = lax.axis_index("span")
    lead_edge = total_axial // 4
    axial_index = span_at * axial_cols + jnp.arange(axial_cols, dtype=jnp.int32)
    blade_flag = (axial_index >= lead_edge) & (axial_index < total_axial - lead_edge)
    blade_mask = blade_flag.astype(jnp.float32)[:, None]
    phase_now = phase_angles[0]
    phase_lag = phase_angles[1]
    low_guess = wall_amplitude(blade_mode, phase_now, blade_mask) * unit_normal(
        node_offset[:, :, 0], node_offset[:, :, 1]
    )
    high_guess = wall_amplitude(blade_mode, phase_now + phase_lag, blade_mask) * unit_normal(
        node_offset[:, :, pitch_rows - 2], node_offset[:, :, pitch_rows - 1]
    )
    gathered = lax.all_gather(jnp.stack([low_guess, high_guess]), "pitch")
    low_wall = gathered[0, 0]
    high_wall = gathered[n_pitch - 1, 1]
    pitch_index = pitch_at * pitch_rows + jnp.arange(pitch_rows, dtype=jnp.int32)
    blend_row = (pitch_index.astype(jnp.float32) / (total_pitch - 1))[:, None]
    shift_field = (1.0 - blend_row) * low_wall[:, :, None, :] + blend_row * high_wall[:, :, None, :]
    moved_offset = node_offset + shift_field
    grid_field = jnp.concatenate([moved_offset, shift_field], 0)
    rim_width = 2
    grid_pad = padded_2(grid_field, (("pitch", 2), ("span", 1)), rim_width)
    first_pad = padded_2(flow_state, (("pitch", 2), ("span", 1)), rim_width)
    low_end = pitch_at == 0
    high_end = pitch_at == n_pitch - 1
    first_end = span_at == 0
    last_end = span_at == n_span - 1
    grid_pad = fill_ends(grid_pad, 1, rim_width, first_end, last_end)
    grid_pad = fill_ends(grid_pad, 2, 2, low_end, high_end)
    geo_terms, volume_old, volume_new = geometry(grid_pad)
    corr_low = lag_shift(lag_series[1], phase_now, -phase_lag)
    corr_high = lag_shift(lag_series[0], phase_now, phase_lag)
    padded = finish_flow(
        first_pad, 2, blade_flag, corr_low, corr_high, low_end, high_end, first_end, last_end
    )
    section_one = (
        volume_old * flow_state - SECTION_WEIGHTS[0] * TIME_STEP * residual(padded, geo_terms)
    ) / volume_new
    second_pad = padded_2(section_one, (("pitch", 2), ("span", 1)), 2)
    padded = finish_flow(
        second_pad, 2, blade_flag, corr_low, corr_high, low_end, high_end, first_end, last_end
    )
    current = (
        volume_old * flow_state - SECTION_WEIGHTS[1] * TIME_STEP * residual(padded, geo_terms)
    ) / volume_new
    return (current, moved_offset)


def solution(mesh):
    placed = (
        P(None, "span", "pitch", None),
        P(None, "span", "pitch", None),
        P(None, "span", None),
        P(),
        P(None, None, None, None, "span", None),
    )
    return jax.shard_map(
        per_device,
        mesh=mesh,
        in_specs=placed,
        out_specs=(P(None, "span", "pitch", None), P(None, "span", "pitch", None)),
        check_vma=False,
    )
```

```python
import jax
import jax.numpy as jnp
from jax import lax
from jax.sharding import PartitionSpec as P
from jax.experimental import pallas as pl
from jax.experimental.pallas import tpu as pltpu

HEAT_RATIO = 1.4
TIME_STEP = 0.25
DAMPING = 0.02
SECTION_WEIGHTS = (0.5, 1.0)


def broadcast(value, axis, root):
    mine = lax.axis_index(axis) == root
    return lax.psum(jnp.where(mine, value, jnp.zeros_like(value)), axis)


def padded_2(block, sides, width):
    for axis, dim in sides:
        count = lax.axis_size(axis)
        forward = [(i, i + 1) for i in range(count - 1)]
        forward.append((count - 1, 0))
        backward = [(target, source) for source, target in forward]
        low = lax.ppermute(
            lax.slice_in_dim(block, block.shape[dim] - width, None, axis=dim), axis, forward
        )
        high = lax.ppermute(lax.slice_in_dim(block, 0, width, axis=dim), axis, backward)
        block = jnp.concatenate([low, block, high], axis=dim)
    return block


def fill_ends(padded, axis_pos, depth, at_first, at_last):
    length = padded.shape[axis_pos]
    inner_first = lax.slice_in_dim(padded, depth, depth + 1, axis=axis_pos)
    inner_second = lax.slice_in_dim(padded, depth + 1, depth + 2, axis=axis_pos)
    inner_last = lax.slice_in_dim(padded, length - depth - 1, length - depth, axis=axis_pos)
    inner_before = lax.slice_in_dim(padded, length - depth - 2, length - depth - 1, axis=axis_pos)
    step_low = inner_first - inner_second
    step_high = inner_last - inner_before
    low_side = jnp.concatenate(
        [inner_first + float(count) * step_low for count in range(depth, 0, -1)], axis=axis_pos
    )
    high_side = jnp.concatenate(
        [inner_last + float(count) * step_high for count in range(1, depth + 1)], axis=axis_pos
    )
    low_side = jnp.where(at_first, low_side, lax.slice_in_dim(padded, 0, depth, axis=axis_pos))
    high_side = jnp.where(
        at_last, high_side, lax.slice_in_dim(padded, length - depth, length, axis=axis_pos)
    )
    return jnp.concatenate(
        [low_side, lax.slice_in_dim(padded, depth, length - depth, axis=axis_pos), high_side],
        axis=axis_pos,
    )


def radial_damping(values, axis_pos):
    count = values.shape[axis_pos]
    first_row = lax.slice_in_dim(values, 0, 1, axis=axis_pos)
    last_row = lax.slice_in_dim(values, count - 1, count, axis=axis_pos)
    extended = jnp.concatenate([first_row, first_row, values, last_row, last_row], axis=axis_pos)
    return (
        lax.slice_in_dim(extended, 4, 4 + count, axis=axis_pos)
        - 4.0 * lax.slice_in_dim(extended, 3, 3 + count, axis=axis_pos)
        + 6.0 * values
        - 4.0 * lax.slice_in_dim(extended, 1, 1 + count, axis=axis_pos)
        + lax.slice_in_dim(extended, 0, count, axis=axis_pos)
    )


def unit_normal(earlier, later):
    along_x = later[0] - earlier[0]
    along_y = 1.0 + later[1] - earlier[1]
    length = jnp.sqrt(along_x * along_x + along_y * along_y)
    return jnp.stack([along_x / length, along_y / length])


def wall_amplitude(shape_mode, angle, blade_mask):
    return (shape_mode[0] * jnp.cos(angle) - shape_mode[1] * jnp.sin(angle)) * blade_mask


def lag_shift(series, phase_now, phase_move):
    series_sum = jnp.zeros(series.shape[2:], jnp.float32)
    for number in range(series.shape[0]):
        harmonic = float(number + 1)
        change_cos = jnp.cos(harmonic * (phase_now + phase_move)) - jnp.cos(harmonic * phase_now)
        change_sin = jnp.sin(harmonic * (phase_now + phase_move)) - jnp.sin(harmonic * phase_now)
        series_sum = series_sum + series[number, 0] * change_cos - series[number, 1] * change_sin
    return series_sum


def metric_terms(offset_x, offset_y):
    x_zeta = 1.0 + (offset_x[2:, 1:-1] - offset_x[:-2, 1:-1]) * 0.5
    x_xi = (offset_x[1:-1, 2:] - offset_x[1:-1, :-2]) * 0.5
    y_xi = 1.0 + (offset_y[1:-1, 2:] - offset_y[1:-1, :-2]) * 0.5
    y_zeta = (offset_y[2:, 1:-1] - offset_y[:-2, 1:-1]) * 0.5
    return (x_zeta, x_xi, y_xi, y_zeta)


def geometry(grid_pad):
    x_zeta, x_xi, y_xi, y_zeta = metric_terms(grid_pad[0], grid_pad[1])
    old_zeta, old_xi, oldy_xi, oldy_zeta = metric_terms(
        grid_pad[0] - grid_pad[2], grid_pad[1] - grid_pad[3]
    )
    volume_new = (x_zeta * y_xi - x_xi * y_zeta)[1:-1, 1:-1]
    volume_old = (old_zeta * oldy_xi - old_xi * oldy_zeta)[1:-1, 1:-1]
    speed_x = grid_pad[2][1:-1, 1:-1] / TIME_STEP
    speed_y = grid_pad[3][1:-1, 1:-1] / TIME_STEP
    first_pitch = -y_zeta
    sweep_pitch = first_pitch * speed_x + x_zeta * speed_y
    second_axial = -x_xi
    sweep_axial = y_xi * speed_x + second_axial * speed_y
    return (
        (first_pitch, x_zeta, sweep_pitch, y_xi, second_axial, sweep_axial),
        volume_old,
        volume_new,
    )


def directional(strip_cells, first_coef, second_coef, sweep_term):
    density = strip_cells[0]
    vel_x = strip_cells[1] / density
    vel_y = strip_cells[2] / density
    energy = strip_cells[3]
    pressure = (HEAT_RATIO - 1.0) * (energy - 0.5 * density * (vel_x * vel_x + vel_y * vel_y))
    flux_x = jnp.stack(
        [
            strip_cells[1],
            strip_cells[1] * vel_x + pressure,
            strip_cells[1] * vel_y,
            (energy + pressure) * vel_x,
        ]
    )
    flux_y = jnp.stack(
        [
            strip_cells[2],
            strip_cells[2] * vel_x,
            strip_cells[2] * vel_y + pressure,
            (energy + pressure) * vel_y,
        ]
    )
    return first_coef * flux_x + second_coef * flux_y - sweep_term * strip_cells


def residual(padded, geo_terms):
    first_pitch, second_pitch, sweep_pitch, first_axial, second_axial, sweep_axial = geo_terms
    pitch_flux = directional(
        padded[:, 2:-2, 1:-1], first_pitch[1:-1], second_pitch[1:-1], sweep_pitch[1:-1]
    )
    axial_flux = directional(
        padded[:, 1:-1, 2:-2], first_axial[:, 1:-1], second_axial[:, 1:-1], sweep_axial[:, 1:-1]
    )
    divergence = (pitch_flux[:, :, 2:] - pitch_flux[:, :, :-2]) * 0.5 + (
        axial_flux[:, 2:] - axial_flux[:, :-2]
    ) * 0.5
    centre = padded[:, 2:-2, 2:-2]
    fourth = (
        padded[:, 2:-2, 4:]
        - 4.0 * padded[:, 2:-2, 3:-1]
        + 6.0 * centre
        - 4.0 * padded[:, 2:-2, 1:-3]
        + padded[:, 2:-2, :-4]
        + (
            padded[:, 4:, 2:-2]
            - 4.0 * padded[:, 3:-1, 2:-2]
            + 6.0 * centre
            - 4.0 * padded[:, 1:-3, 2:-2]
            + padded[:, :-4, 2:-2]
        )
    )
    return divergence + DAMPING * fourth + DAMPING * radial_damping(centre, 3)


def flow_ghosts(
    row_zero,
    row_one,
    row_last,
    row_before,
    wrap_low0,
    wrap_low1,
    wrap_high0,
    wrap_high1,
    blade_flag,
    corr_low,
    corr_high,
):
    sign_flip = jnp.array([1.0, 1.0, -1.0, 1.0], jnp.float32).reshape(
        (4,) + (1,) * (row_zero.ndim - 1)
    )
    ghost_m2 = jnp.where(blade_flag, row_one * sign_flip, wrap_low0 + corr_low)
    ghost_m1 = jnp.where(blade_flag, row_zero * sign_flip, wrap_low1 + corr_low)
    ghost_p0 = jnp.where(blade_flag, row_last * sign_flip, wrap_high0 + corr_high)
    ghost_p1 = jnp.where(blade_flag, row_before * sign_flip, wrap_high1 + corr_high)
    return (ghost_m2, ghost_m1, ghost_p0, ghost_p1)


def finish_flow(
    padded, depth, row_flag, corr_low, corr_high, low_end, high_end, first_end, last_end
):
    middle_rows = padded[:, 2:-2]
    width = middle_rows.shape[2]
    ghost_m2, ghost_m1, ghost_p0, ghost_p1 = flow_ghosts(
        middle_rows[:, :, 2],
        middle_rows[:, :, 3],
        middle_rows[:, :, width - 3],
        middle_rows[:, :, width - 4],
        middle_rows[:, :, 0],
        middle_rows[:, :, 1],
        middle_rows[:, :, width - 2],
        middle_rows[:, :, width - 1],
        row_flag[:, None],
        corr_low,
        corr_high,
    )
    low_pair = jnp.where(low_end, jnp.stack([ghost_m2, ghost_m1], 2), middle_rows[:, :, 0:2])
    high_pair = jnp.where(
        high_end, jnp.stack([ghost_p0, ghost_p1], 2), middle_rows[:, :, width - 2 :]
    )
    middle_rows = jnp.concatenate([low_pair, middle_rows[:, :, 2 : width - 2], high_pair], 2)
    whole = jnp.concatenate([padded[:, 0:2], middle_rows, padded[:, -2:]], 1)
    top_copy = jnp.repeat(whole[:, depth : depth + 1], depth, axis=1)
    bottom_copy = jnp.repeat(whole[:, -depth - 1 : -depth], depth, axis=1)
    top_rows = jnp.where(first_end, top_copy, whole[:, :depth])
    bottom_rows = jnp.where(last_end, bottom_copy, whole[:, -depth:])
    return jnp.concatenate([top_rows, whole[:, depth:-depth], bottom_rows], 1)


def _flux(rho, mx, my, en, first, second, sweep):
    u = mx / rho
    v = my / rho
    pr = (HEAT_RATIO - 1.0) * (en - 0.5 * rho * (u * u + v * v))
    ep = en + pr
    return (
        first * mx + second * my - sweep * rho,
        first * (mx * u + pr) + second * (my * u) - sweep * mx,
        first * (mx * v) + second * (my * v + pr) - sweep * my,
        first * (ep * u) + second * (ep * v) - sweep * en,
    )


def _radial(c0, lane, forward):
    width = c0.shape[-1]
    last = width - 1

    def down(x):
        a = pltpu.roll(x, 1, 1)
        b = pltpu.roll(x, last, 1)
        return jnp.where(forward, a, b)

    def up(x):
        a = pltpu.roll(x, 1, 1)
        b = pltpu.roll(x, last, 1)
        return jnp.where(forward, b, a)

    m1 = jnp.where(lane == 0, c0, down(c0))
    p1 = jnp.where(lane == last, c0, up(c0))
    m2 = jnp.where(lane == 0, c0, down(m1))
    p2 = jnp.where(lane == last, c0, up(p1))
    return p2 - 4.0 * p1 + 6.0 * c0 - 4.0 * m1 + m2


def _section_body(scale, pad, fp, sp, wp, fa, sa, wa, vold, vnew, q0, out, af, pf):
    na = out.shape[1]
    npch = out.shape[2]
    width = out.shape[3]

    def axial_row(j, carry):
        q = [pad[k, j + 1, 2 : npch + 2] for k in range(4)]
        f = _flux(*q, fa[j, 1 : npch + 1], sa[j, 1 : npch + 1], wa[j, 1 : npch + 1])
        for k in range(4):
            af[k, j] = f[k]
        return carry

    lax.fori_loop(0, na + 2, axial_row, 0)
    lane = lax.broadcasted_iota(jnp.int32, (npch, width), 1)
    probe = pltpu.roll(lane, 1, 1)
    forward = probe == jnp.where(lane == 0, width - 1, lane - 1)

    def row(a, carry):
        q = [pad[k, a + 2, 1 : npch + 3] for k in range(4)]
        f = _flux(*q, fp[a + 1], sp[a + 1], wp[a + 1])
        for k in range(4):
            pf[k] = f[k]
        volume_old = vold[a]
        volume_new = vnew[a]
        for k in range(4):
            div = (pf[k, 2 : npch + 2] - pf[k, 0:npch]) * 0.5 + (af[k, a + 2] - af[k, a]) * 0.5
            c0 = pad[k, a + 2, 2 : npch + 2]
            fourth = (
                pad[k, a + 2, 4 : npch + 4]
                - 4.0 * pad[k, a + 2, 3 : npch + 3]
                + 6.0 * c0
                - 4.0 * pad[k, a + 2, 1 : npch + 1]
                + pad[k, a + 2, 0:npch]
            ) + (
                pad[k, a + 4, 2 : npch + 2]
                - 4.0 * pad[k, a + 3, 2 : npch + 2]
                + 6.0 * c0
                - 4.0 * pad[k, a + 1, 2 : npch + 2]
                + pad[k, a, 2 : npch + 2]
            )
            res = div + DAMPING * fourth + DAMPING * _radial(c0, lane, forward)
            out[k, a] = (volume_old * q0[k, a] - scale * res) / volume_new
        return carry

    lax.fori_loop(0, na, row, 0)


def section_kernel(padded, geo_terms, volume_old, volume_new, start, scale, interpret=False):
    _, na, npch, width = start.shape
    body = lambda *refs: _section_body(scale, *refs)
    cells = na * npch * width
    return pl.pallas_call(
        body,
        out_shape=jax.ShapeDtypeStruct(start.shape, start.dtype),
        scratch_shapes=[
            pltpu.VMEM((4, na + 2, npch, width), jnp.float32),
            pltpu.VMEM((4, npch + 2, width), jnp.float32),
        ],
        compiler_params=pltpu.CompilerParams(vmem_limit_bytes=60 * 1024 * 1024),
        cost_estimate=pl.CostEstimate(
            flops=400 * cells, transcendentals=0, bytes_accessed=4 * 20 * cells
        ),
        interpret=interpret,
    )(padded, *geo_terms, volume_old, volume_new, start)


def per_device(flow_state, node_offset, blade_mode, phase_angles, lag_series):
    n_pitch = lax.axis_size("pitch")
    n_span = lax.axis_size("span")
    pitch_rows = flow_state.shape[2]
    axial_cols = flow_state.shape[1]
    total_pitch = pitch_rows * n_pitch
    total_axial = axial_cols * n_span
    pitch_at = lax.axis_index("pitch")
    span_at = lax.axis_index("span")
    lead_edge = total_axial // 4
    axial_index = span_at * axial_cols + jnp.arange(axial_cols, dtype=jnp.int32)
    blade_flag = (axial_index >= lead_edge) & (axial_index < total_axial - lead_edge)
    blade_mask = blade_flag.astype(jnp.float32)[:, None]
    phase_now = phase_angles[0]
    phase_lag = phase_angles[1]
    low_guess = wall_amplitude(blade_mode, phase_now, blade_mask) * unit_normal(
        node_offset[:, :, 0], node_offset[:, :, 1]
    )
    high_guess = wall_amplitude(blade_mode, phase_now + phase_lag, blade_mask) * unit_normal(
        node_offset[:, :, pitch_rows - 2], node_offset[:, :, pitch_rows - 1]
    )
    gathered = lax.all_gather(jnp.stack([low_guess, high_guess]), "pitch")
    low_wall = gathered[0, 0]
    high_wall = gathered[n_pitch - 1, 1]
    pitch_index = pitch_at * pitch_rows + jnp.arange(pitch_rows, dtype=jnp.int32)
    blend_row = (pitch_index.astype(jnp.float32) / (total_pitch - 1))[:, None]
    shift_field = (1.0 - blend_row) * low_wall[:, :, None, :] + blend_row * high_wall[:, :, None, :]
    moved_offset = node_offset + shift_field
    grid_field = jnp.concatenate([moved_offset, shift_field], 0)
    rim_width = 2
    grid_pad = padded_2(grid_field, (("pitch", 2), ("span", 1)), rim_width)
    first_pad = padded_2(flow_state, (("pitch", 2), ("span", 1)), rim_width)
    low_end = pitch_at == 0
    high_end = pitch_at == n_pitch - 1
    first_end = span_at == 0
    last_end = span_at == n_span - 1
    grid_pad = fill_ends(grid_pad, 1, rim_width, first_end, last_end)
    grid_pad = fill_ends(grid_pad, 2, 2, low_end, high_end)
    geo_terms, volume_old, volume_new = geometry(grid_pad)
    corr_low = lag_shift(lag_series[1], phase_now, -phase_lag)
    corr_high = lag_shift(lag_series[0], phase_now, phase_lag)
    padded = finish_flow(
        first_pad, 2, blade_flag, corr_low, corr_high, low_end, high_end, first_end, last_end
    )
    section_one = section_kernel(
        padded, geo_terms, volume_old, volume_new, flow_state, SECTION_WEIGHTS[0] * TIME_STEP
    )
    second_pad = padded_2(section_one, (("pitch", 2), ("span", 1)), 2)
    padded = finish_flow(
        second_pad, 2, blade_flag, corr_low, corr_high, low_end, high_end, first_end, last_end
    )
    current = section_kernel(
        padded, geo_terms, volume_old, volume_new, flow_state, SECTION_WEIGHTS[1] * TIME_STEP
    )
    return (current, moved_offset)


def solution(mesh):
    placed = (
        P(None, "span", "pitch", None),
        P(None, "span", "pitch", None),
        P(None, "span", None),
        P(),
        P(None, None, None, None, "span", None),
    )
    return jax.shard_map(
        per_device,
        mesh=mesh,
        in_specs=placed,
        out_specs=(P(None, "span", "pitch", None), P(None, "span", "pitch", None)),
        check_vma=False,
    )
```

```python
import jax
import jax.numpy as jnp
from jax import lax
from jax.sharding import PartitionSpec as P
from jax.experimental import pallas as pl
from jax.experimental.pallas import tpu as pltpu

HEAT_RATIO = 1.4
TIME_STEP = 0.25
DAMPING = 0.02
SECTION_WEIGHTS = (0.5, 1.0)


def broadcast(value, axis, root):
    mine = lax.axis_index(axis) == root
    return lax.psum(jnp.where(mine, value, jnp.zeros_like(value)), axis)


def padded_2(block, sides, width):
    for axis, dim in sides:
        count = lax.axis_size(axis)
        forward = [(i, i + 1) for i in range(count - 1)]
        forward.append((count - 1, 0))
        backward = [(target, source) for source, target in forward]
        low = lax.ppermute(
            lax.slice_in_dim(block, block.shape[dim] - width, None, axis=dim), axis, forward
        )
        high = lax.ppermute(lax.slice_in_dim(block, 0, width, axis=dim), axis, backward)
        block = jnp.concatenate([low, block, high], axis=dim)
    return block


def fill_ends(padded, axis_pos, depth, at_first, at_last):
    length = padded.shape[axis_pos]
    inner_first = lax.slice_in_dim(padded, depth, depth + 1, axis=axis_pos)
    inner_second = lax.slice_in_dim(padded, depth + 1, depth + 2, axis=axis_pos)
    inner_last = lax.slice_in_dim(padded, length - depth - 1, length - depth, axis=axis_pos)
    inner_before = lax.slice_in_dim(padded, length - depth - 2, length - depth - 1, axis=axis_pos)
    step_low = inner_first - inner_second
    step_high = inner_last - inner_before
    low_side = jnp.concatenate(
        [inner_first + float(count) * step_low for count in range(depth, 0, -1)], axis=axis_pos
    )
    high_side = jnp.concatenate(
        [inner_last + float(count) * step_high for count in range(1, depth + 1)], axis=axis_pos
    )
    low_side = jnp.where(at_first, low_side, lax.slice_in_dim(padded, 0, depth, axis=axis_pos))
    high_side = jnp.where(
        at_last, high_side, lax.slice_in_dim(padded, length - depth, length, axis=axis_pos)
    )
    return jnp.concatenate(
        [low_side, lax.slice_in_dim(padded, depth, length - depth, axis=axis_pos), high_side],
        axis=axis_pos,
    )


def radial_damping(values, axis_pos):
    count = values.shape[axis_pos]
    first_row = lax.slice_in_dim(values, 0, 1, axis=axis_pos)
    last_row = lax.slice_in_dim(values, count - 1, count, axis=axis_pos)
    extended = jnp.concatenate([first_row, first_row, values, last_row, last_row], axis=axis_pos)
    return (
        lax.slice_in_dim(extended, 4, 4 + count, axis=axis_pos)
        - 4.0 * lax.slice_in_dim(extended, 3, 3 + count, axis=axis_pos)
        + 6.0 * values
        - 4.0 * lax.slice_in_dim(extended, 1, 1 + count, axis=axis_pos)
        + lax.slice_in_dim(extended, 0, count, axis=axis_pos)
    )


def unit_normal(earlier, later):
    along_x = later[0] - earlier[0]
    along_y = 1.0 + later[1] - earlier[1]
    length = jnp.sqrt(along_x * along_x + along_y * along_y)
    return jnp.stack([along_x / length, along_y / length])


def wall_amplitude(shape_mode, angle, blade_mask):
    return (shape_mode[0] * jnp.cos(angle) - shape_mode[1] * jnp.sin(angle)) * blade_mask


def lag_shift(series, phase_now, phase_move):
    series_sum = jnp.zeros(series.shape[2:], jnp.float32)
    for number in range(series.shape[0]):
        harmonic = float(number + 1)
        change_cos = jnp.cos(harmonic * (phase_now + phase_move)) - jnp.cos(harmonic * phase_now)
        change_sin = jnp.sin(harmonic * (phase_now + phase_move)) - jnp.sin(harmonic * phase_now)
        series_sum = series_sum + series[number, 0] * change_cos - series[number, 1] * change_sin
    return series_sum


def metric_terms(offset_x, offset_y):
    x_zeta = 1.0 + (offset_x[2:, 1:-1] - offset_x[:-2, 1:-1]) * 0.5
    x_xi = (offset_x[1:-1, 2:] - offset_x[1:-1, :-2]) * 0.5
    y_xi = 1.0 + (offset_y[1:-1, 2:] - offset_y[1:-1, :-2]) * 0.5
    y_zeta = (offset_y[2:, 1:-1] - offset_y[:-2, 1:-1]) * 0.5
    return (x_zeta, x_xi, y_xi, y_zeta)


def geometry(grid_pad):
    x_zeta, x_xi, y_xi, y_zeta = metric_terms(grid_pad[0], grid_pad[1])
    old_zeta, old_xi, oldy_xi, oldy_zeta = metric_terms(
        grid_pad[0] - grid_pad[2], grid_pad[1] - grid_pad[3]
    )
    volume_new = (x_zeta * y_xi - x_xi * y_zeta)[1:-1, 1:-1]
    volume_old = (old_zeta * oldy_xi - old_xi * oldy_zeta)[1:-1, 1:-1]
    speed_x = grid_pad[2][1:-1, 1:-1] / TIME_STEP
    speed_y = grid_pad[3][1:-1, 1:-1] / TIME_STEP
    first_pitch = -y_zeta
    sweep_pitch = first_pitch * speed_x + x_zeta * speed_y
    second_axial = -x_xi
    sweep_axial = y_xi * speed_x + second_axial * speed_y
    return (
        (first_pitch, x_zeta, sweep_pitch, y_xi, second_axial, sweep_axial),
        volume_old,
        volume_new,
    )


def directional(strip_cells, first_coef, second_coef, sweep_term):
    density = strip_cells[0]
    vel_x = strip_cells[1] / density
    vel_y = strip_cells[2] / density
    energy = strip_cells[3]
    pressure = (HEAT_RATIO - 1.0) * (energy - 0.5 * density * (vel_x * vel_x + vel_y * vel_y))
    flux_x = jnp.stack(
        [
            strip_cells[1],
            strip_cells[1] * vel_x + pressure,
            strip_cells[1] * vel_y,
            (energy + pressure) * vel_x,
        ]
    )
    flux_y = jnp.stack(
        [
            strip_cells[2],
            strip_cells[2] * vel_x,
            strip_cells[2] * vel_y + pressure,
            (energy + pressure) * vel_y,
        ]
    )
    return first_coef * flux_x + second_coef * flux_y - sweep_term * strip_cells


def residual(padded, geo_terms):
    first_pitch, second_pitch, sweep_pitch, first_axial, second_axial, sweep_axial = geo_terms
    pitch_flux = directional(
        padded[:, 2:-2, 1:-1], first_pitch[1:-1], second_pitch[1:-1], sweep_pitch[1:-1]
    )
    axial_flux = directional(
        padded[:, 1:-1, 2:-2], first_axial[:, 1:-1], second_axial[:, 1:-1], sweep_axial[:, 1:-1]
    )
    divergence = (pitch_flux[:, :, 2:] - pitch_flux[:, :, :-2]) * 0.5 + (
        axial_flux[:, 2:] - axial_flux[:, :-2]
    ) * 0.5
    centre = padded[:, 2:-2, 2:-2]
    fourth = (
        padded[:, 2:-2, 4:]
        - 4.0 * padded[:, 2:-2, 3:-1]
        + 6.0 * centre
        - 4.0 * padded[:, 2:-2, 1:-3]
        + padded[:, 2:-2, :-4]
        + (
            padded[:, 4:, 2:-2]
            - 4.0 * padded[:, 3:-1, 2:-2]
            + 6.0 * centre
            - 4.0 * padded[:, 1:-3, 2:-2]
            + padded[:, :-4, 2:-2]
        )
    )
    return divergence + DAMPING * fourth + DAMPING * radial_damping(centre, 3)


def flow_ghosts(
    row_zero,
    row_one,
    row_last,
    row_before,
    wrap_low0,
    wrap_low1,
    wrap_high0,
    wrap_high1,
    blade_flag,
    corr_low,
    corr_high,
):
    sign_flip = jnp.array([1.0, 1.0, -1.0, 1.0], jnp.float32).reshape(
        (4,) + (1,) * (row_zero.ndim - 1)
    )
    ghost_m2 = jnp.where(blade_flag, row_one * sign_flip, wrap_low0 + corr_low)
    ghost_m1 = jnp.where(blade_flag, row_zero * sign_flip, wrap_low1 + corr_low)
    ghost_p0 = jnp.where(blade_flag, row_last * sign_flip, wrap_high0 + corr_high)
    ghost_p1 = jnp.where(blade_flag, row_before * sign_flip, wrap_high1 + corr_high)
    return (ghost_m2, ghost_m1, ghost_p0, ghost_p1)


def finish_flow(
    padded, depth, row_flag, corr_low, corr_high, low_end, high_end, first_end, last_end
):
    middle_rows = padded[:, 2:-2]
    width = middle_rows.shape[2]
    ghost_m2, ghost_m1, ghost_p0, ghost_p1 = flow_ghosts(
        middle_rows[:, :, 2],
        middle_rows[:, :, 3],
        middle_rows[:, :, width - 3],
        middle_rows[:, :, width - 4],
        middle_rows[:, :, 0],
        middle_rows[:, :, 1],
        middle_rows[:, :, width - 2],
        middle_rows[:, :, width - 1],
        row_flag[:, None],
        corr_low,
        corr_high,
    )
    low_pair = jnp.where(low_end, jnp.stack([ghost_m2, ghost_m1], 2), middle_rows[:, :, 0:2])
    high_pair = jnp.where(
        high_end, jnp.stack([ghost_p0, ghost_p1], 2), middle_rows[:, :, width - 2 :]
    )
    middle_rows = jnp.concatenate([low_pair, middle_rows[:, :, 2 : width - 2], high_pair], 2)
    whole = jnp.concatenate([padded[:, 0:2], middle_rows, padded[:, -2:]], 1)
    top_copy = jnp.repeat(whole[:, depth : depth + 1], depth, axis=1)
    bottom_copy = jnp.repeat(whole[:, -depth - 1 : -depth], depth, axis=1)
    top_rows = jnp.where(first_end, top_copy, whole[:, :depth])
    bottom_rows = jnp.where(last_end, bottom_copy, whole[:, -depth:])
    return jnp.concatenate([top_rows, whole[:, depth:-depth], bottom_rows], 1)


def _flux(rho, mx, my, en, first, second, sweep):
    u = mx / rho
    v = my / rho
    pr = (HEAT_RATIO - 1.0) * (en - 0.5 * rho * (u * u + v * v))
    ep = en + pr
    return (
        first * mx + second * my - sweep * rho,
        first * (mx * u + pr) + second * (my * u) - sweep * mx,
        first * (mx * v) + second * (my * v + pr) - sweep * my,
        first * (ep * u) + second * (ep * v) - sweep * en,
    )


def _radial(c0, lane, forward):
    width = c0.shape[-1]
    last = width - 1

    def down(x):
        a = pltpu.roll(x, 1, 1)
        b = pltpu.roll(x, last, 1)
        return jnp.where(forward, a, b)

    def up(x):
        a = pltpu.roll(x, 1, 1)
        b = pltpu.roll(x, last, 1)
        return jnp.where(forward, b, a)

    m1 = jnp.where(lane == 0, c0, down(c0))
    p1 = jnp.where(lane == last, c0, up(c0))
    m2 = jnp.where(lane == 0, c0, down(m1))
    p2 = jnp.where(lane == last, c0, up(p1))
    return p2 - 4.0 * p1 + 6.0 * c0 - 4.0 * m1 + m2


def _section_body(scale, pad, fp, sp, wp, fa, sa, wa, vold, vnew, q0, out, af, pf):
    na = out.shape[1]
    npch = out.shape[2]
    width = out.shape[3]

    def axial_row(j, carry):
        q = [pad[k, j + 1, 2 : npch + 2] for k in range(4)]
        f = _flux(*q, fa[j, 1 : npch + 1], sa[j, 1 : npch + 1], wa[j, 1 : npch + 1])
        for k in range(4):
            af[k, j] = f[k]
        return carry

    lax.fori_loop(0, na + 2, axial_row, 0)
    lane = lax.broadcasted_iota(jnp.int32, (npch, width), 1)
    probe = pltpu.roll(lane, 1, 1)
    forward = probe == jnp.where(lane == 0, width - 1, lane - 1)

    def row(a, carry):
        q = [pad[k, a + 2, 1 : npch + 3] for k in range(4)]
        f = _flux(*q, fp[a + 1], sp[a + 1], wp[a + 1])
        for k in range(4):
            pf[k] = f[k]
        volume_old = vold[a]
        volume_new = vnew[a]
        for k in range(4):
            div = (pf[k, 2 : npch + 2] - pf[k, 0:npch]) * 0.5 + (af[k, a + 2] - af[k, a]) * 0.5
            c0 = pad[k, a + 2, 2 : npch + 2]
            fourth = (
                pad[k, a + 2, 4 : npch + 4]
                - 4.0 * pad[k, a + 2, 3 : npch + 3]
                + 6.0 * c0
                - 4.0 * pad[k, a + 2, 1 : npch + 1]
                + pad[k, a + 2, 0:npch]
            ) + (
                pad[k, a + 4, 2 : npch + 2]
                - 4.0 * pad[k, a + 3, 2 : npch + 2]
                + 6.0 * c0
                - 4.0 * pad[k, a + 1, 2 : npch + 2]
                + pad[k, a, 2 : npch + 2]
            )
            res = div + DAMPING * fourth + DAMPING * _radial(c0, lane, forward)
            out[k, a] = (volume_old * q0[k, a] - scale * res) / volume_new
        return carry

    lax.fori_loop(0, na, row, 0)


def section_kernel(padded, geo_terms, volume_old, volume_new, start, scale, interpret=False):
    _, na, npch, width = start.shape
    body = lambda *refs: _section_body(scale, *refs)
    cells = na * npch * width
    return pl.pallas_call(
        body,
        out_shape=jax.ShapeDtypeStruct(start.shape, start.dtype),
        scratch_shapes=[
            pltpu.VMEM((4, na + 2, npch, width), jnp.float32),
            pltpu.VMEM((4, npch + 2, width), jnp.float32),
        ],
        compiler_params=pltpu.CompilerParams(vmem_limit_bytes=60 * 1024 * 1024),
        cost_estimate=pl.CostEstimate(
            flops=400 * cells, transcendentals=0, bytes_accessed=4 * 20 * cells
        ),
        interpret=interpret,
    )(padded, *geo_terms, volume_old, volume_new, start)


def per_device(flow_state, node_offset, blade_mode, phase_angles, lag_series):
    n_pitch = lax.axis_size("pitch")
    n_span = lax.axis_size("span")
    pitch_rows = flow_state.shape[2]
    axial_cols = flow_state.shape[1]
    total_pitch = pitch_rows * n_pitch
    total_axial = axial_cols * n_span
    pitch_at = lax.axis_index("pitch")
    span_at = lax.axis_index("span")
    lead_edge = total_axial // 4
    axial_index = span_at * axial_cols + jnp.arange(axial_cols, dtype=jnp.int32)
    blade_flag = (axial_index >= lead_edge) & (axial_index < total_axial - lead_edge)
    blade_mask = blade_flag.astype(jnp.float32)[:, None]
    phase_now = phase_angles[0]
    phase_lag = phase_angles[1]
    low_guess = wall_amplitude(blade_mode, phase_now, blade_mask) * unit_normal(
        node_offset[:, :, 0], node_offset[:, :, 1]
    )
    high_guess = wall_amplitude(blade_mode, phase_now + phase_lag, blade_mask) * unit_normal(
        node_offset[:, :, pitch_rows - 2], node_offset[:, :, pitch_rows - 1]
    )
    low_wall = low_guess
    high_wall = high_guess
    sent = jnp.where(pitch_at == 0, low_guess, high_guess)
    for shift in range(1, n_pitch):
        got = lax.ppermute(sent, "pitch", [(0, shift), (n_pitch - 1, shift - 1)])
        low_wall = jnp.where(pitch_at == shift, got, low_wall)
        high_wall = jnp.where(pitch_at == shift - 1, got, high_wall)
    pitch_index = pitch_at * pitch_rows + jnp.arange(pitch_rows, dtype=jnp.int32)
    blend_row = (pitch_index.astype(jnp.float32) / (total_pitch - 1))[:, None]
    shift_field = (1.0 - blend_row) * low_wall[:, :, None, :] + blend_row * high_wall[:, :, None, :]
    moved_offset = node_offset + shift_field
    grid_field = jnp.concatenate([moved_offset, shift_field], 0)
    rim_width = 2
    grid_pad = padded_2(grid_field, (("pitch", 2), ("span", 1)), rim_width)
    first_pad = padded_2(flow_state, (("pitch", 2), ("span", 1)), rim_width)
    low_end = pitch_at == 0
    high_end = pitch_at == n_pitch - 1
    first_end = span_at == 0
    last_end = span_at == n_span - 1
    grid_pad = fill_ends(grid_pad, 1, rim_width, first_end, last_end)
    grid_pad = fill_ends(grid_pad, 2, 2, low_end, high_end)
    geo_terms, volume_old, volume_new = geometry(grid_pad)
    corr_low = lag_shift(lag_series[1], phase_now, -phase_lag)
    corr_high = lag_shift(lag_series[0], phase_now, phase_lag)
    padded = finish_flow(
        first_pad, 2, blade_flag, corr_low, corr_high, low_end, high_end, first_end, last_end
    )
    section_one = section_kernel(
        padded, geo_terms, volume_old, volume_new, flow_state, SECTION_WEIGHTS[0] * TIME_STEP
    )
    second_pad = padded_2(section_one, (("pitch", 2), ("span", 1)), 2)
    padded = finish_flow(
        second_pad, 2, blade_flag, corr_low, corr_high, low_end, high_end, first_end, last_end
    )
    current = section_kernel(
        padded, geo_terms, volume_old, volume_new, flow_state, SECTION_WEIGHTS[1] * TIME_STEP
    )
    return (current, moved_offset)


def solution(mesh):
    placed = (
        P(None, "span", "pitch", None),
        P(None, "span", "pitch", None),
        P(None, "span", None),
        P(),
        P(None, None, None, None, "span", None),
    )
    return jax.shard_map(
        per_device,
        mesh=mesh,
        in_specs=placed,
        out_specs=(P(None, "span", "pitch", None), P(None, "span", "pitch", None)),
        check_vma=False,
    )
```

```python
import jax
import jax.numpy as jnp
from jax import lax
from jax.sharding import PartitionSpec as P
from jax.experimental import pallas as pl
from jax.experimental.pallas import tpu as pltpu

HEAT_RATIO = 1.4
TIME_STEP = 0.25
DAMPING = 0.02
SECTION_WEIGHTS = (0.5, 1.0)


def broadcast(value, axis, root):
    mine = lax.axis_index(axis) == root
    return lax.psum(jnp.where(mine, value, jnp.zeros_like(value)), axis)


def padded_2(block, sides, width):
    for axis, dim in sides:
        count = lax.axis_size(axis)
        forward = [(i, i + 1) for i in range(count - 1)]
        forward.append((count - 1, 0))
        backward = [(target, source) for source, target in forward]
        low = lax.ppermute(
            lax.slice_in_dim(block, block.shape[dim] - width, None, axis=dim), axis, forward
        )
        high = lax.ppermute(lax.slice_in_dim(block, 0, width, axis=dim), axis, backward)
        block = jnp.concatenate([low, block, high], axis=dim)
    return block


def padded_cross(block, width):
    rims = []
    for axis, dim in (("pitch", 2), ("span", 1)):
        count = lax.axis_size(axis)
        forward = [(i, (i + 1) % count) for i in range(count)]
        backward = [(target, source) for source, target in forward]
        low = lax.ppermute(
            lax.slice_in_dim(block, block.shape[dim] - width, None, axis=dim), axis, forward
        )
        high = lax.ppermute(lax.slice_in_dim(block, 0, width, axis=dim), axis, backward)
        rims.append((low, high))
    (pitch_low, pitch_high), (span_low, span_high) = rims
    middle = jnp.concatenate([pitch_low, block, pitch_high], axis=2)
    corner = jnp.zeros(span_low.shape[:2] + (width,) + span_low.shape[3:], block.dtype)
    top = jnp.concatenate([corner, span_low, corner], axis=2)
    bottom = jnp.concatenate([corner, span_high, corner], axis=2)
    return jnp.concatenate([top, middle, bottom], axis=1)


def fill_ends(padded, axis_pos, depth, at_first, at_last):
    length = padded.shape[axis_pos]
    inner_first = lax.slice_in_dim(padded, depth, depth + 1, axis=axis_pos)
    inner_second = lax.slice_in_dim(padded, depth + 1, depth + 2, axis=axis_pos)
    inner_last = lax.slice_in_dim(padded, length - depth - 1, length - depth, axis=axis_pos)
    inner_before = lax.slice_in_dim(padded, length - depth - 2, length - depth - 1, axis=axis_pos)
    step_low = inner_first - inner_second
    step_high = inner_last - inner_before
    low_side = jnp.concatenate(
        [inner_first + float(count) * step_low for count in range(depth, 0, -1)], axis=axis_pos
    )
    high_side = jnp.concatenate(
        [inner_last + float(count) * step_high for count in range(1, depth + 1)], axis=axis_pos
    )
    low_side = jnp.where(at_first, low_side, lax.slice_in_dim(padded, 0, depth, axis=axis_pos))
    high_side = jnp.where(
        at_last, high_side, lax.slice_in_dim(padded, length - depth, length, axis=axis_pos)
    )
    return jnp.concatenate(
        [low_side, lax.slice_in_dim(padded, depth, length - depth, axis=axis_pos), high_side],
        axis=axis_pos,
    )


def radial_damping(values, axis_pos):
    count = values.shape[axis_pos]
    first_row = lax.slice_in_dim(values, 0, 1, axis=axis_pos)
    last_row = lax.slice_in_dim(values, count - 1, count, axis=axis_pos)
    extended = jnp.concatenate([first_row, first_row, values, last_row, last_row], axis=axis_pos)
    return (
        lax.slice_in_dim(extended, 4, 4 + count, axis=axis_pos)
        - 4.0 * lax.slice_in_dim(extended, 3, 3 + count, axis=axis_pos)
        + 6.0 * values
        - 4.0 * lax.slice_in_dim(extended, 1, 1 + count, axis=axis_pos)
        + lax.slice_in_dim(extended, 0, count, axis=axis_pos)
    )


def unit_normal(earlier, later):
    along_x = later[0] - earlier[0]
    along_y = 1.0 + later[1] - earlier[1]
    length = jnp.sqrt(along_x * along_x + along_y * along_y)
    return jnp.stack([along_x / length, along_y / length])


def wall_amplitude(shape_mode, angle, blade_mask):
    return (shape_mode[0] * jnp.cos(angle) - shape_mode[1] * jnp.sin(angle)) * blade_mask


def lag_shift(series, phase_now, phase_move):
    series_sum = jnp.zeros(series.shape[2:], jnp.float32)
    for number in range(series.shape[0]):
        harmonic = float(number + 1)
        change_cos = jnp.cos(harmonic * (phase_now + phase_move)) - jnp.cos(harmonic * phase_now)
        change_sin = jnp.sin(harmonic * (phase_now + phase_move)) - jnp.sin(harmonic * phase_now)
        series_sum = series_sum + series[number, 0] * change_cos - series[number, 1] * change_sin
    return series_sum


def metric_terms(offset_x, offset_y):
    x_zeta = 1.0 + (offset_x[2:, 1:-1] - offset_x[:-2, 1:-1]) * 0.5
    x_xi = (offset_x[1:-1, 2:] - offset_x[1:-1, :-2]) * 0.5
    y_xi = 1.0 + (offset_y[1:-1, 2:] - offset_y[1:-1, :-2]) * 0.5
    y_zeta = (offset_y[2:, 1:-1] - offset_y[:-2, 1:-1]) * 0.5
    return (x_zeta, x_xi, y_xi, y_zeta)


def geometry(grid_pad):
    x_zeta, x_xi, y_xi, y_zeta = metric_terms(grid_pad[0], grid_pad[1])
    old_zeta, old_xi, oldy_xi, oldy_zeta = metric_terms(
        grid_pad[0] - grid_pad[2], grid_pad[1] - grid_pad[3]
    )
    volume_new = (x_zeta * y_xi - x_xi * y_zeta)[1:-1, 1:-1]
    volume_old = (old_zeta * oldy_xi - old_xi * oldy_zeta)[1:-1, 1:-1]
    speed_x = grid_pad[2][1:-1, 1:-1] / TIME_STEP
    speed_y = grid_pad[3][1:-1, 1:-1] / TIME_STEP
    first_pitch = -y_zeta
    sweep_pitch = first_pitch * speed_x + x_zeta * speed_y
    second_axial = -x_xi
    sweep_axial = y_xi * speed_x + second_axial * speed_y
    return (
        (first_pitch, x_zeta, sweep_pitch, y_xi, second_axial, sweep_axial),
        volume_old,
        volume_new,
    )


def directional(strip_cells, first_coef, second_coef, sweep_term):
    density = strip_cells[0]
    vel_x = strip_cells[1] / density
    vel_y = strip_cells[2] / density
    energy = strip_cells[3]
    pressure = (HEAT_RATIO - 1.0) * (energy - 0.5 * density * (vel_x * vel_x + vel_y * vel_y))
    flux_x = jnp.stack(
        [
            strip_cells[1],
            strip_cells[1] * vel_x + pressure,
            strip_cells[1] * vel_y,
            (energy + pressure) * vel_x,
        ]
    )
    flux_y = jnp.stack(
        [
            strip_cells[2],
            strip_cells[2] * vel_x,
            strip_cells[2] * vel_y + pressure,
            (energy + pressure) * vel_y,
        ]
    )
    return first_coef * flux_x + second_coef * flux_y - sweep_term * strip_cells


def residual(padded, geo_terms):
    first_pitch, second_pitch, sweep_pitch, first_axial, second_axial, sweep_axial = geo_terms
    pitch_flux = directional(
        padded[:, 2:-2, 1:-1], first_pitch[1:-1], second_pitch[1:-1], sweep_pitch[1:-1]
    )
    axial_flux = directional(
        padded[:, 1:-1, 2:-2], first_axial[:, 1:-1], second_axial[:, 1:-1], sweep_axial[:, 1:-1]
    )
    divergence = (pitch_flux[:, :, 2:] - pitch_flux[:, :, :-2]) * 0.5 + (
        axial_flux[:, 2:] - axial_flux[:, :-2]
    ) * 0.5
    centre = padded[:, 2:-2, 2:-2]
    fourth = (
        padded[:, 2:-2, 4:]
        - 4.0 * padded[:, 2:-2, 3:-1]
        + 6.0 * centre
        - 4.0 * padded[:, 2:-2, 1:-3]
        + padded[:, 2:-2, :-4]
        + (
            padded[:, 4:, 2:-2]
            - 4.0 * padded[:, 3:-1, 2:-2]
            + 6.0 * centre
            - 4.0 * padded[:, 1:-3, 2:-2]
            + padded[:, :-4, 2:-2]
        )
    )
    return divergence + DAMPING * fourth + DAMPING * radial_damping(centre, 3)


def flow_ghosts(
    row_zero,
    row_one,
    row_last,
    row_before,
    wrap_low0,
    wrap_low1,
    wrap_high0,
    wrap_high1,
    blade_flag,
    corr_low,
    corr_high,
):
    sign_flip = jnp.array([1.0, 1.0, -1.0, 1.0], jnp.float32).reshape(
        (4,) + (1,) * (row_zero.ndim - 1)
    )
    ghost_m2 = jnp.where(blade_flag, row_one * sign_flip, wrap_low0 + corr_low)
    ghost_m1 = jnp.where(blade_flag, row_zero * sign_flip, wrap_low1 + corr_low)
    ghost_p0 = jnp.where(blade_flag, row_last * sign_flip, wrap_high0 + corr_high)
    ghost_p1 = jnp.where(blade_flag, row_before * sign_flip, wrap_high1 + corr_high)
    return (ghost_m2, ghost_m1, ghost_p0, ghost_p1)


def finish_flow(
    padded, depth, row_flag, corr_low, corr_high, low_end, high_end, first_end, last_end
):
    middle_rows = padded[:, 2:-2]
    width = middle_rows.shape[2]
    ghost_m2, ghost_m1, ghost_p0, ghost_p1 = flow_ghosts(
        middle_rows[:, :, 2],
        middle_rows[:, :, 3],
        middle_rows[:, :, width - 3],
        middle_rows[:, :, width - 4],
        middle_rows[:, :, 0],
        middle_rows[:, :, 1],
        middle_rows[:, :, width - 2],
        middle_rows[:, :, width - 1],
        row_flag[:, None],
        corr_low,
        corr_high,
    )
    low_pair = jnp.where(low_end, jnp.stack([ghost_m2, ghost_m1], 2), middle_rows[:, :, 0:2])
    high_pair = jnp.where(
        high_end, jnp.stack([ghost_p0, ghost_p1], 2), middle_rows[:, :, width - 2 :]
    )
    middle_rows = jnp.concatenate([low_pair, middle_rows[:, :, 2 : width - 2], high_pair], 2)
    whole = jnp.concatenate([padded[:, 0:2], middle_rows, padded[:, -2:]], 1)
    top_copy = jnp.repeat(whole[:, depth : depth + 1], depth, axis=1)
    bottom_copy = jnp.repeat(whole[:, -depth - 1 : -depth], depth, axis=1)
    top_rows = jnp.where(first_end, top_copy, whole[:, :depth])
    bottom_rows = jnp.where(last_end, bottom_copy, whole[:, -depth:])
    return jnp.concatenate([top_rows, whole[:, depth:-depth], bottom_rows], 1)


def _flux(rho, mx, my, en, first, second, sweep):
    u = mx / rho
    v = my / rho
    pr = (HEAT_RATIO - 1.0) * (en - 0.5 * rho * (u * u + v * v))
    ep = en + pr
    return (
        first * mx + second * my - sweep * rho,
        first * (mx * u + pr) + second * (my * u) - sweep * mx,
        first * (mx * v) + second * (my * v + pr) - sweep * my,
        first * (ep * u) + second * (ep * v) - sweep * en,
    )


def _radial(c0, lane, forward):
    width = c0.shape[-1]
    last = width - 1

    def down(x):
        a = pltpu.roll(x, 1, 1)
        b = pltpu.roll(x, last, 1)
        return jnp.where(forward, a, b)

    def up(x):
        a = pltpu.roll(x, 1, 1)
        b = pltpu.roll(x, last, 1)
        return jnp.where(forward, b, a)

    m1 = jnp.where(lane == 0, c0, down(c0))
    p1 = jnp.where(lane == last, c0, up(c0))
    m2 = jnp.where(lane == 0, c0, down(m1))
    p2 = jnp.where(lane == last, c0, up(p1))
    return p2 - 4.0 * p1 + 6.0 * c0 - 4.0 * m1 + m2


def _section_body(scale, pad, fp, sp, wp, fa, sa, wa, vold, vnew, q0, out, af, pf):
    na = out.shape[1]
    npch = out.shape[2]
    width = out.shape[3]

    def axial_row(j, carry):
        q = [pad[k, j + 1, 2 : npch + 2] for k in range(4)]
        f = _flux(*q, fa[j, 1 : npch + 1], sa[j, 1 : npch + 1], wa[j, 1 : npch + 1])
        for k in range(4):
            af[k, j] = f[k]
        return carry

    lax.fori_loop(0, na + 2, axial_row, 0)
    lane = lax.broadcasted_iota(jnp.int32, (npch, width), 1)
    probe = pltpu.roll(lane, 1, 1)
    forward = probe == jnp.where(lane == 0, width - 1, lane - 1)

    def row(a, carry):
        q = [pad[k, a + 2, 1 : npch + 3] for k in range(4)]
        f = _flux(*q, fp[a + 1], sp[a + 1], wp[a + 1])
        for k in range(4):
            pf[k] = f[k]
        volume_old = vold[a]
        volume_new = vnew[a]
        for k in range(4):
            div = (pf[k, 2 : npch + 2] - pf[k, 0:npch]) * 0.5 + (af[k, a + 2] - af[k, a]) * 0.5
            c0 = pad[k, a + 2, 2 : npch + 2]
            fourth = (
                pad[k, a + 2, 4 : npch + 4]
                - 4.0 * pad[k, a + 2, 3 : npch + 3]
                + 6.0 * c0
                - 4.0 * pad[k, a + 2, 1 : npch + 1]
                + pad[k, a + 2, 0:npch]
            ) + (
                pad[k, a + 4, 2 : npch + 2]
                - 4.0 * pad[k, a + 3, 2 : npch + 2]
                + 6.0 * c0
                - 4.0 * pad[k, a + 1, 2 : npch + 2]
                + pad[k, a, 2 : npch + 2]
            )
            res = div + DAMPING * fourth + DAMPING * _radial(c0, lane, forward)
            out[k, a] = (volume_old * q0[k, a] - scale * res) / volume_new
        return carry

    lax.fori_loop(0, na, row, 0)


def section_kernel(padded, geo_terms, volume_old, volume_new, start, scale, interpret=False):
    _, na, npch, width = start.shape
    body = lambda *refs: _section_body(scale, *refs)
    cells = na * npch * width
    return pl.pallas_call(
        body,
        out_shape=jax.ShapeDtypeStruct(start.shape, start.dtype),
        scratch_shapes=[
            pltpu.VMEM((4, na + 2, npch, width), jnp.float32),
            pltpu.VMEM((4, npch + 2, width), jnp.float32),
        ],
        compiler_params=pltpu.CompilerParams(vmem_limit_bytes=60 * 1024 * 1024),
        cost_estimate=pl.CostEstimate(
            flops=400 * cells, transcendentals=0, bytes_accessed=4 * 20 * cells
        ),
        interpret=interpret,
    )(padded, *geo_terms, volume_old, volume_new, start)


def per_device(flow_state, node_offset, blade_mode, phase_angles, lag_series):
    n_pitch = lax.axis_size("pitch")
    n_span = lax.axis_size("span")
    pitch_rows = flow_state.shape[2]
    axial_cols = flow_state.shape[1]
    total_pitch = pitch_rows * n_pitch
    total_axial = axial_cols * n_span
    pitch_at = lax.axis_index("pitch")
    span_at = lax.axis_index("span")
    lead_edge = total_axial // 4
    axial_index = span_at * axial_cols + jnp.arange(axial_cols, dtype=jnp.int32)
    blade_flag = (axial_index >= lead_edge) & (axial_index < total_axial - lead_edge)
    blade_mask = blade_flag.astype(jnp.float32)[:, None]
    phase_now = phase_angles[0]
    phase_lag = phase_angles[1]
    low_guess = wall_amplitude(blade_mode, phase_now, blade_mask) * unit_normal(
        node_offset[:, :, 0], node_offset[:, :, 1]
    )
    high_guess = wall_amplitude(blade_mode, phase_now + phase_lag, blade_mask) * unit_normal(
        node_offset[:, :, pitch_rows - 2], node_offset[:, :, pitch_rows - 1]
    )
    low_wall = low_guess
    high_wall = high_guess
    sent = jnp.where(pitch_at == 0, low_guess, high_guess)
    for shift in range(1, n_pitch):
        got = lax.ppermute(sent, "pitch", [(0, shift), (n_pitch - 1, shift - 1)])
        low_wall = jnp.where(pitch_at == shift, got, low_wall)
        high_wall = jnp.where(pitch_at == shift - 1, got, high_wall)
    pitch_index = pitch_at * pitch_rows + jnp.arange(pitch_rows, dtype=jnp.int32)
    blend_row = (pitch_index.astype(jnp.float32) / (total_pitch - 1))[:, None]
    shift_field = (1.0 - blend_row) * low_wall[:, :, None, :] + blend_row * high_wall[:, :, None, :]
    moved_offset = node_offset + shift_field
    grid_field = jnp.concatenate([moved_offset, shift_field], 0)
    rim_width = 2
    both_pad = padded_2(
        jnp.concatenate([grid_field, flow_state], 0), (("pitch", 2), ("span", 1)), rim_width
    )
    grid_pad = both_pad[:4]
    first_pad = both_pad[4:]
    low_end = pitch_at == 0
    high_end = pitch_at == n_pitch - 1
    first_end = span_at == 0
    last_end = span_at == n_span - 1
    grid_pad = fill_ends(grid_pad, 1, rim_width, first_end, last_end)
    grid_pad = fill_ends(grid_pad, 2, 2, low_end, high_end)
    geo_terms, volume_old, volume_new = geometry(grid_pad)
    corr_low = lag_shift(lag_series[1], phase_now, -phase_lag)
    corr_high = lag_shift(lag_series[0], phase_now, phase_lag)
    padded = finish_flow(
        first_pad, 2, blade_flag, corr_low, corr_high, low_end, high_end, first_end, last_end
    )
    section_one = section_kernel(
        padded, geo_terms, volume_old, volume_new, flow_state, SECTION_WEIGHTS[0] * TIME_STEP
    )
    second_pad = padded_cross(section_one, 2)
    padded = finish_flow(
        second_pad, 2, blade_flag, corr_low, corr_high, low_end, high_end, first_end, last_end
    )
    current = section_kernel(
        padded, geo_terms, volume_old, volume_new, flow_state, SECTION_WEIGHTS[1] * TIME_STEP
    )
    return (current, moved_offset)


def solution(mesh):
    placed = (
        P(None, "span", "pitch", None),
        P(None, "span", "pitch", None),
        P(None, "span", None),
        P(),
        P(None, None, None, None, "span", None),
    )
    return jax.shard_map(
        per_device,
        mesh=mesh,
        in_specs=placed,
        out_specs=(P(None, "span", "pitch", None), P(None, "span", "pitch", None)),
        check_vma=False,
    )
```

```python
import jax
import jax.numpy as jnp
from jax import lax
from jax.sharding import PartitionSpec as P
from jax.experimental import pallas as pl
from jax.experimental.pallas import tpu as pltpu

HEAT_RATIO = 1.4
TIME_STEP = 0.25
DAMPING = 0.02
SECTION_WEIGHTS = (0.5, 1.0)


def broadcast(value, axis, root):
    mine = lax.axis_index(axis) == root
    return lax.psum(jnp.where(mine, value, jnp.zeros_like(value)), axis)


def padded_2(block, sides, width):
    for axis, dim in sides:
        count = lax.axis_size(axis)
        forward = [(i, i + 1) for i in range(count - 1)]
        forward.append((count - 1, 0))
        backward = [(target, source) for source, target in forward]
        low = lax.ppermute(
            lax.slice_in_dim(block, block.shape[dim] - width, None, axis=dim), axis, forward
        )
        high = lax.ppermute(lax.slice_in_dim(block, 0, width, axis=dim), axis, backward)
        block = jnp.concatenate([low, block, high], axis=dim)
    return block


def padded_cross(block, width):
    rims = []
    for axis, dim in (("pitch", 2), ("span", 1)):
        count = lax.axis_size(axis)
        forward = [(i, (i + 1) % count) for i in range(count)]
        backward = [(target, source) for source, target in forward]
        low = lax.ppermute(
            lax.slice_in_dim(block, block.shape[dim] - width, None, axis=dim), axis, forward
        )
        high = lax.ppermute(lax.slice_in_dim(block, 0, width, axis=dim), axis, backward)
        rims.append((low, high))
    (pitch_low, pitch_high), (span_low, span_high) = rims
    middle = jnp.concatenate([pitch_low, block, pitch_high], axis=2)
    corner = jnp.zeros(span_low.shape[:2] + (width,) + span_low.shape[3:], block.dtype)
    top = jnp.concatenate([corner, span_low, corner], axis=2)
    bottom = jnp.concatenate([corner, span_high, corner], axis=2)
    return jnp.concatenate([top, middle, bottom], axis=1)


def fill_ends(padded, axis_pos, depth, at_first, at_last):
    length = padded.shape[axis_pos]
    inner_first = lax.slice_in_dim(padded, depth, depth + 1, axis=axis_pos)
    inner_second = lax.slice_in_dim(padded, depth + 1, depth + 2, axis=axis_pos)
    inner_last = lax.slice_in_dim(padded, length - depth - 1, length - depth, axis=axis_pos)
    inner_before = lax.slice_in_dim(padded, length - depth - 2, length - depth - 1, axis=axis_pos)
    step_low = inner_first - inner_second
    step_high = inner_last - inner_before
    low_side = jnp.concatenate(
        [inner_first + float(count) * step_low for count in range(depth, 0, -1)], axis=axis_pos
    )
    high_side = jnp.concatenate(
        [inner_last + float(count) * step_high for count in range(1, depth + 1)], axis=axis_pos
    )
    low_side = jnp.where(at_first, low_side, lax.slice_in_dim(padded, 0, depth, axis=axis_pos))
    high_side = jnp.where(
        at_last, high_side, lax.slice_in_dim(padded, length - depth, length, axis=axis_pos)
    )
    return jnp.concatenate(
        [low_side, lax.slice_in_dim(padded, depth, length - depth, axis=axis_pos), high_side],
        axis=axis_pos,
    )


def radial_damping(values, axis_pos):
    count = values.shape[axis_pos]
    first_row = lax.slice_in_dim(values, 0, 1, axis=axis_pos)
    last_row = lax.slice_in_dim(values, count - 1, count, axis=axis_pos)
    extended = jnp.concatenate([first_row, first_row, values, last_row, last_row], axis=axis_pos)
    return (
        lax.slice_in_dim(extended, 4, 4 + count, axis=axis_pos)
        - 4.0 * lax.slice_in_dim(extended, 3, 3 + count, axis=axis_pos)
        + 6.0 * values
        - 4.0 * lax.slice_in_dim(extended, 1, 1 + count, axis=axis_pos)
        + lax.slice_in_dim(extended, 0, count, axis=axis_pos)
    )


def unit_normal(earlier, later):
    along_x = later[0] - earlier[0]
    along_y = 1.0 + later[1] - earlier[1]
    length = jnp.sqrt(along_x * along_x + along_y * along_y)
    return jnp.stack([along_x / length, along_y / length])


def wall_amplitude(shape_mode, angle, blade_mask):
    return (shape_mode[0] * jnp.cos(angle) - shape_mode[1] * jnp.sin(angle)) * blade_mask


def lag_shift(series, phase_now, phase_move):
    series_sum = jnp.zeros(series.shape[2:], jnp.float32)
    for number in range(series.shape[0]):
        harmonic = float(number + 1)
        change_cos = jnp.cos(harmonic * (phase_now + phase_move)) - jnp.cos(harmonic * phase_now)
        change_sin = jnp.sin(harmonic * (phase_now + phase_move)) - jnp.sin(harmonic * phase_now)
        series_sum = series_sum + series[number, 0] * change_cos - series[number, 1] * change_sin
    return series_sum


def metric_terms(offset_x, offset_y):
    x_zeta = 1.0 + (offset_x[2:, 1:-1] - offset_x[:-2, 1:-1]) * 0.5
    x_xi = (offset_x[1:-1, 2:] - offset_x[1:-1, :-2]) * 0.5
    y_xi = 1.0 + (offset_y[1:-1, 2:] - offset_y[1:-1, :-2]) * 0.5
    y_zeta = (offset_y[2:, 1:-1] - offset_y[:-2, 1:-1]) * 0.5
    return (x_zeta, x_xi, y_xi, y_zeta)


def geometry(grid_pad):
    x_zeta, x_xi, y_xi, y_zeta = metric_terms(grid_pad[0], grid_pad[1])
    old_zeta, old_xi, oldy_xi, oldy_zeta = metric_terms(
        grid_pad[0] - grid_pad[2], grid_pad[1] - grid_pad[3]
    )
    volume_new = (x_zeta * y_xi - x_xi * y_zeta)[1:-1, 1:-1]
    volume_old = (old_zeta * oldy_xi - old_xi * oldy_zeta)[1:-1, 1:-1]
    speed_x = grid_pad[2][1:-1, 1:-1] / TIME_STEP
    speed_y = grid_pad[3][1:-1, 1:-1] / TIME_STEP
    first_pitch = -y_zeta
    sweep_pitch = first_pitch * speed_x + x_zeta * speed_y
    second_axial = -x_xi
    sweep_axial = y_xi * speed_x + second_axial * speed_y
    return (
        (first_pitch, x_zeta, sweep_pitch, y_xi, second_axial, sweep_axial),
        volume_old,
        volume_new,
    )


def directional(strip_cells, first_coef, second_coef, sweep_term):
    density = strip_cells[0]
    vel_x = strip_cells[1] / density
    vel_y = strip_cells[2] / density
    energy = strip_cells[3]
    pressure = (HEAT_RATIO - 1.0) * (energy - 0.5 * density * (vel_x * vel_x + vel_y * vel_y))
    flux_x = jnp.stack(
        [
            strip_cells[1],
            strip_cells[1] * vel_x + pressure,
            strip_cells[1] * vel_y,
            (energy + pressure) * vel_x,
        ]
    )
    flux_y = jnp.stack(
        [
            strip_cells[2],
            strip_cells[2] * vel_x,
            strip_cells[2] * vel_y + pressure,
            (energy + pressure) * vel_y,
        ]
    )
    return first_coef * flux_x + second_coef * flux_y - sweep_term * strip_cells


def residual(padded, geo_terms):
    first_pitch, second_pitch, sweep_pitch, first_axial, second_axial, sweep_axial = geo_terms
    pitch_flux = directional(
        padded[:, 2:-2, 1:-1], first_pitch[1:-1], second_pitch[1:-1], sweep_pitch[1:-1]
    )
    axial_flux = directional(
        padded[:, 1:-1, 2:-2], first_axial[:, 1:-1], second_axial[:, 1:-1], sweep_axial[:, 1:-1]
    )
    divergence = (pitch_flux[:, :, 2:] - pitch_flux[:, :, :-2]) * 0.5 + (
        axial_flux[:, 2:] - axial_flux[:, :-2]
    ) * 0.5
    centre = padded[:, 2:-2, 2:-2]
    fourth = (
        padded[:, 2:-2, 4:]
        - 4.0 * padded[:, 2:-2, 3:-1]
        + 6.0 * centre
        - 4.0 * padded[:, 2:-2, 1:-3]
        + padded[:, 2:-2, :-4]
        + (
            padded[:, 4:, 2:-2]
            - 4.0 * padded[:, 3:-1, 2:-2]
            + 6.0 * centre
            - 4.0 * padded[:, 1:-3, 2:-2]
            + padded[:, :-4, 2:-2]
        )
    )
    return divergence + DAMPING * fourth + DAMPING * radial_damping(centre, 3)


def flow_ghosts(
    row_zero,
    row_one,
    row_last,
    row_before,
    wrap_low0,
    wrap_low1,
    wrap_high0,
    wrap_high1,
    blade_flag,
    corr_low,
    corr_high,
):
    sign_flip = jnp.array([1.0, 1.0, -1.0, 1.0], jnp.float32).reshape(
        (4,) + (1,) * (row_zero.ndim - 1)
    )
    ghost_m2 = jnp.where(blade_flag, row_one * sign_flip, wrap_low0 + corr_low)
    ghost_m1 = jnp.where(blade_flag, row_zero * sign_flip, wrap_low1 + corr_low)
    ghost_p0 = jnp.where(blade_flag, row_last * sign_flip, wrap_high0 + corr_high)
    ghost_p1 = jnp.where(blade_flag, row_before * sign_flip, wrap_high1 + corr_high)
    return (ghost_m2, ghost_m1, ghost_p0, ghost_p1)


def finish_flow(
    padded, depth, row_flag, corr_low, corr_high, low_end, high_end, first_end, last_end
):
    middle_rows = padded[:, 2:-2]
    width = middle_rows.shape[2]
    ghost_m2, ghost_m1, ghost_p0, ghost_p1 = flow_ghosts(
        middle_rows[:, :, 2],
        middle_rows[:, :, 3],
        middle_rows[:, :, width - 3],
        middle_rows[:, :, width - 4],
        middle_rows[:, :, 0],
        middle_rows[:, :, 1],
        middle_rows[:, :, width - 2],
        middle_rows[:, :, width - 1],
        row_flag[:, None],
        corr_low,
        corr_high,
    )
    low_pair = jnp.where(low_end, jnp.stack([ghost_m2, ghost_m1], 2), middle_rows[:, :, 0:2])
    high_pair = jnp.where(
        high_end, jnp.stack([ghost_p0, ghost_p1], 2), middle_rows[:, :, width - 2 :]
    )
    middle_rows = jnp.concatenate([low_pair, middle_rows[:, :, 2 : width - 2], high_pair], 2)
    whole = jnp.concatenate([padded[:, 0:2], middle_rows, padded[:, -2:]], 1)
    top_copy = jnp.repeat(whole[:, depth : depth + 1], depth, axis=1)
    bottom_copy = jnp.repeat(whole[:, -depth - 1 : -depth], depth, axis=1)
    top_rows = jnp.where(first_end, top_copy, whole[:, :depth])
    bottom_rows = jnp.where(last_end, bottom_copy, whole[:, -depth:])
    return jnp.concatenate([top_rows, whole[:, depth:-depth], bottom_rows], 1)


def _flux(rho, mx, my, en, first, second, sweep):
    u = mx / rho
    v = my / rho
    pr = (HEAT_RATIO - 1.0) * (en - 0.5 * rho * (u * u + v * v))
    ep = en + pr
    return (
        first * mx + second * my - sweep * rho,
        first * (mx * u + pr) + second * (my * u) - sweep * mx,
        first * (mx * v) + second * (my * v + pr) - sweep * my,
        first * (ep * u) + second * (ep * v) - sweep * en,
    )


def _radial(c0, lane, forward):
    width = c0.shape[-1]
    last = width - 1

    def down(x):
        a = pltpu.roll(x, 1, 1)
        b = pltpu.roll(x, last, 1)
        return jnp.where(forward, a, b)

    def up(x):
        a = pltpu.roll(x, 1, 1)
        b = pltpu.roll(x, last, 1)
        return jnp.where(forward, b, a)

    m1 = jnp.where(lane == 0, c0, down(c0))
    p1 = jnp.where(lane == last, c0, up(c0))
    m2 = jnp.where(lane == 0, c0, down(m1))
    p2 = jnp.where(lane == last, c0, up(p1))
    return p2 - 4.0 * p1 + 6.0 * c0 - 4.0 * m1 + m2


def _section_body(scale, pad, fp, sp, wp, fa, sa, wa, vold, vnew, q0, out, af, pf):
    na = out.shape[1]
    npch = out.shape[2]
    width = out.shape[3]

    def axial_row(j, carry):
        q = [pad[k, j + 1, 2 : npch + 2] for k in range(4)]
        f = _flux(*q, fa[j, 1 : npch + 1], sa[j, 1 : npch + 1], wa[j, 1 : npch + 1])
        for k in range(4):
            af[k, j] = f[k]
        return carry

    lax.fori_loop(0, na + 2, axial_row, 0)
    lane = lax.broadcasted_iota(jnp.int32, (npch, width), 1)
    probe = pltpu.roll(lane, 1, 1)
    forward = probe == jnp.where(lane == 0, width - 1, lane - 1)

    def row(a, carry):
        q = [pad[k, a + 2, 1 : npch + 3] for k in range(4)]
        f = _flux(*q, fp[a + 1], sp[a + 1], wp[a + 1])
        for k in range(4):
            pf[k] = f[k]
        volume_old = vold[a]
        volume_new = vnew[a]
        for k in range(4):
            div = (pf[k, 2 : npch + 2] - pf[k, 0:npch]) * 0.5 + (af[k, a + 2] - af[k, a]) * 0.5
            c0 = pad[k, a + 2, 2 : npch + 2]
            fourth = (
                pad[k, a + 2, 4 : npch + 4]
                - 4.0 * pad[k, a + 2, 3 : npch + 3]
                + 6.0 * c0
                - 4.0 * pad[k, a + 2, 1 : npch + 1]
                + pad[k, a + 2, 0:npch]
            ) + (
                pad[k, a + 4, 2 : npch + 2]
                - 4.0 * pad[k, a + 3, 2 : npch + 2]
                + 6.0 * c0
                - 4.0 * pad[k, a + 1, 2 : npch + 2]
                + pad[k, a, 2 : npch + 2]
            )
            res = div + DAMPING * fourth + DAMPING * _radial(c0, lane, forward)
            out[k, a] = (volume_old * q0[k, a] - scale * res) / volume_new
        return carry

    lax.fori_loop(0, na, row, 0)


def section_kernel(padded, geo_terms, volume_old, volume_new, start, scale, interpret=False):
    _, na, npch, width = start.shape
    body = lambda *refs: _section_body(scale, *refs)
    cells = na * npch * width
    return pl.pallas_call(
        body,
        out_shape=jax.ShapeDtypeStruct(start.shape, start.dtype),
        scratch_shapes=[
            pltpu.VMEM((4, na + 2, npch, width), jnp.float32),
            pltpu.VMEM((4, npch + 2, width), jnp.float32),
        ],
        compiler_params=pltpu.CompilerParams(vmem_limit_bytes=60 * 1024 * 1024),
        cost_estimate=pl.CostEstimate(
            flops=400 * cells, transcendentals=0, bytes_accessed=4 * 20 * cells
        ),
        interpret=interpret,
    )(padded, *geo_terms, volume_old, volume_new, start)


def per_device(flow_state, node_offset, blade_mode, phase_angles, lag_series):
    n_pitch = lax.axis_size("pitch")
    n_span = lax.axis_size("span")
    pitch_rows = flow_state.shape[2]
    axial_cols = flow_state.shape[1]
    total_pitch = pitch_rows * n_pitch
    total_axial = axial_cols * n_span
    pitch_at = lax.axis_index("pitch")
    span_at = lax.axis_index("span")
    lead_edge = total_axial // 4
    axial_index = span_at * axial_cols + jnp.arange(axial_cols, dtype=jnp.int32)
    blade_flag = (axial_index >= lead_edge) & (axial_index < total_axial - lead_edge)
    blade_mask = blade_flag.astype(jnp.float32)[:, None]
    phase_now = phase_angles[0]
    phase_lag = phase_angles[1]
    low_guess = wall_amplitude(blade_mode, phase_now, blade_mask) * unit_normal(
        node_offset[:, :, 0], node_offset[:, :, 1]
    )
    high_guess = wall_amplitude(blade_mode, phase_now + phase_lag, blade_mask) * unit_normal(
        node_offset[:, :, pitch_rows - 2], node_offset[:, :, pitch_rows - 1]
    )
    low_wall = low_guess
    high_wall = high_guess
    sent = jnp.where(pitch_at == 0, low_guess, high_guess)
    for shift in range(1, n_pitch):
        got = lax.ppermute(sent, "pitch", [(0, shift), (n_pitch - 1, shift - 1)])
        low_wall = jnp.where(pitch_at == shift, got, low_wall)
        high_wall = jnp.where(pitch_at == shift - 1, got, high_wall)
    pitch_index = pitch_at * pitch_rows + jnp.arange(pitch_rows, dtype=jnp.int32)
    blend_row = (pitch_index.astype(jnp.float32) / (total_pitch - 1))[:, None]
    shift_field = (1.0 - blend_row) * low_wall[:, :, None, :] + blend_row * high_wall[:, :, None, :]
    moved_offset = node_offset + shift_field
    grid_field = jnp.concatenate([moved_offset, shift_field], 0)
    rim_width = 2
    grid_pad = padded_2(grid_field, (("pitch", 2), ("span", 1)), rim_width)
    first_pad = padded_cross(flow_state, rim_width)
    low_end = pitch_at == 0
    high_end = pitch_at == n_pitch - 1
    first_end = span_at == 0
    last_end = span_at == n_span - 1
    grid_pad = fill_ends(grid_pad, 1, rim_width, first_end, last_end)
    grid_pad = fill_ends(grid_pad, 2, 2, low_end, high_end)
    geo_terms, volume_old, volume_new = geometry(grid_pad)
    corr_low = lag_shift(lag_series[1], phase_now, -phase_lag)
    corr_high = lag_shift(lag_series[0], phase_now, phase_lag)
    padded = finish_flow(
        first_pad, 2, blade_flag, corr_low, corr_high, low_end, high_end, first_end, last_end
    )
    section_one = section_kernel(
        padded, geo_terms, volume_old, volume_new, flow_state, SECTION_WEIGHTS[0] * TIME_STEP
    )
    second_pad = padded_cross(section_one, 2)
    padded = finish_flow(
        second_pad, 2, blade_flag, corr_low, corr_high, low_end, high_end, first_end, last_end
    )
    current = section_kernel(
        padded, geo_terms, volume_old, volume_new, flow_state, SECTION_WEIGHTS[1] * TIME_STEP
    )
    return (current, moved_offset)


def solution(mesh):
    placed = (
        P(None, "span", "pitch", None),
        P(None, "span", "pitch", None),
        P(None, "span", None),
        P(),
        P(None, None, None, None, "span", None),
    )
    return jax.shard_map(
        per_device,
        mesh=mesh,
        in_specs=placed,
        out_specs=(P(None, "span", "pitch", None), P(None, "span", "pitch", None)),
        check_vma=False,
    )
```

```python
import jax
import jax.numpy as jnp
from jax import lax
from jax.sharding import PartitionSpec as P
from jax.experimental import pallas as pl
from jax.experimental.pallas import tpu as pltpu

HEAT_RATIO = 1.4
TIME_STEP = 0.25
DAMPING = 0.02
SECTION_WEIGHTS = (0.5, 1.0)


def broadcast(value, axis, root):
    mine = lax.axis_index(axis) == root
    return lax.psum(jnp.where(mine, value, jnp.zeros_like(value)), axis)


def padded_2(block, sides, width):
    for axis, dim in sides:
        count = lax.axis_size(axis)
        forward = [(i, i + 1) for i in range(count - 1)]
        forward.append((count - 1, 0))
        backward = [(target, source) for source, target in forward]
        low = lax.ppermute(
            lax.slice_in_dim(block, block.shape[dim] - width, None, axis=dim), axis, forward
        )
        high = lax.ppermute(lax.slice_in_dim(block, 0, width, axis=dim), axis, backward)
        block = jnp.concatenate([low, block, high], axis=dim)
    return block


def padded_cross(block, width):
    rims = []
    for axis, dim in (("pitch", 2), ("span", 1)):
        count = lax.axis_size(axis)
        forward = [(i, (i + 1) % count) for i in range(count)]
        backward = [(target, source) for source, target in forward]
        low = lax.ppermute(
            lax.slice_in_dim(block, block.shape[dim] - width, None, axis=dim), axis, forward
        )
        high = lax.ppermute(lax.slice_in_dim(block, 0, width, axis=dim), axis, backward)
        rims.append((low, high))
    (pitch_low, pitch_high), (span_low, span_high) = rims
    middle = jnp.concatenate([pitch_low, block, pitch_high], axis=2)
    corner = jnp.zeros(span_low.shape[:2] + (width,) + span_low.shape[3:], block.dtype)
    top = jnp.concatenate([corner, span_low, corner], axis=2)
    bottom = jnp.concatenate([corner, span_high, corner], axis=2)
    return jnp.concatenate([top, middle, bottom], axis=1)


def fill_ends(padded, axis_pos, depth, at_first, at_last):
    length = padded.shape[axis_pos]
    inner_first = lax.slice_in_dim(padded, depth, depth + 1, axis=axis_pos)
    inner_second = lax.slice_in_dim(padded, depth + 1, depth + 2, axis=axis_pos)
    inner_last = lax.slice_in_dim(padded, length - depth - 1, length - depth, axis=axis_pos)
    inner_before = lax.slice_in_dim(padded, length - depth - 2, length - depth - 1, axis=axis_pos)
    step_low = inner_first - inner_second
    step_high = inner_last - inner_before
    low_side = jnp.concatenate(
        [inner_first + float(count) * step_low for count in range(depth, 0, -1)], axis=axis_pos
    )
    high_side = jnp.concatenate(
        [inner_last + float(count) * step_high for count in range(1, depth + 1)], axis=axis_pos
    )
    low_side = jnp.where(at_first, low_side, lax.slice_in_dim(padded, 0, depth, axis=axis_pos))
    high_side = jnp.where(
        at_last, high_side, lax.slice_in_dim(padded, length - depth, length, axis=axis_pos)
    )
    return jnp.concatenate(
        [low_side, lax.slice_in_dim(padded, depth, length - depth, axis=axis_pos), high_side],
        axis=axis_pos,
    )


def radial_damping(values, axis_pos):
    count = values.shape[axis_pos]
    first_row = lax.slice_in_dim(values, 0, 1, axis=axis_pos)
    last_row = lax.slice_in_dim(values, count - 1, count, axis=axis_pos)
    extended = jnp.concatenate([first_row, first_row, values, last_row, last_row], axis=axis_pos)
    return (
        lax.slice_in_dim(extended, 4, 4 + count, axis=axis_pos)
        - 4.0 * lax.slice_in_dim(extended, 3, 3 + count, axis=axis_pos)
        + 6.0 * values
        - 4.0 * lax.slice_in_dim(extended, 1, 1 + count, axis=axis_pos)
        + lax.slice_in_dim(extended, 0, count, axis=axis_pos)
    )


def unit_normal(earlier, later):
    along_x = later[0] - earlier[0]
    along_y = 1.0 + later[1] - earlier[1]
    length = jnp.sqrt(along_x * along_x + along_y * along_y)
    return jnp.stack([along_x / length, along_y / length])


def wall_amplitude(shape_mode, angle, blade_mask):
    return (shape_mode[0] * jnp.cos(angle) - shape_mode[1] * jnp.sin(angle)) * blade_mask


def lag_shift(series, phase_now, phase_move):
    series_sum = jnp.zeros(series.shape[2:], jnp.float32)
    for number in range(series.shape[0]):
        harmonic = float(number + 1)
        change_cos = jnp.cos(harmonic * (phase_now + phase_move)) - jnp.cos(harmonic * phase_now)
        change_sin = jnp.sin(harmonic * (phase_now + phase_move)) - jnp.sin(harmonic * phase_now)
        series_sum = series_sum + series[number, 0] * change_cos - series[number, 1] * change_sin
    return series_sum


def metric_terms(offset_x, offset_y):
    x_zeta = 1.0 + (offset_x[2:, 1:-1] - offset_x[:-2, 1:-1]) * 0.5
    x_xi = (offset_x[1:-1, 2:] - offset_x[1:-1, :-2]) * 0.5
    y_xi = 1.0 + (offset_y[1:-1, 2:] - offset_y[1:-1, :-2]) * 0.5
    y_zeta = (offset_y[2:, 1:-1] - offset_y[:-2, 1:-1]) * 0.5
    return (x_zeta, x_xi, y_xi, y_zeta)


def geometry(grid_pad):
    x_zeta, x_xi, y_xi, y_zeta = metric_terms(grid_pad[0], grid_pad[1])
    old_zeta, old_xi, oldy_xi, oldy_zeta = metric_terms(
        grid_pad[0] - grid_pad[2], grid_pad[1] - grid_pad[3]
    )
    volume_new = (x_zeta * y_xi - x_xi * y_zeta)[1:-1, 1:-1]
    volume_old = (old_zeta * oldy_xi - old_xi * oldy_zeta)[1:-1, 1:-1]
    speed_x = grid_pad[2][1:-1, 1:-1] / TIME_STEP
    speed_y = grid_pad[3][1:-1, 1:-1] / TIME_STEP
    first_pitch = -y_zeta
    sweep_pitch = first_pitch * speed_x + x_zeta * speed_y
    second_axial = -x_xi
    sweep_axial = y_xi * speed_x + second_axial * speed_y
    return (
        (first_pitch, x_zeta, sweep_pitch, y_xi, second_axial, sweep_axial),
        volume_old,
        volume_new,
    )


def directional(strip_cells, first_coef, second_coef, sweep_term):
    density = strip_cells[0]
    vel_x = strip_cells[1] / density
    vel_y = strip_cells[2] / density
    energy = strip_cells[3]
    pressure = (HEAT_RATIO - 1.0) * (energy - 0.5 * density * (vel_x * vel_x + vel_y * vel_y))
    flux_x = jnp.stack(
        [
            strip_cells[1],
            strip_cells[1] * vel_x + pressure,
            strip_cells[1] * vel_y,
            (energy + pressure) * vel_x,
        ]
    )
    flux_y = jnp.stack(
        [
            strip_cells[2],
            strip_cells[2] * vel_x,
            strip_cells[2] * vel_y + pressure,
            (energy + pressure) * vel_y,
        ]
    )
    return first_coef * flux_x + second_coef * flux_y - sweep_term * strip_cells


def residual(padded, geo_terms):
    first_pitch, second_pitch, sweep_pitch, first_axial, second_axial, sweep_axial = geo_terms
    pitch_flux = directional(
        padded[:, 2:-2, 1:-1], first_pitch[1:-1], second_pitch[1:-1], sweep_pitch[1:-1]
    )
    axial_flux = directional(
        padded[:, 1:-1, 2:-2], first_axial[:, 1:-1], second_axial[:, 1:-1], sweep_axial[:, 1:-1]
    )
    divergence = (pitch_flux[:, :, 2:] - pitch_flux[:, :, :-2]) * 0.5 + (
        axial_flux[:, 2:] - axial_flux[:, :-2]
    ) * 0.5
    centre = padded[:, 2:-2, 2:-2]
    fourth = (
        padded[:, 2:-2, 4:]
        - 4.0 * padded[:, 2:-2, 3:-1]
        + 6.0 * centre
        - 4.0 * padded[:, 2:-2, 1:-3]
        + padded[:, 2:-2, :-4]
        + (
            padded[:, 4:, 2:-2]
            - 4.0 * padded[:, 3:-1, 2:-2]
            + 6.0 * centre
            - 4.0 * padded[:, 1:-3, 2:-2]
            + padded[:, :-4, 2:-2]
        )
    )
    return divergence + DAMPING * fourth + DAMPING * radial_damping(centre, 3)


def flow_ghosts(
    row_zero,
    row_one,
    row_last,
    row_before,
    wrap_low0,
    wrap_low1,
    wrap_high0,
    wrap_high1,
    blade_flag,
    corr_low,
    corr_high,
):
    sign_flip = jnp.array([1.0, 1.0, -1.0, 1.0], jnp.float32).reshape(
        (4,) + (1,) * (row_zero.ndim - 1)
    )
    ghost_m2 = jnp.where(blade_flag, row_one * sign_flip, wrap_low0 + corr_low)
    ghost_m1 = jnp.where(blade_flag, row_zero * sign_flip, wrap_low1 + corr_low)
    ghost_p0 = jnp.where(blade_flag, row_last * sign_flip, wrap_high0 + corr_high)
    ghost_p1 = jnp.where(blade_flag, row_before * sign_flip, wrap_high1 + corr_high)
    return (ghost_m2, ghost_m1, ghost_p0, ghost_p1)


def finish_flow(
    padded, depth, row_flag, corr_low, corr_high, low_end, high_end, first_end, last_end
):
    middle_rows = padded[:, 2:-2]
    width = middle_rows.shape[2]
    ghost_m2, ghost_m1, ghost_p0, ghost_p1 = flow_ghosts(
        middle_rows[:, :, 2],
        middle_rows[:, :, 3],
        middle_rows[:, :, width - 3],
        middle_rows[:, :, width - 4],
        middle_rows[:, :, 0],
        middle_rows[:, :, 1],
        middle_rows[:, :, width - 2],
        middle_rows[:, :, width - 1],
        row_flag[:, None],
        corr_low,
        corr_high,
    )
    low_pair = jnp.where(low_end, jnp.stack([ghost_m2, ghost_m1], 2), middle_rows[:, :, 0:2])
    high_pair = jnp.where(
        high_end, jnp.stack([ghost_p0, ghost_p1], 2), middle_rows[:, :, width - 2 :]
    )
    middle_rows = jnp.concatenate([low_pair, middle_rows[:, :, 2 : width - 2], high_pair], 2)
    whole = jnp.concatenate([padded[:, 0:2], middle_rows, padded[:, -2:]], 1)
    top_copy = jnp.repeat(whole[:, depth : depth + 1], depth, axis=1)
    bottom_copy = jnp.repeat(whole[:, -depth - 1 : -depth], depth, axis=1)
    top_rows = jnp.where(first_end, top_copy, whole[:, :depth])
    bottom_rows = jnp.where(last_end, bottom_copy, whole[:, -depth:])
    return jnp.concatenate([top_rows, whole[:, depth:-depth], bottom_rows], 1)


def _flux(rho, mx, my, en, first, second, sweep):
    u = mx / rho
    v = my / rho
    pr = (HEAT_RATIO - 1.0) * (en - 0.5 * rho * (u * u + v * v))
    ep = en + pr
    return (
        first * mx + second * my - sweep * rho,
        first * (mx * u + pr) + second * (my * u) - sweep * mx,
        first * (mx * v) + second * (my * v + pr) - sweep * my,
        first * (ep * u) + second * (ep * v) - sweep * en,
    )


def _radial(c0, lane, forward):
    width = c0.shape[-1]
    last = width - 1

    def down(x):
        a = pltpu.roll(x, 1, 1)
        b = pltpu.roll(x, last, 1)
        return jnp.where(forward, a, b)

    def up(x):
        a = pltpu.roll(x, 1, 1)
        b = pltpu.roll(x, last, 1)
        return jnp.where(forward, b, a)

    m1 = jnp.where(lane == 0, c0, down(c0))
    p1 = jnp.where(lane == last, c0, up(c0))
    m2 = jnp.where(lane == 0, c0, down(m1))
    p2 = jnp.where(lane == last, c0, up(p1))
    return p2 - 4.0 * p1 + 6.0 * c0 - 4.0 * m1 + m2


def _volume(grid, a, npch, old):
    def comp(c, row, lo, hi):
        value = grid[c, row, lo:hi]
        if old:
            value = value - grid[c + 2, row, lo:hi]
        return value

    x_zeta = 1.0 + (comp(0, a + 3, 2, npch + 2) - comp(0, a + 1, 2, npch + 2)) * 0.5
    x_xi = (comp(0, a + 2, 3, npch + 3) - comp(0, a + 2, 1, npch + 1)) * 0.5
    y_xi = 1.0 + (comp(1, a + 2, 3, npch + 3) - comp(1, a + 2, 1, npch + 1)) * 0.5
    y_zeta = (comp(1, a + 3, 2, npch + 2) - comp(1, a + 1, 2, npch + 2)) * 0.5
    return x_zeta * y_xi - x_xi * y_zeta


def _section_body(scale, pad, grid, q0, out, af, pf):
    na = out.shape[1]
    npch = out.shape[2]
    width = out.shape[3]

    def axial_row(j, carry):
        x_xi = (grid[0, j + 1, 3 : npch + 3] - grid[0, j + 1, 1 : npch + 1]) * 0.5
        y_xi = 1.0 + (grid[1, j + 1, 3 : npch + 3] - grid[1, j + 1, 1 : npch + 1]) * 0.5
        speed_x = grid[2, j + 1, 2 : npch + 2] / TIME_STEP
        speed_y = grid[3, j + 1, 2 : npch + 2] / TIME_STEP
        second = -x_xi
        sweep = y_xi * speed_x + second * speed_y
        q = [pad[k, j + 1, 2 : npch + 2] for k in range(4)]
        f = _flux(*q, y_xi, second, sweep)
        for k in range(4):
            af[k, j] = f[k]
        return carry

    lax.fori_loop(0, na + 2, axial_row, 0)
    lane = lax.broadcasted_iota(jnp.int32, (npch, width), 1)
    probe = pltpu.roll(lane, 1, 1)
    forward = probe == jnp.where(lane == 0, width - 1, lane - 1)

    def row(a, carry):
        x_zeta = 1.0 + (grid[0, a + 3, 1 : npch + 3] - grid[0, a + 1, 1 : npch + 3]) * 0.5
        y_zeta = (grid[1, a + 3, 1 : npch + 3] - grid[1, a + 1, 1 : npch + 3]) * 0.5
        speed_x = grid[2, a + 2, 1 : npch + 3] / TIME_STEP
        speed_y = grid[3, a + 2, 1 : npch + 3] / TIME_STEP
        first = -y_zeta
        sweep = first * speed_x + x_zeta * speed_y
        q = [pad[k, a + 2, 1 : npch + 3] for k in range(4)]
        f = _flux(*q, first, x_zeta, sweep)
        for k in range(4):
            pf[k] = f[k]
        volume_old = _volume(grid, a, npch, True)
        volume_new = _volume(grid, a, npch, False)
        for k in range(4):
            div = (pf[k, 2 : npch + 2] - pf[k, 0:npch]) * 0.5 + (af[k, a + 2] - af[k, a]) * 0.5
            c0 = pad[k, a + 2, 2 : npch + 2]
            fourth = (
                pad[k, a + 2, 4 : npch + 4]
                - 4.0 * pad[k, a + 2, 3 : npch + 3]
                + 6.0 * c0
                - 4.0 * pad[k, a + 2, 1 : npch + 1]
                + pad[k, a + 2, 0:npch]
            ) + (
                pad[k, a + 4, 2 : npch + 2]
                - 4.0 * pad[k, a + 3, 2 : npch + 2]
                + 6.0 * c0
                - 4.0 * pad[k, a + 1, 2 : npch + 2]
                + pad[k, a, 2 : npch + 2]
            )
            res = div + DAMPING * fourth + DAMPING * _radial(c0, lane, forward)
            out[k, a] = (volume_old * q0[k, a] - scale * res) / volume_new
        return carry

    lax.fori_loop(0, na, row, 0)


def section_kernel(padded, grid_pad, start, scale, interpret=False):
    _, na, npch, width = start.shape
    body = lambda *refs: _section_body(scale, *refs)
    cells = na * npch * width
    return pl.pallas_call(
        body,
        out_shape=jax.ShapeDtypeStruct(start.shape, start.dtype),
        scratch_shapes=[
            pltpu.VMEM((4, na + 2, npch, width), jnp.float32),
            pltpu.VMEM((4, npch + 2, width), jnp.float32),
        ],
        compiler_params=pltpu.CompilerParams(vmem_limit_bytes=60 * 1024 * 1024),
        cost_estimate=pl.CostEstimate(
            flops=500 * cells, transcendentals=0, bytes_accessed=4 * 14 * cells
        ),
        interpret=interpret,
    )(padded, grid_pad, start)


def per_device(flow_state, node_offset, blade_mode, phase_angles, lag_series):
    n_pitch = lax.axis_size("pitch")
    n_span = lax.axis_size("span")
    pitch_rows = flow_state.shape[2]
    axial_cols = flow_state.shape[1]
    total_pitch = pitch_rows * n_pitch
    total_axial = axial_cols * n_span
    pitch_at = lax.axis_index("pitch")
    span_at = lax.axis_index("span")
    lead_edge = total_axial // 4
    axial_index = span_at * axial_cols + jnp.arange(axial_cols, dtype=jnp.int32)
    blade_flag = (axial_index >= lead_edge) & (axial_index < total_axial - lead_edge)
    blade_mask = blade_flag.astype(jnp.float32)[:, None]
    phase_now = phase_angles[0]
    phase_lag = phase_angles[1]
    low_guess = wall_amplitude(blade_mode, phase_now, blade_mask) * unit_normal(
        node_offset[:, :, 0], node_offset[:, :, 1]
    )
    high_guess = wall_amplitude(blade_mode, phase_now + phase_lag, blade_mask) * unit_normal(
        node_offset[:, :, pitch_rows - 2], node_offset[:, :, pitch_rows - 1]
    )
    low_wall = low_guess
    high_wall = high_guess
    sent = jnp.where(pitch_at == 0, low_guess, high_guess)
    for shift in range(1, n_pitch):
        got = lax.ppermute(sent, "pitch", [(0, shift), (n_pitch - 1, shift - 1)])
        low_wall = jnp.where(pitch_at == shift, got, low_wall)
        high_wall = jnp.where(pitch_at == shift - 1, got, high_wall)
    pitch_index = pitch_at * pitch_rows + jnp.arange(pitch_rows, dtype=jnp.int32)
    blend_row = (pitch_index.astype(jnp.float32) / (total_pitch - 1))[:, None]
    shift_field = (1.0 - blend_row) * low_wall[:, :, None, :] + blend_row * high_wall[:, :, None, :]
    moved_offset = node_offset + shift_field
    grid_field = jnp.concatenate([moved_offset, shift_field], 0)
    rim_width = 2
    grid_pad = padded_2(grid_field, (("pitch", 2), ("span", 1)), rim_width)
    first_pad = padded_cross(flow_state, rim_width)
    low_end = pitch_at == 0
    high_end = pitch_at == n_pitch - 1
    first_end = span_at == 0
    last_end = span_at == n_span - 1
    grid_pad = fill_ends(grid_pad, 1, rim_width, first_end, last_end)
    grid_pad = fill_ends(grid_pad, 2, 2, low_end, high_end)
    corr_low = lag_shift(lag_series[1], phase_now, -phase_lag)
    corr_high = lag_shift(lag_series[0], phase_now, phase_lag)
    padded = finish_flow(
        first_pad, 2, blade_flag, corr_low, corr_high, low_end, high_end, first_end, last_end
    )
    section_one = section_kernel(padded, grid_pad, flow_state, SECTION_WEIGHTS[0] * TIME_STEP)
    second_pad = padded_cross(section_one, 2)
    padded = finish_flow(
        second_pad, 2, blade_flag, corr_low, corr_high, low_end, high_end, first_end, last_end
    )
    current = section_kernel(padded, grid_pad, flow_state, SECTION_WEIGHTS[1] * TIME_STEP)
    return (current, moved_offset)


def solution(mesh):
    placed = (
        P(None, "span", "pitch", None),
        P(None, "span", "pitch", None),
        P(None, "span", None),
        P(),
        P(None, None, None, None, "span", None),
    )
    return jax.shard_map(
        per_device,
        mesh=mesh,
        in_specs=placed,
        out_specs=(P(None, "span", "pitch", None), P(None, "span", "pitch", None)),
        check_vma=False,
    )
```

```python
import jax
import jax.numpy as jnp
from jax import lax
from jax.sharding import PartitionSpec as P
from jax.experimental import pallas as pl
from jax.experimental.pallas import tpu as pltpu

HEAT_RATIO = 1.4
TIME_STEP = 0.25
DAMPING = 0.02
SECTION_WEIGHTS = (0.5, 1.0)


def broadcast(value, axis, root):
    mine = lax.axis_index(axis) == root
    return lax.psum(jnp.where(mine, value, jnp.zeros_like(value)), axis)


def padded_2(block, sides, width):
    for axis, dim in sides:
        count = lax.axis_size(axis)
        forward = [(i, i + 1) for i in range(count - 1)]
        forward.append((count - 1, 0))
        backward = [(target, source) for source, target in forward]
        low = lax.ppermute(
            lax.slice_in_dim(block, block.shape[dim] - width, None, axis=dim), axis, forward
        )
        high = lax.ppermute(lax.slice_in_dim(block, 0, width, axis=dim), axis, backward)
        block = jnp.concatenate([low, block, high], axis=dim)
    return block


def padded_cross(block, width):
    rims = []
    for axis, dim in (("pitch", 2), ("span", 1)):
        count = lax.axis_size(axis)
        forward = [(i, (i + 1) % count) for i in range(count)]
        backward = [(target, source) for source, target in forward]
        low = lax.ppermute(
            lax.slice_in_dim(block, block.shape[dim] - width, None, axis=dim), axis, forward
        )
        high = lax.ppermute(lax.slice_in_dim(block, 0, width, axis=dim), axis, backward)
        rims.append((low, high))
    (pitch_low, pitch_high), (span_low, span_high) = rims
    middle = jnp.concatenate([pitch_low, block, pitch_high], axis=2)
    corner = jnp.zeros(span_low.shape[:2] + (width,) + span_low.shape[3:], block.dtype)
    top = jnp.concatenate([corner, span_low, corner], axis=2)
    bottom = jnp.concatenate([corner, span_high, corner], axis=2)
    return jnp.concatenate([top, middle, bottom], axis=1)


def fill_ends(padded, axis_pos, depth, at_first, at_last):
    length = padded.shape[axis_pos]
    inner_first = lax.slice_in_dim(padded, depth, depth + 1, axis=axis_pos)
    inner_second = lax.slice_in_dim(padded, depth + 1, depth + 2, axis=axis_pos)
    inner_last = lax.slice_in_dim(padded, length - depth - 1, length - depth, axis=axis_pos)
    inner_before = lax.slice_in_dim(padded, length - depth - 2, length - depth - 1, axis=axis_pos)
    step_low = inner_first - inner_second
    step_high = inner_last - inner_before
    low_side = jnp.concatenate(
        [inner_first + float(count) * step_low for count in range(depth, 0, -1)], axis=axis_pos
    )
    high_side = jnp.concatenate(
        [inner_last + float(count) * step_high for count in range(1, depth + 1)], axis=axis_pos
    )
    low_side = jnp.where(at_first, low_side, lax.slice_in_dim(padded, 0, depth, axis=axis_pos))
    high_side = jnp.where(
        at_last, high_side, lax.slice_in_dim(padded, length - depth, length, axis=axis_pos)
    )
    return jnp.concatenate(
        [low_side, lax.slice_in_dim(padded, depth, length - depth, axis=axis_pos), high_side],
        axis=axis_pos,
    )


def radial_damping(values, axis_pos):
    count = values.shape[axis_pos]
    first_row = lax.slice_in_dim(values, 0, 1, axis=axis_pos)
    last_row = lax.slice_in_dim(values, count - 1, count, axis=axis_pos)
    extended = jnp.concatenate([first_row, first_row, values, last_row, last_row], axis=axis_pos)
    return (
        lax.slice_in_dim(extended, 4, 4 + count, axis=axis_pos)
        - 4.0 * lax.slice_in_dim(extended, 3, 3 + count, axis=axis_pos)
        + 6.0 * values
        - 4.0 * lax.slice_in_dim(extended, 1, 1 + count, axis=axis_pos)
        + lax.slice_in_dim(extended, 0, count, axis=axis_pos)
    )


def unit_normal(earlier, later):
    along_x = later[0] - earlier[0]
    along_y = 1.0 + later[1] - earlier[1]
    length = jnp.sqrt(along_x * along_x + along_y * along_y)
    return jnp.stack([along_x / length, along_y / length])


def wall_amplitude(shape_mode, angle, blade_mask):
    return (shape_mode[0] * jnp.cos(angle) - shape_mode[1] * jnp.sin(angle)) * blade_mask


def lag_shift(series, phase_now, phase_move):
    series_sum = jnp.zeros(series.shape[2:], jnp.float32)
    for number in range(series.shape[0]):
        harmonic = float(number + 1)
        change_cos = jnp.cos(harmonic * (phase_now + phase_move)) - jnp.cos(harmonic * phase_now)
        change_sin = jnp.sin(harmonic * (phase_now + phase_move)) - jnp.sin(harmonic * phase_now)
        series_sum = series_sum + series[number, 0] * change_cos - series[number, 1] * change_sin
    return series_sum


def metric_terms(offset_x, offset_y):
    x_zeta = 1.0 + (offset_x[2:, 1:-1] - offset_x[:-2, 1:-1]) * 0.5
    x_xi = (offset_x[1:-1, 2:] - offset_x[1:-1, :-2]) * 0.5
    y_xi = 1.0 + (offset_y[1:-1, 2:] - offset_y[1:-1, :-2]) * 0.5
    y_zeta = (offset_y[2:, 1:-1] - offset_y[:-2, 1:-1]) * 0.5
    return (x_zeta, x_xi, y_xi, y_zeta)


def geometry(grid_pad):
    x_zeta, x_xi, y_xi, y_zeta = metric_terms(grid_pad[0], grid_pad[1])
    old_zeta, old_xi, oldy_xi, oldy_zeta = metric_terms(
        grid_pad[0] - grid_pad[2], grid_pad[1] - grid_pad[3]
    )
    volume_new = (x_zeta * y_xi - x_xi * y_zeta)[1:-1, 1:-1]
    volume_old = (old_zeta * oldy_xi - old_xi * oldy_zeta)[1:-1, 1:-1]
    speed_x = grid_pad[2][1:-1, 1:-1] / TIME_STEP
    speed_y = grid_pad[3][1:-1, 1:-1] / TIME_STEP
    first_pitch = -y_zeta
    sweep_pitch = first_pitch * speed_x + x_zeta * speed_y
    second_axial = -x_xi
    sweep_axial = y_xi * speed_x + second_axial * speed_y
    return (
        (first_pitch, x_zeta, sweep_pitch, y_xi, second_axial, sweep_axial),
        volume_old,
        volume_new,
    )


def directional(strip_cells, first_coef, second_coef, sweep_term):
    density = strip_cells[0]
    vel_x = strip_cells[1] / density
    vel_y = strip_cells[2] / density
    energy = strip_cells[3]
    pressure = (HEAT_RATIO - 1.0) * (energy - 0.5 * density * (vel_x * vel_x + vel_y * vel_y))
    flux_x = jnp.stack(
        [
            strip_cells[1],
            strip_cells[1] * vel_x + pressure,
            strip_cells[1] * vel_y,
            (energy + pressure) * vel_x,
        ]
    )
    flux_y = jnp.stack(
        [
            strip_cells[2],
            strip_cells[2] * vel_x,
            strip_cells[2] * vel_y + pressure,
            (energy + pressure) * vel_y,
        ]
    )
    return first_coef * flux_x + second_coef * flux_y - sweep_term * strip_cells


def residual(padded, geo_terms):
    first_pitch, second_pitch, sweep_pitch, first_axial, second_axial, sweep_axial = geo_terms
    pitch_flux = directional(
        padded[:, 2:-2, 1:-1], first_pitch[1:-1], second_pitch[1:-1], sweep_pitch[1:-1]
    )
    axial_flux = directional(
        padded[:, 1:-1, 2:-2], first_axial[:, 1:-1], second_axial[:, 1:-1], sweep_axial[:, 1:-1]
    )
    divergence = (pitch_flux[:, :, 2:] - pitch_flux[:, :, :-2]) * 0.5 + (
        axial_flux[:, 2:] - axial_flux[:, :-2]
    ) * 0.5
    centre = padded[:, 2:-2, 2:-2]
    fourth = (
        padded[:, 2:-2, 4:]
        - 4.0 * padded[:, 2:-2, 3:-1]
        + 6.0 * centre
        - 4.0 * padded[:, 2:-2, 1:-3]
        + padded[:, 2:-2, :-4]
        + (
            padded[:, 4:, 2:-2]
            - 4.0 * padded[:, 3:-1, 2:-2]
            + 6.0 * centre
            - 4.0 * padded[:, 1:-3, 2:-2]
            + padded[:, :-4, 2:-2]
        )
    )
    return divergence + DAMPING * fourth + DAMPING * radial_damping(centre, 3)


def flow_ghosts(
    row_zero,
    row_one,
    row_last,
    row_before,
    wrap_low0,
    wrap_low1,
    wrap_high0,
    wrap_high1,
    blade_flag,
    corr_low,
    corr_high,
):
    sign_flip = jnp.array([1.0, 1.0, -1.0, 1.0], jnp.float32).reshape(
        (4,) + (1,) * (row_zero.ndim - 1)
    )
    ghost_m2 = jnp.where(blade_flag, row_one * sign_flip, wrap_low0 + corr_low)
    ghost_m1 = jnp.where(blade_flag, row_zero * sign_flip, wrap_low1 + corr_low)
    ghost_p0 = jnp.where(blade_flag, row_last * sign_flip, wrap_high0 + corr_high)
    ghost_p1 = jnp.where(blade_flag, row_before * sign_flip, wrap_high1 + corr_high)
    return (ghost_m2, ghost_m1, ghost_p0, ghost_p1)


def finish_flow(
    padded, depth, row_flag, corr_low, corr_high, low_end, high_end, first_end, last_end
):
    middle_rows = padded[:, 2:-2]
    width = middle_rows.shape[2]
    ghost_m2, ghost_m1, ghost_p0, ghost_p1 = flow_ghosts(
        middle_rows[:, :, 2],
        middle_rows[:, :, 3],
        middle_rows[:, :, width - 3],
        middle_rows[:, :, width - 4],
        middle_rows[:, :, 0],
        middle_rows[:, :, 1],
        middle_rows[:, :, width - 2],
        middle_rows[:, :, width - 1],
        row_flag[:, None],
        corr_low,
        corr_high,
    )
    low_pair = jnp.where(low_end, jnp.stack([ghost_m2, ghost_m1], 2), middle_rows[:, :, 0:2])
    high_pair = jnp.where(
        high_end, jnp.stack([ghost_p0, ghost_p1], 2), middle_rows[:, :, width - 2 :]
    )
    middle_rows = jnp.concatenate([low_pair, middle_rows[:, :, 2 : width - 2], high_pair], 2)
    whole = jnp.concatenate([padded[:, 0:2], middle_rows, padded[:, -2:]], 1)
    top_copy = jnp.repeat(whole[:, depth : depth + 1], depth, axis=1)
    bottom_copy = jnp.repeat(whole[:, -depth - 1 : -depth], depth, axis=1)
    top_rows = jnp.where(first_end, top_copy, whole[:, :depth])
    bottom_rows = jnp.where(last_end, bottom_copy, whole[:, -depth:])
    return jnp.concatenate([top_rows, whole[:, depth:-depth], bottom_rows], 1)


def _flux(rho, mx, my, en, first, second, sweep):
    inverse = 1.0 / rho
    u = mx * inverse
    v = my * inverse
    pr = (HEAT_RATIO - 1.0) * (en - 0.5 * rho * (u * u + v * v))
    ep = en + pr
    return (
        first * mx + second * my - sweep * rho,
        first * (mx * u + pr) + second * (my * u) - sweep * mx,
        first * (mx * v) + second * (my * v + pr) - sweep * my,
        first * (ep * u) + second * (ep * v) - sweep * en,
    )


def _radial_pairs(c0, lane, forward):
    width = c0.shape[-1]
    last = width - 1
    one_a = pltpu.roll(c0, 1, 1)
    one_b = pltpu.roll(c0, last, 1)
    two_a = pltpu.roll(c0, 2, 1)
    two_b = pltpu.roll(c0, width - 2, 1)
    m1 = jnp.where(lane == 0, c0, jnp.where(forward, one_a, one_b))
    p1 = jnp.where(lane == last, c0, jnp.where(forward, one_b, one_a))
    m2 = jnp.where(lane <= 1, m1, jnp.where(forward, two_a, two_b))
    p2 = jnp.where(lane >= last - 1, p1, jnp.where(forward, two_b, two_a))
    return m1 + p1, m2 + p2


def _volume(grid, a, npch, old):
    def comp(c, row, lo, hi):
        value = grid[c, row, lo:hi]
        if old:
            value = value - grid[c + 2, row, lo:hi]
        return value

    x_zeta = 1.0 + (comp(0, a + 3, 2, npch + 2) - comp(0, a + 1, 2, npch + 2)) * 0.5
    x_xi = (comp(0, a + 2, 3, npch + 3) - comp(0, a + 2, 1, npch + 1)) * 0.5
    y_xi = 1.0 + (comp(1, a + 2, 3, npch + 3) - comp(1, a + 2, 1, npch + 1)) * 0.5
    y_zeta = (comp(1, a + 3, 2, npch + 2) - comp(1, a + 1, 2, npch + 2)) * 0.5
    return x_zeta * y_xi - x_xi * y_zeta


def _section_body(scale, pad, grid, q0, out, af, pf):
    na = out.shape[1]
    npch = out.shape[2]
    width = out.shape[3]

    def axial_row(j, carry):
        x_xi = (grid[0, j + 1, 3 : npch + 3] - grid[0, j + 1, 1 : npch + 1]) * 0.5
        y_xi = 1.0 + (grid[1, j + 1, 3 : npch + 3] - grid[1, j + 1, 1 : npch + 1]) * 0.5
        speed_x = grid[2, j + 1, 2 : npch + 2] / TIME_STEP
        speed_y = grid[3, j + 1, 2 : npch + 2] / TIME_STEP
        second = -x_xi
        sweep = y_xi * speed_x + second * speed_y
        q = [pad[k, j + 1, 2 : npch + 2] for k in range(4)]
        f = _flux(*q, y_xi, second, sweep)
        for k in range(4):
            af[k, j] = f[k]
        return carry

    lax.fori_loop(0, na + 2, axial_row, 0)
    lane = lax.broadcasted_iota(jnp.int32, (npch, width), 1)
    probe = pltpu.roll(lane, 1, 1)
    forward = probe == jnp.where(lane == 0, width - 1, lane - 1)

    def row(a, carry):
        x_zeta = 1.0 + (grid[0, a + 3, 1 : npch + 3] - grid[0, a + 1, 1 : npch + 3]) * 0.5
        y_zeta = (grid[1, a + 3, 1 : npch + 3] - grid[1, a + 1, 1 : npch + 3]) * 0.5
        speed_x = grid[2, a + 2, 1 : npch + 3] / TIME_STEP
        speed_y = grid[3, a + 2, 1 : npch + 3] / TIME_STEP
        first = -y_zeta
        sweep = first * speed_x + x_zeta * speed_y
        q = [pad[k, a + 2, 1 : npch + 3] for k in range(4)]
        f = _flux(*q, first, x_zeta, sweep)
        for k in range(4):
            pf[k] = f[k]
        volume_old = _volume(grid, a, npch, True)
        inverse_new = 1.0 / _volume(grid, a, npch, False)
        for k in range(4):
            div = (pf[k, 2 : npch + 2] - pf[k, 0:npch]) * 0.5 + (af[k, a + 2] - af[k, a]) * 0.5
            c0 = pad[k, a + 2, 2 : npch + 2]
            near_r, far_r = _radial_pairs(c0, lane, forward)
            near = (
                pad[k, a + 2, 3 : npch + 3]
                + pad[k, a + 2, 1 : npch + 1]
                + pad[k, a + 3, 2 : npch + 2]
                + pad[k, a + 1, 2 : npch + 2]
                + near_r
            )
            far = (
                pad[k, a + 2, 4 : npch + 4]
                + pad[k, a + 2, 0:npch]
                + pad[k, a + 4, 2 : npch + 2]
                + pad[k, a, 2 : npch + 2]
                + far_r
            )
            res = div + DAMPING * (far - 4.0 * near + 18.0 * c0)
            out[k, a] = (volume_old * q0[k, a] - scale * res) * inverse_new
        return carry

    lax.fori_loop(0, na, row, 0)


def section_kernel(padded, grid_pad, start, scale, interpret=False):
    _, na, npch, width = start.shape
    body = lambda *refs: _section_body(scale, *refs)
    cells = na * npch * width
    return pl.pallas_call(
        body,
        out_shape=jax.ShapeDtypeStruct(start.shape, start.dtype),
        scratch_shapes=[
            pltpu.VMEM((4, na + 2, npch, width), jnp.float32),
            pltpu.VMEM((4, npch + 2, width), jnp.float32),
        ],
        compiler_params=pltpu.CompilerParams(vmem_limit_bytes=60 * 1024 * 1024),
        cost_estimate=pl.CostEstimate(
            flops=500 * cells, transcendentals=0, bytes_accessed=4 * 14 * cells
        ),
        interpret=interpret,
    )(padded, grid_pad, start)


def per_device(flow_state, node_offset, blade_mode, phase_angles, lag_series):
    n_pitch = lax.axis_size("pitch")
    n_span = lax.axis_size("span")
    pitch_rows = flow_state.shape[2]
    axial_cols = flow_state.shape[1]
    total_pitch = pitch_rows * n_pitch
    total_axial = axial_cols * n_span
    pitch_at = lax.axis_index("pitch")
    span_at = lax.axis_index("span")
    lead_edge = total_axial // 4
    axial_index = span_at * axial_cols + jnp.arange(axial_cols, dtype=jnp.int32)
    blade_flag = (axial_index >= lead_edge) & (axial_index < total_axial - lead_edge)
    blade_mask = blade_flag.astype(jnp.float32)[:, None]
    phase_now = phase_angles[0]
    phase_lag = phase_angles[1]
    low_guess = wall_amplitude(blade_mode, phase_now, blade_mask) * unit_normal(
        node_offset[:, :, 0], node_offset[:, :, 1]
    )
    high_guess = wall_amplitude(blade_mode, phase_now + phase_lag, blade_mask) * unit_normal(
        node_offset[:, :, pitch_rows - 2], node_offset[:, :, pitch_rows - 1]
    )
    low_wall = low_guess
    high_wall = high_guess
    sent = jnp.where(pitch_at == 0, low_guess, high_guess)
    for shift in range(1, n_pitch):
        got = lax.ppermute(sent, "pitch", [(0, shift), (n_pitch - 1, shift - 1)])
        low_wall = jnp.where(pitch_at == shift, got, low_wall)
        high_wall = jnp.where(pitch_at == shift - 1, got, high_wall)
    pitch_index = pitch_at * pitch_rows + jnp.arange(pitch_rows, dtype=jnp.int32)
    blend_row = (pitch_index.astype(jnp.float32) / (total_pitch - 1))[:, None]
    shift_field = (1.0 - blend_row) * low_wall[:, :, None, :] + blend_row * high_wall[:, :, None, :]
    moved_offset = node_offset + shift_field
    grid_field = jnp.concatenate([moved_offset, shift_field], 0)
    rim_width = 2
    grid_pad = padded_2(grid_field, (("pitch", 2), ("span", 1)), rim_width)
    first_pad = padded_cross(flow_state, rim_width)
    low_end = pitch_at == 0
    high_end = pitch_at == n_pitch - 1
    first_end = span_at == 0
    last_end = span_at == n_span - 1
    grid_pad = fill_ends(grid_pad, 1, rim_width, first_end, last_end)
    grid_pad = fill_ends(grid_pad, 2, 2, low_end, high_end)
    corr_low = lag_shift(lag_series[1], phase_now, -phase_lag)
    corr_high = lag_shift(lag_series[0], phase_now, phase_lag)
    padded = finish_flow(
        first_pad, 2, blade_flag, corr_low, corr_high, low_end, high_end, first_end, last_end
    )
    section_one = section_kernel(padded, grid_pad, flow_state, SECTION_WEIGHTS[0] * TIME_STEP)
    second_pad = padded_cross(section_one, 2)
    padded = finish_flow(
        second_pad, 2, blade_flag, corr_low, corr_high, low_end, high_end, first_end, last_end
    )
    current = section_kernel(padded, grid_pad, flow_state, SECTION_WEIGHTS[1] * TIME_STEP)
    return (current, moved_offset)


def solution(mesh):
    placed = (
        P(None, "span", "pitch", None),
        P(None, "span", "pitch", None),
        P(None, "span", None),
        P(),
        P(None, None, None, None, "span", None),
    )
    return jax.shard_map(
        per_device,
        mesh=mesh,
        in_specs=placed,
        out_specs=(P(None, "span", "pitch", None), P(None, "span", "pitch", None)),
        check_vma=False,
    )
```

```python
import jax
import jax.numpy as jnp
from jax import lax
from jax.sharding import PartitionSpec as P
from jax.experimental import pallas as pl
from jax.experimental.pallas import tpu as pltpu

HEAT_RATIO = 1.4
TIME_STEP = 0.25
DAMPING = 0.02
SECTION_WEIGHTS = (0.5, 1.0)


def broadcast(value, axis, root):
    mine = lax.axis_index(axis) == root
    return lax.psum(jnp.where(mine, value, jnp.zeros_like(value)), axis)


def padded_2(block, sides, width):
    for axis, dim in sides:
        count = lax.axis_size(axis)
        forward = [(i, i + 1) for i in range(count - 1)]
        forward.append((count - 1, 0))
        backward = [(target, source) for source, target in forward]
        low = lax.ppermute(
            lax.slice_in_dim(block, block.shape[dim] - width, None, axis=dim), axis, forward
        )
        high = lax.ppermute(lax.slice_in_dim(block, 0, width, axis=dim), axis, backward)
        block = jnp.concatenate([low, block, high], axis=dim)
    return block


def padded_cross(block, width):
    rims = []
    for axis, dim in (("pitch", 2), ("span", 1)):
        count = lax.axis_size(axis)
        forward = [(i, (i + 1) % count) for i in range(count)]
        backward = [(target, source) for source, target in forward]
        low = lax.ppermute(
            lax.slice_in_dim(block, block.shape[dim] - width, None, axis=dim), axis, forward
        )
        high = lax.ppermute(lax.slice_in_dim(block, 0, width, axis=dim), axis, backward)
        rims.append((low, high))
    (pitch_low, pitch_high), (span_low, span_high) = rims
    middle = jnp.concatenate([pitch_low, block, pitch_high], axis=2)
    corner = jnp.zeros(span_low.shape[:2] + (width,) + span_low.shape[3:], block.dtype)
    top = jnp.concatenate([corner, span_low, corner], axis=2)
    bottom = jnp.concatenate([corner, span_high, corner], axis=2)
    return jnp.concatenate([top, middle, bottom], axis=1)


def fill_ends(padded, axis_pos, depth, at_first, at_last):
    length = padded.shape[axis_pos]
    inner_first = lax.slice_in_dim(padded, depth, depth + 1, axis=axis_pos)
    inner_second = lax.slice_in_dim(padded, depth + 1, depth + 2, axis=axis_pos)
    inner_last = lax.slice_in_dim(padded, length - depth - 1, length - depth, axis=axis_pos)
    inner_before = lax.slice_in_dim(padded, length - depth - 2, length - depth - 1, axis=axis_pos)
    step_low = inner_first - inner_second
    step_high = inner_last - inner_before
    low_side = jnp.concatenate(
        [inner_first + float(count) * step_low for count in range(depth, 0, -1)], axis=axis_pos
    )
    high_side = jnp.concatenate(
        [inner_last + float(count) * step_high for count in range(1, depth + 1)], axis=axis_pos
    )
    low_side = jnp.where(at_first, low_side, lax.slice_in_dim(padded, 0, depth, axis=axis_pos))
    high_side = jnp.where(
        at_last, high_side, lax.slice_in_dim(padded, length - depth, length, axis=axis_pos)
    )
    return jnp.concatenate(
        [low_side, lax.slice_in_dim(padded, depth, length - depth, axis=axis_pos), high_side],
        axis=axis_pos,
    )


def radial_damping(values, axis_pos):
    count = values.shape[axis_pos]
    first_row = lax.slice_in_dim(values, 0, 1, axis=axis_pos)
    last_row = lax.slice_in_dim(values, count - 1, count, axis=axis_pos)
    extended = jnp.concatenate([first_row, first_row, values, last_row, last_row], axis=axis_pos)
    return (
        lax.slice_in_dim(extended, 4, 4 + count, axis=axis_pos)
        - 4.0 * lax.slice_in_dim(extended, 3, 3 + count, axis=axis_pos)
        + 6.0 * values
        - 4.0 * lax.slice_in_dim(extended, 1, 1 + count, axis=axis_pos)
        + lax.slice_in_dim(extended, 0, count, axis=axis_pos)
    )


def unit_normal(earlier, later):
    along_x = later[0] - earlier[0]
    along_y = 1.0 + later[1] - earlier[1]
    length = jnp.sqrt(along_x * along_x + along_y * along_y)
    return jnp.stack([along_x / length, along_y / length])


def wall_amplitude(shape_mode, angle, blade_mask):
    return (shape_mode[0] * jnp.cos(angle) - shape_mode[1] * jnp.sin(angle)) * blade_mask


def lag_shift(series, phase_now, phase_move):
    series_sum = jnp.zeros(series.shape[2:], jnp.float32)
    for number in range(series.shape[0]):
        harmonic = float(number + 1)
        change_cos = jnp.cos(harmonic * (phase_now + phase_move)) - jnp.cos(harmonic * phase_now)
        change_sin = jnp.sin(harmonic * (phase_now + phase_move)) - jnp.sin(harmonic * phase_now)
        series_sum = series_sum + series[number, 0] * change_cos - series[number, 1] * change_sin
    return series_sum


def metric_terms(offset_x, offset_y):
    x_zeta = 1.0 + (offset_x[2:, 1:-1] - offset_x[:-2, 1:-1]) * 0.5
    x_xi = (offset_x[1:-1, 2:] - offset_x[1:-1, :-2]) * 0.5
    y_xi = 1.0 + (offset_y[1:-1, 2:] - offset_y[1:-1, :-2]) * 0.5
    y_zeta = (offset_y[2:, 1:-1] - offset_y[:-2, 1:-1]) * 0.5
    return (x_zeta, x_xi, y_xi, y_zeta)


def geometry(grid_pad):
    x_zeta, x_xi, y_xi, y_zeta = metric_terms(grid_pad[0], grid_pad[1])
    old_zeta, old_xi, oldy_xi, oldy_zeta = metric_terms(
        grid_pad[0] - grid_pad[2], grid_pad[1] - grid_pad[3]
    )
    volume_new = (x_zeta * y_xi - x_xi * y_zeta)[1:-1, 1:-1]
    volume_old = (old_zeta * oldy_xi - old_xi * oldy_zeta)[1:-1, 1:-1]
    speed_x = grid_pad[2][1:-1, 1:-1] / TIME_STEP
    speed_y = grid_pad[3][1:-1, 1:-1] / TIME_STEP
    first_pitch = -y_zeta
    sweep_pitch = first_pitch * speed_x + x_zeta * speed_y
    second_axial = -x_xi
    sweep_axial = y_xi * speed_x + second_axial * speed_y
    return (
        (first_pitch, x_zeta, sweep_pitch, y_xi, second_axial, sweep_axial),
        volume_old,
        volume_new,
    )


def directional(strip_cells, first_coef, second_coef, sweep_term):
    density = strip_cells[0]
    vel_x = strip_cells[1] / density
    vel_y = strip_cells[2] / density
    energy = strip_cells[3]
    pressure = (HEAT_RATIO - 1.0) * (energy - 0.5 * density * (vel_x * vel_x + vel_y * vel_y))
    flux_x = jnp.stack(
        [
            strip_cells[1],
            strip_cells[1] * vel_x + pressure,
            strip_cells[1] * vel_y,
            (energy + pressure) * vel_x,
        ]
    )
    flux_y = jnp.stack(
        [
            strip_cells[2],
            strip_cells[2] * vel_x,
            strip_cells[2] * vel_y + pressure,
            (energy + pressure) * vel_y,
        ]
    )
    return first_coef * flux_x + second_coef * flux_y - sweep_term * strip_cells


def residual(padded, geo_terms):
    first_pitch, second_pitch, sweep_pitch, first_axial, second_axial, sweep_axial = geo_terms
    pitch_flux = directional(
        padded[:, 2:-2, 1:-1], first_pitch[1:-1], second_pitch[1:-1], sweep_pitch[1:-1]
    )
    axial_flux = directional(
        padded[:, 1:-1, 2:-2], first_axial[:, 1:-1], second_axial[:, 1:-1], sweep_axial[:, 1:-1]
    )
    divergence = (pitch_flux[:, :, 2:] - pitch_flux[:, :, :-2]) * 0.5 + (
        axial_flux[:, 2:] - axial_flux[:, :-2]
    ) * 0.5
    centre = padded[:, 2:-2, 2:-2]
    fourth = (
        padded[:, 2:-2, 4:]
        - 4.0 * padded[:, 2:-2, 3:-1]
        + 6.0 * centre
        - 4.0 * padded[:, 2:-2, 1:-3]
        + padded[:, 2:-2, :-4]
        + (
            padded[:, 4:, 2:-2]
            - 4.0 * padded[:, 3:-1, 2:-2]
            + 6.0 * centre
            - 4.0 * padded[:, 1:-3, 2:-2]
            + padded[:, :-4, 2:-2]
        )
    )
    return divergence + DAMPING * fourth + DAMPING * radial_damping(centre, 3)


def flow_ghosts(
    row_zero,
    row_one,
    row_last,
    row_before,
    wrap_low0,
    wrap_low1,
    wrap_high0,
    wrap_high1,
    blade_flag,
    corr_low,
    corr_high,
):
    sign_flip = jnp.array([1.0, 1.0, -1.0, 1.0], jnp.float32).reshape(
        (4,) + (1,) * (row_zero.ndim - 1)
    )
    ghost_m2 = jnp.where(blade_flag, row_one * sign_flip, wrap_low0 + corr_low)
    ghost_m1 = jnp.where(blade_flag, row_zero * sign_flip, wrap_low1 + corr_low)
    ghost_p0 = jnp.where(blade_flag, row_last * sign_flip, wrap_high0 + corr_high)
    ghost_p1 = jnp.where(blade_flag, row_before * sign_flip, wrap_high1 + corr_high)
    return (ghost_m2, ghost_m1, ghost_p0, ghost_p1)


def finish_flow(
    padded, depth, row_flag, corr_low, corr_high, low_end, high_end, first_end, last_end
):
    middle_rows = padded[:, 2:-2]
    width = middle_rows.shape[2]
    ghost_m2, ghost_m1, ghost_p0, ghost_p1 = flow_ghosts(
        middle_rows[:, :, 2],
        middle_rows[:, :, 3],
        middle_rows[:, :, width - 3],
        middle_rows[:, :, width - 4],
        middle_rows[:, :, 0],
        middle_rows[:, :, 1],
        middle_rows[:, :, width - 2],
        middle_rows[:, :, width - 1],
        row_flag[:, None],
        corr_low,
        corr_high,
    )
    low_pair = jnp.where(low_end, jnp.stack([ghost_m2, ghost_m1], 2), middle_rows[:, :, 0:2])
    high_pair = jnp.where(
        high_end, jnp.stack([ghost_p0, ghost_p1], 2), middle_rows[:, :, width - 2 :]
    )
    middle_rows = jnp.concatenate([low_pair, middle_rows[:, :, 2 : width - 2], high_pair], 2)
    whole = jnp.concatenate([padded[:, 0:2], middle_rows, padded[:, -2:]], 1)
    top_copy = jnp.repeat(whole[:, depth : depth + 1], depth, axis=1)
    bottom_copy = jnp.repeat(whole[:, -depth - 1 : -depth], depth, axis=1)
    top_rows = jnp.where(first_end, top_copy, whole[:, :depth])
    bottom_rows = jnp.where(last_end, bottom_copy, whole[:, -depth:])
    return jnp.concatenate([top_rows, whole[:, depth:-depth], bottom_rows], 1)


def _flux(rho, mx, my, en, first, second, sweep):
    inverse = 1.0 / rho
    u = mx * inverse
    v = my * inverse
    pr = (HEAT_RATIO - 1.0) * (en - 0.5 * rho * (u * u + v * v))
    ep = en + pr
    return (
        first * mx + second * my - sweep * rho,
        first * (mx * u + pr) + second * (my * u) - sweep * mx,
        first * (mx * v) + second * (my * v + pr) - sweep * my,
        first * (ep * u) + second * (ep * v) - sweep * en,
    )


def _radial_pairs(c0, lane, forward):
    width = c0.shape[-1]
    last = width - 1
    one_a = pltpu.roll(c0, 1, 1)
    one_b = pltpu.roll(c0, last, 1)
    two_a = pltpu.roll(c0, 2, 1)
    two_b = pltpu.roll(c0, width - 2, 1)
    m1 = jnp.where(lane == 0, c0, jnp.where(forward, one_a, one_b))
    p1 = jnp.where(lane == last, c0, jnp.where(forward, one_b, one_a))
    m2 = jnp.where(lane <= 1, m1, jnp.where(forward, two_a, two_b))
    p2 = jnp.where(lane >= last - 1, p1, jnp.where(forward, two_b, two_a))
    return m1 + p1, m2 + p2


def _volume(grid, a, npch, old):
    def comp(c, row, lo, hi):
        value = grid[c, row, lo:hi]
        if old:
            value = value - grid[c + 2, row, lo:hi]
        return value

    x_zeta = 1.0 + (comp(0, a + 3, 2, npch + 2) - comp(0, a + 1, 2, npch + 2)) * 0.5
    x_xi = (comp(0, a + 2, 3, npch + 3) - comp(0, a + 2, 1, npch + 1)) * 0.5
    y_xi = 1.0 + (comp(1, a + 2, 3, npch + 3) - comp(1, a + 2, 1, npch + 1)) * 0.5
    y_zeta = (comp(1, a + 3, 2, npch + 2) - comp(1, a + 1, 2, npch + 2)) * 0.5
    return x_zeta * y_xi - x_xi * y_zeta


def _section_body(scale, pad, grid, q0, out, af, pf):
    na = out.shape[1]
    npch = out.shape[2]
    width = out.shape[3]

    def axial_row(j, carry):
        x_xi = (grid[0, j + 1, 3 : npch + 3] - grid[0, j + 1, 1 : npch + 1]) * 0.5
        y_xi = 1.0 + (grid[1, j + 1, 3 : npch + 3] - grid[1, j + 1, 1 : npch + 1]) * 0.5
        speed_x = grid[2, j + 1, 2 : npch + 2] / TIME_STEP
        speed_y = grid[3, j + 1, 2 : npch + 2] / TIME_STEP
        second = -x_xi
        sweep = y_xi * speed_x + second * speed_y
        q = [pad[k, j + 1, 2 : npch + 2] for k in range(4)]
        f = _flux(*q, y_xi, second, sweep)
        for k in range(4):
            af[k, j] = f[k]
        return carry

    lax.fori_loop(0, na + 2, axial_row, 0)
    lane = lax.broadcasted_iota(jnp.int32, (npch, width), 1)
    probe = pltpu.roll(lane, 1, 1)
    forward = probe == jnp.where(lane == 0, width - 1, lane - 1)

    def row(a, carry):
        x_zeta = 1.0 + (grid[0, a + 3, 1 : npch + 3] - grid[0, a + 1, 1 : npch + 3]) * 0.5
        y_zeta = (grid[1, a + 3, 1 : npch + 3] - grid[1, a + 1, 1 : npch + 3]) * 0.5
        speed_x = grid[2, a + 2, 1 : npch + 3] / TIME_STEP
        speed_y = grid[3, a + 2, 1 : npch + 3] / TIME_STEP
        first = -y_zeta
        sweep = first * speed_x + x_zeta * speed_y
        q = [pad[k, a + 2, 1 : npch + 3] for k in range(4)]
        f = _flux(*q, first, x_zeta, sweep)
        for k in range(4):
            pf[k] = f[k]
        volume_old = _volume(grid, a, npch, True)
        inverse_new = 1.0 / _volume(grid, a, npch, False)
        for k in range(4):
            div = (pf[k, 2 : npch + 2] - pf[k, 0:npch]) * 0.5 + (af[k, a + 2] - af[k, a]) * 0.5
            c0 = pad[k, a + 2, 2 : npch + 2]
            near_r, far_r = _radial_pairs(c0, lane, forward)
            near = (
                pad[k, a + 2, 3 : npch + 3]
                + pad[k, a + 2, 1 : npch + 1]
                + pad[k, a + 3, 2 : npch + 2]
                + pad[k, a + 1, 2 : npch + 2]
                + near_r
            )
            far = (
                pad[k, a + 2, 4 : npch + 4]
                + pad[k, a + 2, 0:npch]
                + pad[k, a + 4, 2 : npch + 2]
                + pad[k, a, 2 : npch + 2]
                + far_r
            )
            res = div + DAMPING * (far - 4.0 * near + 18.0 * c0)
            out[k, a] = (volume_old * q0[k, a] - scale * res) * inverse_new
        return carry

    lax.fori_loop(0, na, row, 0)


def section_kernel(padded, grid_pad, start, scale, interpret=False):
    _, na, npch, width = start.shape
    body = lambda *refs: _section_body(scale, *refs)
    cells = na * npch * width
    return pl.pallas_call(
        body,
        out_shape=jax.ShapeDtypeStruct(start.shape, start.dtype),
        scratch_shapes=[
            pltpu.VMEM((4, na + 2, npch, width), jnp.float32),
            pltpu.VMEM((4, npch + 2, width), jnp.float32),
        ],
        compiler_params=pltpu.CompilerParams(vmem_limit_bytes=60 * 1024 * 1024),
        cost_estimate=pl.CostEstimate(
            flops=500 * cells, transcendentals=0, bytes_accessed=4 * 14 * cells
        ),
        interpret=interpret,
    )(padded, grid_pad, start)


def per_device(flow_state, node_offset, blade_mode, phase_angles, lag_series):
    n_pitch = lax.axis_size("pitch")
    n_span = lax.axis_size("span")
    pitch_rows = flow_state.shape[2]
    axial_cols = flow_state.shape[1]
    total_pitch = pitch_rows * n_pitch
    total_axial = axial_cols * n_span
    pitch_at = lax.axis_index("pitch")
    span_at = lax.axis_index("span")
    lead_edge = total_axial // 4
    axial_index = span_at * axial_cols + jnp.arange(axial_cols, dtype=jnp.int32)
    blade_flag = (axial_index >= lead_edge) & (axial_index < total_axial - lead_edge)
    blade_mask = blade_flag.astype(jnp.float32)[:, None]
    phase_now = phase_angles[0]
    phase_lag = phase_angles[1]
    low_guess = wall_amplitude(blade_mode, phase_now, blade_mask) * unit_normal(
        node_offset[:, :, 0], node_offset[:, :, 1]
    )
    high_guess = wall_amplitude(blade_mode, phase_now + phase_lag, blade_mask) * unit_normal(
        node_offset[:, :, pitch_rows - 2], node_offset[:, :, pitch_rows - 1]
    )
    low_wall = low_guess
    high_wall = high_guess
    sent = jnp.where(pitch_at == 0, low_guess, high_guess)
    for shift in range(1, n_pitch):
        got = lax.ppermute(sent, "pitch", [(0, shift), (n_pitch - 1, shift - 1)])
        low_wall = jnp.where(pitch_at == shift, got, low_wall)
        high_wall = jnp.where(pitch_at == shift - 1, got, high_wall)
    pitch_index = pitch_at * pitch_rows + jnp.arange(pitch_rows, dtype=jnp.int32)
    blend_row = (pitch_index.astype(jnp.float32) / (total_pitch - 1))[:, None]
    shift_field = (1.0 - blend_row) * low_wall[:, :, None, :] + blend_row * high_wall[:, :, None, :]
    moved_offset = node_offset + shift_field
    rim_width = 2
    node_pad = padded_2(node_offset, (("pitch", 2), ("span", 1)), rim_width)
    wall_pad = padded_2(jnp.stack([low_wall, high_wall]), (("span", 2),), rim_width)
    pitch_wide = pitch_at * pitch_rows + jnp.arange(
        -rim_width, pitch_rows + rim_width, dtype=jnp.int32
    )
    blend_wide = (pitch_wide.astype(jnp.float32) / (total_pitch - 1))[:, None]
    shift_pad = (1.0 - blend_wide) * wall_pad[0][:, :, None, :] + blend_wide * wall_pad[1][
        :, :, None, :
    ]
    grid_pad = jnp.concatenate([node_pad + shift_pad, shift_pad], 0)
    first_pad = padded_cross(flow_state, rim_width)
    low_end = pitch_at == 0
    high_end = pitch_at == n_pitch - 1
    first_end = span_at == 0
    last_end = span_at == n_span - 1
    grid_pad = fill_ends(grid_pad, 1, rim_width, first_end, last_end)
    grid_pad = fill_ends(grid_pad, 2, 2, low_end, high_end)
    corr_low = lag_shift(lag_series[1], phase_now, -phase_lag)
    corr_high = lag_shift(lag_series[0], phase_now, phase_lag)
    padded = finish_flow(
        first_pad, 2, blade_flag, corr_low, corr_high, low_end, high_end, first_end, last_end
    )
    section_one = section_kernel(padded, grid_pad, flow_state, SECTION_WEIGHTS[0] * TIME_STEP)
    second_pad = padded_cross(section_one, 2)
    padded = finish_flow(
        second_pad, 2, blade_flag, corr_low, corr_high, low_end, high_end, first_end, last_end
    )
    current = section_kernel(padded, grid_pad, flow_state, SECTION_WEIGHTS[1] * TIME_STEP)
    return (current, moved_offset)


def solution(mesh):
    placed = (
        P(None, "span", "pitch", None),
        P(None, "span", "pitch", None),
        P(None, "span", None),
        P(),
        P(None, None, None, None, "span", None),
    )
    return jax.shard_map(
        per_device,
        mesh=mesh,
        in_specs=placed,
        out_specs=(P(None, "span", "pitch", None), P(None, "span", "pitch", None)),
        check_vma=False,
    )
```

```python
import jax
import jax.numpy as jnp
from jax import lax
from jax.sharding import PartitionSpec as P
from jax.experimental import pallas as pl
from jax.experimental.pallas import tpu as pltpu

HEAT_RATIO = 1.4
TIME_STEP = 0.25
DAMPING = 0.02
SECTION_WEIGHTS = (0.5, 1.0)


def broadcast(value, axis, root):
    mine = lax.axis_index(axis) == root
    return lax.psum(jnp.where(mine, value, jnp.zeros_like(value)), axis)


def padded_2(block, sides, width):
    for axis, dim in sides:
        count = lax.axis_size(axis)
        forward = [(i, i + 1) for i in range(count - 1)]
        forward.append((count - 1, 0))
        backward = [(target, source) for source, target in forward]
        low = lax.ppermute(
            lax.slice_in_dim(block, block.shape[dim] - width, None, axis=dim), axis, forward
        )
        high = lax.ppermute(lax.slice_in_dim(block, 0, width, axis=dim), axis, backward)
        block = jnp.concatenate([low, block, high], axis=dim)
    return block


def padded_cross(block, width):
    rims = []
    for axis, dim in (("pitch", 2), ("span", 1)):
        count = lax.axis_size(axis)
        forward = [(i, (i + 1) % count) for i in range(count)]
        backward = [(target, source) for source, target in forward]
        low = lax.ppermute(
            lax.slice_in_dim(block, block.shape[dim] - width, None, axis=dim), axis, forward
        )
        high = lax.ppermute(lax.slice_in_dim(block, 0, width, axis=dim), axis, backward)
        rims.append((low, high))
    (pitch_low, pitch_high), (span_low, span_high) = rims
    middle = jnp.concatenate([pitch_low, block, pitch_high], axis=2)
    corner = jnp.zeros(span_low.shape[:2] + (width,) + span_low.shape[3:], block.dtype)
    top = jnp.concatenate([corner, span_low, corner], axis=2)
    bottom = jnp.concatenate([corner, span_high, corner], axis=2)
    return jnp.concatenate([top, middle, bottom], axis=1)


def fill_ends(padded, axis_pos, depth, at_first, at_last):
    length = padded.shape[axis_pos]
    inner_first = lax.slice_in_dim(padded, depth, depth + 1, axis=axis_pos)
    inner_second = lax.slice_in_dim(padded, depth + 1, depth + 2, axis=axis_pos)
    inner_last = lax.slice_in_dim(padded, length - depth - 1, length - depth, axis=axis_pos)
    inner_before = lax.slice_in_dim(padded, length - depth - 2, length - depth - 1, axis=axis_pos)
    step_low = inner_first - inner_second
    step_high = inner_last - inner_before
    low_side = jnp.concatenate(
        [inner_first + float(count) * step_low for count in range(depth, 0, -1)], axis=axis_pos
    )
    high_side = jnp.concatenate(
        [inner_last + float(count) * step_high for count in range(1, depth + 1)], axis=axis_pos
    )
    low_side = jnp.where(at_first, low_side, lax.slice_in_dim(padded, 0, depth, axis=axis_pos))
    high_side = jnp.where(
        at_last, high_side, lax.slice_in_dim(padded, length - depth, length, axis=axis_pos)
    )
    return jnp.concatenate(
        [low_side, lax.slice_in_dim(padded, depth, length - depth, axis=axis_pos), high_side],
        axis=axis_pos,
    )


def radial_damping(values, axis_pos):
    count = values.shape[axis_pos]
    first_row = lax.slice_in_dim(values, 0, 1, axis=axis_pos)
    last_row = lax.slice_in_dim(values, count - 1, count, axis=axis_pos)
    extended = jnp.concatenate([first_row, first_row, values, last_row, last_row], axis=axis_pos)
    return (
        lax.slice_in_dim(extended, 4, 4 + count, axis=axis_pos)
        - 4.0 * lax.slice_in_dim(extended, 3, 3 + count, axis=axis_pos)
        + 6.0 * values
        - 4.0 * lax.slice_in_dim(extended, 1, 1 + count, axis=axis_pos)
        + lax.slice_in_dim(extended, 0, count, axis=axis_pos)
    )


def unit_normal(earlier, later):
    along_x = later[0] - earlier[0]
    along_y = 1.0 + later[1] - earlier[1]
    length = jnp.sqrt(along_x * along_x + along_y * along_y)
    return jnp.stack([along_x / length, along_y / length])


def wall_amplitude(shape_mode, angle, blade_mask):
    return (shape_mode[0] * jnp.cos(angle) - shape_mode[1] * jnp.sin(angle)) * blade_mask


def lag_shift(series, phase_now, phase_move):
    series_sum = jnp.zeros(series.shape[2:], jnp.float32)
    for number in range(series.shape[0]):
        harmonic = float(number + 1)
        change_cos = jnp.cos(harmonic * (phase_now + phase_move)) - jnp.cos(harmonic * phase_now)
        change_sin = jnp.sin(harmonic * (phase_now + phase_move)) - jnp.sin(harmonic * phase_now)
        series_sum = series_sum + series[number, 0] * change_cos - series[number, 1] * change_sin
    return series_sum


def metric_terms(offset_x, offset_y):
    x_zeta = 1.0 + (offset_x[2:, 1:-1] - offset_x[:-2, 1:-1]) * 0.5
    x_xi = (offset_x[1:-1, 2:] - offset_x[1:-1, :-2]) * 0.5
    y_xi = 1.0 + (offset_y[1:-1, 2:] - offset_y[1:-1, :-2]) * 0.5
    y_zeta = (offset_y[2:, 1:-1] - offset_y[:-2, 1:-1]) * 0.5
    return (x_zeta, x_xi, y_xi, y_zeta)


def geometry(grid_pad):
    x_zeta, x_xi, y_xi, y_zeta = metric_terms(grid_pad[0], grid_pad[1])
    old_zeta, old_xi, oldy_xi, oldy_zeta = metric_terms(
        grid_pad[0] - grid_pad[2], grid_pad[1] - grid_pad[3]
    )
    volume_new = (x_zeta * y_xi - x_xi * y_zeta)[1:-1, 1:-1]
    volume_old = (old_zeta * oldy_xi - old_xi * oldy_zeta)[1:-1, 1:-1]
    speed_x = grid_pad[2][1:-1, 1:-1] / TIME_STEP
    speed_y = grid_pad[3][1:-1, 1:-1] / TIME_STEP
    first_pitch = -y_zeta
    sweep_pitch = first_pitch * speed_x + x_zeta * speed_y
    second_axial = -x_xi
    sweep_axial = y_xi * speed_x + second_axial * speed_y
    return (
        (first_pitch, x_zeta, sweep_pitch, y_xi, second_axial, sweep_axial),
        volume_old,
        volume_new,
    )


def directional(strip_cells, first_coef, second_coef, sweep_term):
    density = strip_cells[0]
    vel_x = strip_cells[1] / density
    vel_y = strip_cells[2] / density
    energy = strip_cells[3]
    pressure = (HEAT_RATIO - 1.0) * (energy - 0.5 * density * (vel_x * vel_x + vel_y * vel_y))
    flux_x = jnp.stack(
        [
            strip_cells[1],
            strip_cells[1] * vel_x + pressure,
            strip_cells[1] * vel_y,
            (energy + pressure) * vel_x,
        ]
    )
    flux_y = jnp.stack(
        [
            strip_cells[2],
            strip_cells[2] * vel_x,
            strip_cells[2] * vel_y + pressure,
            (energy + pressure) * vel_y,
        ]
    )
    return first_coef * flux_x + second_coef * flux_y - sweep_term * strip_cells


def residual(padded, geo_terms):
    first_pitch, second_pitch, sweep_pitch, first_axial, second_axial, sweep_axial = geo_terms
    pitch_flux = directional(
        padded[:, 2:-2, 1:-1], first_pitch[1:-1], second_pitch[1:-1], sweep_pitch[1:-1]
    )
    axial_flux = directional(
        padded[:, 1:-1, 2:-2], first_axial[:, 1:-1], second_axial[:, 1:-1], sweep_axial[:, 1:-1]
    )
    divergence = (pitch_flux[:, :, 2:] - pitch_flux[:, :, :-2]) * 0.5 + (
        axial_flux[:, 2:] - axial_flux[:, :-2]
    ) * 0.5
    centre = padded[:, 2:-2, 2:-2]
    fourth = (
        padded[:, 2:-2, 4:]
        - 4.0 * padded[:, 2:-2, 3:-1]
        + 6.0 * centre
        - 4.0 * padded[:, 2:-2, 1:-3]
        + padded[:, 2:-2, :-4]
        + (
            padded[:, 4:, 2:-2]
            - 4.0 * padded[:, 3:-1, 2:-2]
            + 6.0 * centre
            - 4.0 * padded[:, 1:-3, 2:-2]
            + padded[:, :-4, 2:-2]
        )
    )
    return divergence + DAMPING * fourth + DAMPING * radial_damping(centre, 3)


def flow_ghosts(
    row_zero,
    row_one,
    row_last,
    row_before,
    wrap_low0,
    wrap_low1,
    wrap_high0,
    wrap_high1,
    blade_flag,
    corr_low,
    corr_high,
):
    sign_flip = jnp.array([1.0, 1.0, -1.0, 1.0], jnp.float32).reshape(
        (4,) + (1,) * (row_zero.ndim - 1)
    )
    ghost_m2 = jnp.where(blade_flag, row_one * sign_flip, wrap_low0 + corr_low)
    ghost_m1 = jnp.where(blade_flag, row_zero * sign_flip, wrap_low1 + corr_low)
    ghost_p0 = jnp.where(blade_flag, row_last * sign_flip, wrap_high0 + corr_high)
    ghost_p1 = jnp.where(blade_flag, row_before * sign_flip, wrap_high1 + corr_high)
    return (ghost_m2, ghost_m1, ghost_p0, ghost_p1)


def finish_flow(
    padded, depth, row_flag, corr_low, corr_high, low_end, high_end, first_end, last_end
):
    middle_rows = padded[:, 2:-2]
    width = middle_rows.shape[2]
    ghost_m2, ghost_m1, ghost_p0, ghost_p1 = flow_ghosts(
        middle_rows[:, :, 2],
        middle_rows[:, :, 3],
        middle_rows[:, :, width - 3],
        middle_rows[:, :, width - 4],
        middle_rows[:, :, 0],
        middle_rows[:, :, 1],
        middle_rows[:, :, width - 2],
        middle_rows[:, :, width - 1],
        row_flag[:, None],
        corr_low,
        corr_high,
    )
    low_pair = jnp.where(low_end, jnp.stack([ghost_m2, ghost_m1], 2), middle_rows[:, :, 0:2])
    high_pair = jnp.where(
        high_end, jnp.stack([ghost_p0, ghost_p1], 2), middle_rows[:, :, width - 2 :]
    )
    middle_rows = jnp.concatenate([low_pair, middle_rows[:, :, 2 : width - 2], high_pair], 2)
    whole = jnp.concatenate([padded[:, 0:2], middle_rows, padded[:, -2:]], 1)
    top_copy = jnp.repeat(whole[:, depth : depth + 1], depth, axis=1)
    bottom_copy = jnp.repeat(whole[:, -depth - 1 : -depth], depth, axis=1)
    top_rows = jnp.where(first_end, top_copy, whole[:, :depth])
    bottom_rows = jnp.where(last_end, bottom_copy, whole[:, -depth:])
    return jnp.concatenate([top_rows, whole[:, depth:-depth], bottom_rows], 1)


def _flux(rho, mx, my, en, first, second, sweep):
    inverse = 1.0 / rho
    u = mx * inverse
    v = my * inverse
    pr = (HEAT_RATIO - 1.0) * (en - 0.5 * rho * (u * u + v * v))
    ep = en + pr
    return (
        first * mx + second * my - sweep * rho,
        first * (mx * u + pr) + second * (my * u) - sweep * mx,
        first * (mx * v) + second * (my * v + pr) - sweep * my,
        first * (ep * u) + second * (ep * v) - sweep * en,
    )


def _radial_pairs(c0, lane, forward):
    width = c0.shape[-1]
    last = width - 1
    one_a = pltpu.roll(c0, 1, 1)
    one_b = pltpu.roll(c0, last, 1)
    two_a = pltpu.roll(c0, 2, 1)
    two_b = pltpu.roll(c0, width - 2, 1)
    m1 = jnp.where(lane == 0, c0, jnp.where(forward, one_a, one_b))
    p1 = jnp.where(lane == last, c0, jnp.where(forward, one_b, one_a))
    m2 = jnp.where(lane <= 1, m1, jnp.where(forward, two_a, two_b))
    p2 = jnp.where(lane >= last - 1, p1, jnp.where(forward, two_b, two_a))
    return m1 + p1, m2 + p2


def _volume(grid, a, npch, old):
    def comp(c, row, lo, hi):
        value = grid[c, row, lo:hi]
        if old:
            value = value - grid[c + 2, row, lo:hi]
        return value

    x_zeta = 1.0 + (comp(0, a + 3, 2, npch + 2) - comp(0, a + 1, 2, npch + 2)) * 0.5
    x_xi = (comp(0, a + 2, 3, npch + 3) - comp(0, a + 2, 1, npch + 1)) * 0.5
    y_xi = 1.0 + (comp(1, a + 2, 3, npch + 3) - comp(1, a + 2, 1, npch + 1)) * 0.5
    y_zeta = (comp(1, a + 3, 2, npch + 2) - comp(1, a + 1, 2, npch + 2)) * 0.5
    return x_zeta * y_xi - x_xi * y_zeta


def _section_body(scale, pad_hbm, grid_hbm, q0_hbm, out, af, pf, pad, grid, q0, sems):
    na = out.shape[1]
    npch = out.shape[2]
    width = out.shape[3]

    def row_copy(which, j):
        source, target = ((pad_hbm, pad), (grid_hbm, grid), (q0_hbm, q0))[which]
        return pltpu.make_async_copy(
            source.at[:, pl.ds(j, 1)], target.at[:, pl.ds(j, 1)], sems.at[which, j]
        )

    for j in range(na + 4):
        row_copy(0, j).start()
        if 1 <= j <= na + 2:
            row_copy(1, j).start()
    for j in range(na):
        row_copy(2, j).start()

    def axial_row(j, carry):
        row_copy(0, j + 1).wait()
        row_copy(1, j + 1).wait()
        x_xi = (grid[0, j + 1, 3 : npch + 3] - grid[0, j + 1, 1 : npch + 1]) * 0.5
        y_xi = 1.0 + (grid[1, j + 1, 3 : npch + 3] - grid[1, j + 1, 1 : npch + 1]) * 0.5
        speed_x = grid[2, j + 1, 2 : npch + 2] / TIME_STEP
        speed_y = grid[3, j + 1, 2 : npch + 2] / TIME_STEP
        second = -x_xi
        sweep = y_xi * speed_x + second * speed_y
        q = [pad[k, j + 1, 2 : npch + 2] for k in range(4)]
        f = _flux(*q, y_xi, second, sweep)
        for k in range(4):
            af[k, j] = f[k]
        return carry

    lax.fori_loop(0, na + 2, axial_row, 0)
    lane = lax.broadcasted_iota(jnp.int32, (npch, width), 1)
    probe = pltpu.roll(lane, 1, 1)
    forward = probe == jnp.where(lane == 0, width - 1, lane - 1)

    row_copy(0, 0).wait()
    row_copy(0, na + 3).wait()

    def row(a, carry):
        row_copy(2, a).wait()
        x_zeta = 1.0 + (grid[0, a + 3, 1 : npch + 3] - grid[0, a + 1, 1 : npch + 3]) * 0.5
        y_zeta = (grid[1, a + 3, 1 : npch + 3] - grid[1, a + 1, 1 : npch + 3]) * 0.5
        speed_x = grid[2, a + 2, 1 : npch + 3] / TIME_STEP
        speed_y = grid[3, a + 2, 1 : npch + 3] / TIME_STEP
        first = -y_zeta
        sweep = first * speed_x + x_zeta * speed_y
        q = [pad[k, a + 2, 1 : npch + 3] for k in range(4)]
        f = _flux(*q, first, x_zeta, sweep)
        for k in range(4):
            pf[k] = f[k]
        volume_old = _volume(grid, a, npch, True)
        inverse_new = 1.0 / _volume(grid, a, npch, False)
        for k in range(4):
            div = (pf[k, 2 : npch + 2] - pf[k, 0:npch]) * 0.5 + (af[k, a + 2] - af[k, a]) * 0.5
            c0 = pad[k, a + 2, 2 : npch + 2]
            near_r, far_r = _radial_pairs(c0, lane, forward)
            near = (
                pad[k, a + 2, 3 : npch + 3]
                + pad[k, a + 2, 1 : npch + 1]
                + pad[k, a + 3, 2 : npch + 2]
                + pad[k, a + 1, 2 : npch + 2]
                + near_r
            )
            far = (
                pad[k, a + 2, 4 : npch + 4]
                + pad[k, a + 2, 0:npch]
                + pad[k, a + 4, 2 : npch + 2]
                + pad[k, a, 2 : npch + 2]
                + far_r
            )
            res = div + DAMPING * (far - 4.0 * near + 18.0 * c0)
            out[k, a] = (volume_old * q0[k, a] - scale * res) * inverse_new
        return carry

    lax.fori_loop(0, na, row, 0)


def section_kernel(padded, grid_pad, start, scale, interpret=False):
    _, na, npch, width = start.shape
    body = lambda *refs: _section_body(scale, *refs)
    cells = na * npch * width
    return pl.pallas_call(
        body,
        out_shape=jax.ShapeDtypeStruct(start.shape, start.dtype),
        in_specs=[pl.BlockSpec(memory_space=pl.ANY)] * 3,
        scratch_shapes=[
            pltpu.VMEM((4, na + 2, npch, width), jnp.float32),
            pltpu.VMEM((4, npch + 2, width), jnp.float32),
            pltpu.VMEM(padded.shape, jnp.float32),
            pltpu.VMEM(grid_pad.shape, jnp.float32),
            pltpu.VMEM(start.shape, jnp.float32),
            pltpu.SemaphoreType.DMA((3, na + 4)),
        ],
        compiler_params=pltpu.CompilerParams(vmem_limit_bytes=60 * 1024 * 1024),
        cost_estimate=pl.CostEstimate(
            flops=500 * cells, transcendentals=0, bytes_accessed=4 * 14 * cells
        ),
        interpret=interpret,
    )(padded, grid_pad, start)


def per_device(flow_state, node_offset, blade_mode, phase_angles, lag_series):
    n_pitch = lax.axis_size("pitch")
    n_span = lax.axis_size("span")
    pitch_rows = flow_state.shape[2]
    axial_cols = flow_state.shape[1]
    total_pitch = pitch_rows * n_pitch
    total_axial = axial_cols * n_span
    pitch_at = lax.axis_index("pitch")
    span_at = lax.axis_index("span")
    lead_edge = total_axial // 4
    axial_index = span_at * axial_cols + jnp.arange(axial_cols, dtype=jnp.int32)
    blade_flag = (axial_index >= lead_edge) & (axial_index < total_axial - lead_edge)
    blade_mask = blade_flag.astype(jnp.float32)[:, None]
    phase_now = phase_angles[0]
    phase_lag = phase_angles[1]
    low_guess = wall_amplitude(blade_mode, phase_now, blade_mask) * unit_normal(
        node_offset[:, :, 0], node_offset[:, :, 1]
    )
    high_guess = wall_amplitude(blade_mode, phase_now + phase_lag, blade_mask) * unit_normal(
        node_offset[:, :, pitch_rows - 2], node_offset[:, :, pitch_rows - 1]
    )
    low_wall = low_guess
    high_wall = high_guess
    sent = jnp.where(pitch_at == 0, low_guess, high_guess)
    for shift in range(1, n_pitch):
        got = lax.ppermute(sent, "pitch", [(0, shift), (n_pitch - 1, shift - 1)])
        low_wall = jnp.where(pitch_at == shift, got, low_wall)
        high_wall = jnp.where(pitch_at == shift - 1, got, high_wall)
    pitch_index = pitch_at * pitch_rows + jnp.arange(pitch_rows, dtype=jnp.int32)
    blend_row = (pitch_index.astype(jnp.float32) / (total_pitch - 1))[:, None]
    shift_field = (1.0 - blend_row) * low_wall[:, :, None, :] + blend_row * high_wall[:, :, None, :]
    moved_offset = node_offset + shift_field
    grid_field = jnp.concatenate([moved_offset, shift_field], 0)
    rim_width = 2
    grid_pad = padded_2(grid_field, (("pitch", 2), ("span", 1)), rim_width)
    first_pad = padded_cross(flow_state, rim_width)
    low_end = pitch_at == 0
    high_end = pitch_at == n_pitch - 1
    first_end = span_at == 0
    last_end = span_at == n_span - 1
    grid_pad = fill_ends(grid_pad, 1, rim_width, first_end, last_end)
    grid_pad = fill_ends(grid_pad, 2, 2, low_end, high_end)
    corr_low = lag_shift(lag_series[1], phase_now, -phase_lag)
    corr_high = lag_shift(lag_series[0], phase_now, phase_lag)
    padded = finish_flow(
        first_pad, 2, blade_flag, corr_low, corr_high, low_end, high_end, first_end, last_end
    )
    section_one = section_kernel(padded, grid_pad, flow_state, SECTION_WEIGHTS[0] * TIME_STEP)
    second_pad = padded_cross(section_one, 2)
    padded = finish_flow(
        second_pad, 2, blade_flag, corr_low, corr_high, low_end, high_end, first_end, last_end
    )
    current = section_kernel(padded, grid_pad, flow_state, SECTION_WEIGHTS[1] * TIME_STEP)
    return (current, moved_offset)


def solution(mesh):
    placed = (
        P(None, "span", "pitch", None),
        P(None, "span", "pitch", None),
        P(None, "span", None),
        P(),
        P(None, None, None, None, "span", None),
    )
    return jax.shard_map(
        per_device,
        mesh=mesh,
        in_specs=placed,
        out_specs=(P(None, "span", "pitch", None), P(None, "span", "pitch", None)),
        check_vma=False,
    )
```

```python
import jax
import jax.numpy as jnp
from jax import lax
from jax.sharding import PartitionSpec as P
from jax.experimental import pallas as pl
from jax.experimental.pallas import tpu as pltpu

HEAT_RATIO = 1.4
TIME_STEP = 0.25
DAMPING = 0.02
SECTION_WEIGHTS = (0.5, 1.0)


def broadcast(value, axis, root):
    mine = lax.axis_index(axis) == root
    return lax.psum(jnp.where(mine, value, jnp.zeros_like(value)), axis)


def padded_2(block, sides, width):
    for axis, dim in sides:
        count = lax.axis_size(axis)
        forward = [(i, i + 1) for i in range(count - 1)]
        forward.append((count - 1, 0))
        backward = [(target, source) for source, target in forward]
        low = lax.ppermute(
            lax.slice_in_dim(block, block.shape[dim] - width, None, axis=dim), axis, forward
        )
        high = lax.ppermute(lax.slice_in_dim(block, 0, width, axis=dim), axis, backward)
        block = jnp.concatenate([low, block, high], axis=dim)
    return block


def padded_cross(block, width):
    rims = []
    for axis, dim in (("pitch", 2), ("span", 1)):
        count = lax.axis_size(axis)
        forward = [(i, (i + 1) % count) for i in range(count)]
        backward = [(target, source) for source, target in forward]
        low = lax.ppermute(
            lax.slice_in_dim(block, block.shape[dim] - width, None, axis=dim), axis, forward
        )
        high = lax.ppermute(lax.slice_in_dim(block, 0, width, axis=dim), axis, backward)
        rims.append((low, high))
    (pitch_low, pitch_high), (span_low, span_high) = rims
    middle = jnp.concatenate([pitch_low, block, pitch_high], axis=2)
    corner = jnp.zeros(span_low.shape[:2] + (width,) + span_low.shape[3:], block.dtype)
    top = jnp.concatenate([corner, span_low, corner], axis=2)
    bottom = jnp.concatenate([corner, span_high, corner], axis=2)
    return jnp.concatenate([top, middle, bottom], axis=1)


def fill_ends(padded, axis_pos, depth, at_first, at_last):
    length = padded.shape[axis_pos]
    inner_first = lax.slice_in_dim(padded, depth, depth + 1, axis=axis_pos)
    inner_second = lax.slice_in_dim(padded, depth + 1, depth + 2, axis=axis_pos)
    inner_last = lax.slice_in_dim(padded, length - depth - 1, length - depth, axis=axis_pos)
    inner_before = lax.slice_in_dim(padded, length - depth - 2, length - depth - 1, axis=axis_pos)
    step_low = inner_first - inner_second
    step_high = inner_last - inner_before
    low_side = jnp.concatenate(
        [inner_first + float(count) * step_low for count in range(depth, 0, -1)], axis=axis_pos
    )
    high_side = jnp.concatenate(
        [inner_last + float(count) * step_high for count in range(1, depth + 1)], axis=axis_pos
    )
    low_side = jnp.where(at_first, low_side, lax.slice_in_dim(padded, 0, depth, axis=axis_pos))
    high_side = jnp.where(
        at_last, high_side, lax.slice_in_dim(padded, length - depth, length, axis=axis_pos)
    )
    return jnp.concatenate(
        [low_side, lax.slice_in_dim(padded, depth, length - depth, axis=axis_pos), high_side],
        axis=axis_pos,
    )


def radial_damping(values, axis_pos):
    count = values.shape[axis_pos]
    first_row = lax.slice_in_dim(values, 0, 1, axis=axis_pos)
    last_row = lax.slice_in_dim(values, count - 1, count, axis=axis_pos)
    extended = jnp.concatenate([first_row, first_row, values, last_row, last_row], axis=axis_pos)
    return (
        lax.slice_in_dim(extended, 4, 4 + count, axis=axis_pos)
        - 4.0 * lax.slice_in_dim(extended, 3, 3 + count, axis=axis_pos)
        + 6.0 * values
        - 4.0 * lax.slice_in_dim(extended, 1, 1 + count, axis=axis_pos)
        + lax.slice_in_dim(extended, 0, count, axis=axis_pos)
    )


def unit_normal(earlier, later):
    along_x = later[0] - earlier[0]
    along_y = 1.0 + later[1] - earlier[1]
    length = jnp.sqrt(along_x * along_x + along_y * along_y)
    return jnp.stack([along_x / length, along_y / length])


def wall_amplitude(shape_mode, angle, blade_mask):
    return (shape_mode[0] * jnp.cos(angle) - shape_mode[1] * jnp.sin(angle)) * blade_mask


def lag_shift(series, phase_now, phase_move):
    series_sum = jnp.zeros(series.shape[2:], jnp.float32)
    for number in range(series.shape[0]):
        harmonic = float(number + 1)
        change_cos = jnp.cos(harmonic * (phase_now + phase_move)) - jnp.cos(harmonic * phase_now)
        change_sin = jnp.sin(harmonic * (phase_now + phase_move)) - jnp.sin(harmonic * phase_now)
        series_sum = series_sum + series[number, 0] * change_cos - series[number, 1] * change_sin
    return series_sum


def metric_terms(offset_x, offset_y):
    x_zeta = 1.0 + (offset_x[2:, 1:-1] - offset_x[:-2, 1:-1]) * 0.5
    x_xi = (offset_x[1:-1, 2:] - offset_x[1:-1, :-2]) * 0.5
    y_xi = 1.0 + (offset_y[1:-1, 2:] - offset_y[1:-1, :-2]) * 0.5
    y_zeta = (offset_y[2:, 1:-1] - offset_y[:-2, 1:-1]) * 0.5
    return (x_zeta, x_xi, y_xi, y_zeta)


def geometry(grid_pad):
    x_zeta, x_xi, y_xi, y_zeta = metric_terms(grid_pad[0], grid_pad[1])
    old_zeta, old_xi, oldy_xi, oldy_zeta = metric_terms(
        grid_pad[0] - grid_pad[2], grid_pad[1] - grid_pad[3]
    )
    volume_new = (x_zeta * y_xi - x_xi * y_zeta)[1:-1, 1:-1]
    volume_old = (old_zeta * oldy_xi - old_xi * oldy_zeta)[1:-1, 1:-1]
    speed_x = grid_pad[2][1:-1, 1:-1] / TIME_STEP
    speed_y = grid_pad[3][1:-1, 1:-1] / TIME_STEP
    first_pitch = -y_zeta
    sweep_pitch = first_pitch * speed_x + x_zeta * speed_y
    second_axial = -x_xi
    sweep_axial = y_xi * speed_x + second_axial * speed_y
    return (
        (first_pitch, x_zeta, sweep_pitch, y_xi, second_axial, sweep_axial),
        volume_old,
        volume_new,
    )


def directional(strip_cells, first_coef, second_coef, sweep_term):
    density = strip_cells[0]
    vel_x = strip_cells[1] / density
    vel_y = strip_cells[2] / density
    energy = strip_cells[3]
    pressure = (HEAT_RATIO - 1.0) * (energy - 0.5 * density * (vel_x * vel_x + vel_y * vel_y))
    flux_x = jnp.stack(
        [
            strip_cells[1],
            strip_cells[1] * vel_x + pressure,
            strip_cells[1] * vel_y,
            (energy + pressure) * vel_x,
        ]
    )
    flux_y = jnp.stack(
        [
            strip_cells[2],
            strip_cells[2] * vel_x,
            strip_cells[2] * vel_y + pressure,
            (energy + pressure) * vel_y,
        ]
    )
    return first_coef * flux_x + second_coef * flux_y - sweep_term * strip_cells


def residual(padded, geo_terms):
    first_pitch, second_pitch, sweep_pitch, first_axial, second_axial, sweep_axial = geo_terms
    pitch_flux = directional(
        padded[:, 2:-2, 1:-1], first_pitch[1:-1], second_pitch[1:-1], sweep_pitch[1:-1]
    )
    axial_flux = directional(
        padded[:, 1:-1, 2:-2], first_axial[:, 1:-1], second_axial[:, 1:-1], sweep_axial[:, 1:-1]
    )
    divergence = (pitch_flux[:, :, 2:] - pitch_flux[:, :, :-2]) * 0.5 + (
        axial_flux[:, 2:] - axial_flux[:, :-2]
    ) * 0.5
    centre = padded[:, 2:-2, 2:-2]
    fourth = (
        padded[:, 2:-2, 4:]
        - 4.0 * padded[:, 2:-2, 3:-1]
        + 6.0 * centre
        - 4.0 * padded[:, 2:-2, 1:-3]
        + padded[:, 2:-2, :-4]
        + (
            padded[:, 4:, 2:-2]
            - 4.0 * padded[:, 3:-1, 2:-2]
            + 6.0 * centre
            - 4.0 * padded[:, 1:-3, 2:-2]
            + padded[:, :-4, 2:-2]
        )
    )
    return divergence + DAMPING * fourth + DAMPING * radial_damping(centre, 3)


def flow_ghosts(
    row_zero,
    row_one,
    row_last,
    row_before,
    wrap_low0,
    wrap_low1,
    wrap_high0,
    wrap_high1,
    blade_flag,
    corr_low,
    corr_high,
):
    sign_flip = jnp.array([1.0, 1.0, -1.0, 1.0], jnp.float32).reshape(
        (4,) + (1,) * (row_zero.ndim - 1)
    )
    ghost_m2 = jnp.where(blade_flag, row_one * sign_flip, wrap_low0 + corr_low)
    ghost_m1 = jnp.where(blade_flag, row_zero * sign_flip, wrap_low1 + corr_low)
    ghost_p0 = jnp.where(blade_flag, row_last * sign_flip, wrap_high0 + corr_high)
    ghost_p1 = jnp.where(blade_flag, row_before * sign_flip, wrap_high1 + corr_high)
    return (ghost_m2, ghost_m1, ghost_p0, ghost_p1)


def finish_flow(
    padded, depth, row_flag, corr_low, corr_high, low_end, high_end, first_end, last_end
):
    middle_rows = padded[:, 2:-2]
    width = middle_rows.shape[2]
    ghost_m2, ghost_m1, ghost_p0, ghost_p1 = flow_ghosts(
        middle_rows[:, :, 2],
        middle_rows[:, :, 3],
        middle_rows[:, :, width - 3],
        middle_rows[:, :, width - 4],
        middle_rows[:, :, 0],
        middle_rows[:, :, 1],
        middle_rows[:, :, width - 2],
        middle_rows[:, :, width - 1],
        row_flag[:, None],
        corr_low,
        corr_high,
    )
    low_pair = jnp.where(low_end, jnp.stack([ghost_m2, ghost_m1], 2), middle_rows[:, :, 0:2])
    high_pair = jnp.where(
        high_end, jnp.stack([ghost_p0, ghost_p1], 2), middle_rows[:, :, width - 2 :]
    )
    middle_rows = jnp.concatenate([low_pair, middle_rows[:, :, 2 : width - 2], high_pair], 2)
    whole = jnp.concatenate([padded[:, 0:2], middle_rows, padded[:, -2:]], 1)
    top_copy = jnp.repeat(whole[:, depth : depth + 1], depth, axis=1)
    bottom_copy = jnp.repeat(whole[:, -depth - 1 : -depth], depth, axis=1)
    top_rows = jnp.where(first_end, top_copy, whole[:, :depth])
    bottom_rows = jnp.where(last_end, bottom_copy, whole[:, -depth:])
    return jnp.concatenate([top_rows, whole[:, depth:-depth], bottom_rows], 1)


def _flux(rho, mx, my, en, first, second, sweep):
    inverse = 1.0 / rho
    u = mx * inverse
    v = my * inverse
    pr = (HEAT_RATIO - 1.0) * (en - 0.5 * rho * (u * u + v * v))
    ep = en + pr
    return (
        first * mx + second * my - sweep * rho,
        first * (mx * u + pr) + second * (my * u) - sweep * mx,
        first * (mx * v) + second * (my * v + pr) - sweep * my,
        first * (ep * u) + second * (ep * v) - sweep * en,
    )


def _radial_pairs(c0, lane, forward):
    width = c0.shape[-1]
    last = width - 1
    one_a = pltpu.roll(c0, 1, 1)
    one_b = pltpu.roll(c0, last, 1)
    two_a = pltpu.roll(c0, 2, 1)
    two_b = pltpu.roll(c0, width - 2, 1)
    m1 = jnp.where(lane == 0, c0, jnp.where(forward, one_a, one_b))
    p1 = jnp.where(lane == last, c0, jnp.where(forward, one_b, one_a))
    m2 = jnp.where(lane <= 1, m1, jnp.where(forward, two_a, two_b))
    p2 = jnp.where(lane >= last - 1, p1, jnp.where(forward, two_b, two_a))
    return m1 + p1, m2 + p2


def _volume(grid, a, npch, old):
    def comp(c, row, lo, hi):
        value = grid[c, row, lo:hi]
        if old:
            value = value - grid[c + 2, row, lo:hi]
        return value

    x_zeta = 1.0 + (comp(0, a + 3, 2, npch + 2) - comp(0, a + 1, 2, npch + 2)) * 0.5
    x_xi = (comp(0, a + 2, 3, npch + 3) - comp(0, a + 2, 1, npch + 1)) * 0.5
    y_xi = 1.0 + (comp(1, a + 2, 3, npch + 3) - comp(1, a + 2, 1, npch + 1)) * 0.5
    y_zeta = (comp(1, a + 3, 2, npch + 2) - comp(1, a + 1, 2, npch + 2)) * 0.5
    return x_zeta * y_xi - x_xi * y_zeta


def _section_body(scale, pad_hbm, grid_hbm, q0_hbm, out_hbm, af, pf, pad, grid, q0, out, sems):
    na = out.shape[1]
    npch = out.shape[2]
    width = out.shape[3]

    def row_copy(which, j):
        source, target = ((pad_hbm, pad), (grid_hbm, grid), (q0_hbm, q0), (out, out_hbm))[which]
        return pltpu.make_async_copy(
            source.at[:, pl.ds(j, 1)], target.at[:, pl.ds(j, 1)], sems.at[which, j]
        )

    for j in range(na + 4):
        row_copy(0, j).start()
        if 1 <= j <= na + 2:
            row_copy(1, j).start()
    for j in range(na):
        row_copy(2, j).start()

    def axial_row(j, carry):
        row_copy(0, j + 1).wait()
        row_copy(1, j + 1).wait()
        x_xi = (grid[0, j + 1, 3 : npch + 3] - grid[0, j + 1, 1 : npch + 1]) * 0.5
        y_xi = 1.0 + (grid[1, j + 1, 3 : npch + 3] - grid[1, j + 1, 1 : npch + 1]) * 0.5
        speed_x = grid[2, j + 1, 2 : npch + 2] / TIME_STEP
        speed_y = grid[3, j + 1, 2 : npch + 2] / TIME_STEP
        second = -x_xi
        sweep = y_xi * speed_x + second * speed_y
        q = [pad[k, j + 1, 2 : npch + 2] for k in range(4)]
        f = _flux(*q, y_xi, second, sweep)
        for k in range(4):
            af[k, j] = f[k]
        return carry

    lax.fori_loop(0, na + 2, axial_row, 0)
    lane = lax.broadcasted_iota(jnp.int32, (npch, width), 1)
    probe = pltpu.roll(lane, 1, 1)
    forward = probe == jnp.where(lane == 0, width - 1, lane - 1)

    row_copy(0, 0).wait()
    row_copy(0, na + 3).wait()

    def row(a, carry):
        row_copy(2, a).wait()
        x_zeta = 1.0 + (grid[0, a + 3, 1 : npch + 3] - grid[0, a + 1, 1 : npch + 3]) * 0.5
        y_zeta = (grid[1, a + 3, 1 : npch + 3] - grid[1, a + 1, 1 : npch + 3]) * 0.5
        speed_x = grid[2, a + 2, 1 : npch + 3] / TIME_STEP
        speed_y = grid[3, a + 2, 1 : npch + 3] / TIME_STEP
        first = -y_zeta
        sweep = first * speed_x + x_zeta * speed_y
        q = [pad[k, a + 2, 1 : npch + 3] for k in range(4)]
        f = _flux(*q, first, x_zeta, sweep)
        for k in range(4):
            pf[k] = f[k]
        volume_old = _volume(grid, a, npch, True)
        inverse_new = 1.0 / _volume(grid, a, npch, False)
        for k in range(4):
            div = (pf[k, 2 : npch + 2] - pf[k, 0:npch]) * 0.5 + (af[k, a + 2] - af[k, a]) * 0.5
            c0 = pad[k, a + 2, 2 : npch + 2]
            near_r, far_r = _radial_pairs(c0, lane, forward)
            near = (
                pad[k, a + 2, 3 : npch + 3]
                + pad[k, a + 2, 1 : npch + 1]
                + pad[k, a + 3, 2 : npch + 2]
                + pad[k, a + 1, 2 : npch + 2]
                + near_r
            )
            far = (
                pad[k, a + 2, 4 : npch + 4]
                + pad[k, a + 2, 0:npch]
                + pad[k, a + 4, 2 : npch + 2]
                + pad[k, a, 2 : npch + 2]
                + far_r
            )
            res = div + DAMPING * (far - 4.0 * near + 18.0 * c0)
            out[k, a] = (volume_old * q0[k, a] - scale * res) * inverse_new
        row_copy(3, a).start()
        return carry

    lax.fori_loop(0, na, row, 0)
    for j in range(na):
        row_copy(3, j).wait()


def section_kernel(padded, grid_pad, start, scale, interpret=False):
    _, na, npch, width = start.shape
    body = lambda *refs: _section_body(scale, *refs)
    cells = na * npch * width
    return pl.pallas_call(
        body,
        out_shape=jax.ShapeDtypeStruct(start.shape, start.dtype),
        in_specs=[pl.BlockSpec(memory_space=pl.ANY)] * 3,
        out_specs=pl.BlockSpec(memory_space=pl.ANY),
        scratch_shapes=[
            pltpu.VMEM((4, na + 2, npch, width), jnp.float32),
            pltpu.VMEM((4, npch + 2, width), jnp.float32),
            pltpu.VMEM(padded.shape, jnp.float32),
            pltpu.VMEM(grid_pad.shape, jnp.float32),
            pltpu.VMEM(start.shape, jnp.float32),
            pltpu.VMEM(start.shape, jnp.float32),
            pltpu.SemaphoreType.DMA((4, na + 4)),
        ],
        compiler_params=pltpu.CompilerParams(vmem_limit_bytes=60 * 1024 * 1024),
        cost_estimate=pl.CostEstimate(
            flops=500 * cells, transcendentals=0, bytes_accessed=4 * 14 * cells
        ),
        interpret=interpret,
    )(padded, grid_pad, start)


def per_device(flow_state, node_offset, blade_mode, phase_angles, lag_series):
    n_pitch = lax.axis_size("pitch")
    n_span = lax.axis_size("span")
    pitch_rows = flow_state.shape[2]
    axial_cols = flow_state.shape[1]
    total_pitch = pitch_rows * n_pitch
    total_axial = axial_cols * n_span
    pitch_at = lax.axis_index("pitch")
    span_at = lax.axis_index("span")
    lead_edge = total_axial // 4
    axial_index = span_at * axial_cols + jnp.arange(axial_cols, dtype=jnp.int32)
    blade_flag = (axial_index >= lead_edge) & (axial_index < total_axial - lead_edge)
    blade_mask = blade_flag.astype(jnp.float32)[:, None]
    phase_now = phase_angles[0]
    phase_lag = phase_angles[1]
    low_guess = wall_amplitude(blade_mode, phase_now, blade_mask) * unit_normal(
        node_offset[:, :, 0], node_offset[:, :, 1]
    )
    high_guess = wall_amplitude(blade_mode, phase_now + phase_lag, blade_mask) * unit_normal(
        node_offset[:, :, pitch_rows - 2], node_offset[:, :, pitch_rows - 1]
    )
    low_wall = low_guess
    high_wall = high_guess
    sent = jnp.where(pitch_at == 0, low_guess, high_guess)
    for shift in range(1, n_pitch):
        got = lax.ppermute(sent, "pitch", [(0, shift), (n_pitch - 1, shift - 1)])
        low_wall = jnp.where(pitch_at == shift, got, low_wall)
        high_wall = jnp.where(pitch_at == shift - 1, got, high_wall)
    pitch_index = pitch_at * pitch_rows + jnp.arange(pitch_rows, dtype=jnp.int32)
    blend_row = (pitch_index.astype(jnp.float32) / (total_pitch - 1))[:, None]
    shift_field = (1.0 - blend_row) * low_wall[:, :, None, :] + blend_row * high_wall[:, :, None, :]
    moved_offset = node_offset + shift_field
    grid_field = jnp.concatenate([moved_offset, shift_field], 0)
    rim_width = 2
    grid_pad = padded_2(grid_field, (("pitch", 2), ("span", 1)), rim_width)
    first_pad = padded_cross(flow_state, rim_width)
    low_end = pitch_at == 0
    high_end = pitch_at == n_pitch - 1
    first_end = span_at == 0
    last_end = span_at == n_span - 1
    grid_pad = fill_ends(grid_pad, 1, rim_width, first_end, last_end)
    grid_pad = fill_ends(grid_pad, 2, 2, low_end, high_end)
    corr_low = lag_shift(lag_series[1], phase_now, -phase_lag)
    corr_high = lag_shift(lag_series[0], phase_now, phase_lag)
    padded = finish_flow(
        first_pad, 2, blade_flag, corr_low, corr_high, low_end, high_end, first_end, last_end
    )
    section_one = section_kernel(padded, grid_pad, flow_state, SECTION_WEIGHTS[0] * TIME_STEP)
    second_pad = padded_cross(section_one, 2)
    padded = finish_flow(
        second_pad, 2, blade_flag, corr_low, corr_high, low_end, high_end, first_end, last_end
    )
    current = section_kernel(padded, grid_pad, flow_state, SECTION_WEIGHTS[1] * TIME_STEP)
    return (current, moved_offset)


def solution(mesh):
    placed = (
        P(None, "span", "pitch", None),
        P(None, "span", "pitch", None),
        P(None, "span", None),
        P(),
        P(None, None, None, None, "span", None),
    )
    return jax.shard_map(
        per_device,
        mesh=mesh,
        in_specs=placed,
        out_specs=(P(None, "span", "pitch", None), P(None, "span", "pitch", None)),
        check_vma=False,
    )
```

```python
import jax
import jax.numpy as jnp
from jax import lax
from jax.sharding import PartitionSpec as P
from jax.experimental import pallas as pl
from jax.experimental.pallas import tpu as pltpu

HEAT_RATIO = 1.4
TIME_STEP = 0.25
DAMPING = 0.02
SECTION_WEIGHTS = (0.5, 1.0)


def broadcast(value, axis, root):
    mine = lax.axis_index(axis) == root
    return lax.psum(jnp.where(mine, value, jnp.zeros_like(value)), axis)


def padded_2(block, sides, width, wrap=True):
    for axis, dim in sides:
        count = lax.axis_size(axis)
        forward = [(i, i + 1) for i in range(count - 1)]
        if wrap:
            forward.append((count - 1, 0))
        backward = [(target, source) for source, target in forward]
        low = lax.ppermute(
            lax.slice_in_dim(block, block.shape[dim] - width, None, axis=dim), axis, forward
        )
        high = lax.ppermute(lax.slice_in_dim(block, 0, width, axis=dim), axis, backward)
        block = jnp.concatenate([low, block, high], axis=dim)
    return block


def padded_cross(block, width):
    rims = []
    for axis, dim, wrap in (("pitch", 2, True), ("span", 1, False)):
        count = lax.axis_size(axis)
        forward = [(i, i + 1) for i in range(count - 1)]
        if wrap:
            forward.append((count - 1, 0))
        backward = [(target, source) for source, target in forward]
        low = lax.ppermute(
            lax.slice_in_dim(block, block.shape[dim] - width, None, axis=dim), axis, forward
        )
        high = lax.ppermute(lax.slice_in_dim(block, 0, width, axis=dim), axis, backward)
        rims.append((low, high))
    (pitch_low, pitch_high), (span_low, span_high) = rims
    middle = jnp.concatenate([pitch_low, block, pitch_high], axis=2)
    corner = jnp.zeros(span_low.shape[:2] + (width,) + span_low.shape[3:], block.dtype)
    top = jnp.concatenate([corner, span_low, corner], axis=2)
    bottom = jnp.concatenate([corner, span_high, corner], axis=2)
    return jnp.concatenate([top, middle, bottom], axis=1)


def fill_ends(padded, axis_pos, depth, at_first, at_last):
    length = padded.shape[axis_pos]
    inner_first = lax.slice_in_dim(padded, depth, depth + 1, axis=axis_pos)
    inner_second = lax.slice_in_dim(padded, depth + 1, depth + 2, axis=axis_pos)
    inner_last = lax.slice_in_dim(padded, length - depth - 1, length - depth, axis=axis_pos)
    inner_before = lax.slice_in_dim(padded, length - depth - 2, length - depth - 1, axis=axis_pos)
    step_low = inner_first - inner_second
    step_high = inner_last - inner_before
    low_side = jnp.concatenate(
        [inner_first + float(count) * step_low for count in range(depth, 0, -1)], axis=axis_pos
    )
    high_side = jnp.concatenate(
        [inner_last + float(count) * step_high for count in range(1, depth + 1)], axis=axis_pos
    )
    low_side = jnp.where(at_first, low_side, lax.slice_in_dim(padded, 0, depth, axis=axis_pos))
    high_side = jnp.where(
        at_last, high_side, lax.slice_in_dim(padded, length - depth, length, axis=axis_pos)
    )
    return jnp.concatenate(
        [low_side, lax.slice_in_dim(padded, depth, length - depth, axis=axis_pos), high_side],
        axis=axis_pos,
    )


def radial_damping(values, axis_pos):
    count = values.shape[axis_pos]
    first_row = lax.slice_in_dim(values, 0, 1, axis=axis_pos)
    last_row = lax.slice_in_dim(values, count - 1, count, axis=axis_pos)
    extended = jnp.concatenate([first_row, first_row, values, last_row, last_row], axis=axis_pos)
    return (
        lax.slice_in_dim(extended, 4, 4 + count, axis=axis_pos)
        - 4.0 * lax.slice_in_dim(extended, 3, 3 + count, axis=axis_pos)
        + 6.0 * values
        - 4.0 * lax.slice_in_dim(extended, 1, 1 + count, axis=axis_pos)
        + lax.slice_in_dim(extended, 0, count, axis=axis_pos)
    )


def unit_normal(earlier, later):
    along_x = later[0] - earlier[0]
    along_y = 1.0 + later[1] - earlier[1]
    length = jnp.sqrt(along_x * along_x + along_y * along_y)
    return jnp.stack([along_x / length, along_y / length])


def wall_amplitude(shape_mode, angle, blade_mask):
    return (shape_mode[0] * jnp.cos(angle) - shape_mode[1] * jnp.sin(angle)) * blade_mask


def lag_shift(series, phase_now, phase_move):
    series_sum = jnp.zeros(series.shape[2:], jnp.float32)
    for number in range(series.shape[0]):
        harmonic = float(number + 1)
        change_cos = jnp.cos(harmonic * (phase_now + phase_move)) - jnp.cos(harmonic * phase_now)
        change_sin = jnp.sin(harmonic * (phase_now + phase_move)) - jnp.sin(harmonic * phase_now)
        series_sum = series_sum + series[number, 0] * change_cos - series[number, 1] * change_sin
    return series_sum


def metric_terms(offset_x, offset_y):
    x_zeta = 1.0 + (offset_x[2:, 1:-1] - offset_x[:-2, 1:-1]) * 0.5
    x_xi = (offset_x[1:-1, 2:] - offset_x[1:-1, :-2]) * 0.5
    y_xi = 1.0 + (offset_y[1:-1, 2:] - offset_y[1:-1, :-2]) * 0.5
    y_zeta = (offset_y[2:, 1:-1] - offset_y[:-2, 1:-1]) * 0.5
    return (x_zeta, x_xi, y_xi, y_zeta)


def geometry(grid_pad):
    x_zeta, x_xi, y_xi, y_zeta = metric_terms(grid_pad[0], grid_pad[1])
    old_zeta, old_xi, oldy_xi, oldy_zeta = metric_terms(
        grid_pad[0] - grid_pad[2], grid_pad[1] - grid_pad[3]
    )
    volume_new = (x_zeta * y_xi - x_xi * y_zeta)[1:-1, 1:-1]
    volume_old = (old_zeta * oldy_xi - old_xi * oldy_zeta)[1:-1, 1:-1]
    speed_x = grid_pad[2][1:-1, 1:-1] / TIME_STEP
    speed_y = grid_pad[3][1:-1, 1:-1] / TIME_STEP
    first_pitch = -y_zeta
    sweep_pitch = first_pitch * speed_x + x_zeta * speed_y
    second_axial = -x_xi
    sweep_axial = y_xi * speed_x + second_axial * speed_y
    return (
        (first_pitch, x_zeta, sweep_pitch, y_xi, second_axial, sweep_axial),
        volume_old,
        volume_new,
    )


def directional(strip_cells, first_coef, second_coef, sweep_term):
    density = strip_cells[0]
    vel_x = strip_cells[1] / density
    vel_y = strip_cells[2] / density
    energy = strip_cells[3]
    pressure = (HEAT_RATIO - 1.0) * (energy - 0.5 * density * (vel_x * vel_x + vel_y * vel_y))
    flux_x = jnp.stack(
        [
            strip_cells[1],
            strip_cells[1] * vel_x + pressure,
            strip_cells[1] * vel_y,
            (energy + pressure) * vel_x,
        ]
    )
    flux_y = jnp.stack(
        [
            strip_cells[2],
            strip_cells[2] * vel_x,
            strip_cells[2] * vel_y + pressure,
            (energy + pressure) * vel_y,
        ]
    )
    return first_coef * flux_x + second_coef * flux_y - sweep_term * strip_cells


def residual(padded, geo_terms):
    first_pitch, second_pitch, sweep_pitch, first_axial, second_axial, sweep_axial = geo_terms
    pitch_flux = directional(
        padded[:, 2:-2, 1:-1], first_pitch[1:-1], second_pitch[1:-1], sweep_pitch[1:-1]
    )
    axial_flux = directional(
        padded[:, 1:-1, 2:-2], first_axial[:, 1:-1], second_axial[:, 1:-1], sweep_axial[:, 1:-1]
    )
    divergence = (pitch_flux[:, :, 2:] - pitch_flux[:, :, :-2]) * 0.5 + (
        axial_flux[:, 2:] - axial_flux[:, :-2]
    ) * 0.5
    centre = padded[:, 2:-2, 2:-2]
    fourth = (
        padded[:, 2:-2, 4:]
        - 4.0 * padded[:, 2:-2, 3:-1]
        + 6.0 * centre
        - 4.0 * padded[:, 2:-2, 1:-3]
        + padded[:, 2:-2, :-4]
        + (
            padded[:, 4:, 2:-2]
            - 4.0 * padded[:, 3:-1, 2:-2]
            + 6.0 * centre
            - 4.0 * padded[:, 1:-3, 2:-2]
            + padded[:, :-4, 2:-2]
        )
    )
    return divergence + DAMPING * fourth + DAMPING * radial_damping(centre, 3)


def flow_ghosts(
    row_zero,
    row_one,
    row_last,
    row_before,
    wrap_low0,
    wrap_low1,
    wrap_high0,
    wrap_high1,
    blade_flag,
    corr_low,
    corr_high,
):
    sign_flip = jnp.array([1.0, 1.0, -1.0, 1.0], jnp.float32).reshape(
        (4,) + (1,) * (row_zero.ndim - 1)
    )
    ghost_m2 = jnp.where(blade_flag, row_one * sign_flip, wrap_low0 + corr_low)
    ghost_m1 = jnp.where(blade_flag, row_zero * sign_flip, wrap_low1 + corr_low)
    ghost_p0 = jnp.where(blade_flag, row_last * sign_flip, wrap_high0 + corr_high)
    ghost_p1 = jnp.where(blade_flag, row_before * sign_flip, wrap_high1 + corr_high)
    return (ghost_m2, ghost_m1, ghost_p0, ghost_p1)


def finish_flow(
    padded, depth, row_flag, corr_low, corr_high, low_end, high_end, first_end, last_end
):
    middle_rows = padded[:, 2:-2]
    width = middle_rows.shape[2]
    ghost_m2, ghost_m1, ghost_p0, ghost_p1 = flow_ghosts(
        middle_rows[:, :, 2],
        middle_rows[:, :, 3],
        middle_rows[:, :, width - 3],
        middle_rows[:, :, width - 4],
        middle_rows[:, :, 0],
        middle_rows[:, :, 1],
        middle_rows[:, :, width - 2],
        middle_rows[:, :, width - 1],
        row_flag[:, None],
        corr_low,
        corr_high,
    )
    low_pair = jnp.where(low_end, jnp.stack([ghost_m2, ghost_m1], 2), middle_rows[:, :, 0:2])
    high_pair = jnp.where(
        high_end, jnp.stack([ghost_p0, ghost_p1], 2), middle_rows[:, :, width - 2 :]
    )
    middle_rows = jnp.concatenate([low_pair, middle_rows[:, :, 2 : width - 2], high_pair], 2)
    whole = jnp.concatenate([padded[:, 0:2], middle_rows, padded[:, -2:]], 1)
    top_copy = jnp.repeat(whole[:, depth : depth + 1], depth, axis=1)
    bottom_copy = jnp.repeat(whole[:, -depth - 1 : -depth], depth, axis=1)
    top_rows = jnp.where(first_end, top_copy, whole[:, :depth])
    bottom_rows = jnp.where(last_end, bottom_copy, whole[:, -depth:])
    return jnp.concatenate([top_rows, whole[:, depth:-depth], bottom_rows], 1)


def _flux(rho, mx, my, en, first, second, sweep):
    inverse = 1.0 / rho
    u = mx * inverse
    v = my * inverse
    pr = (HEAT_RATIO - 1.0) * (en - 0.5 * rho * (u * u + v * v))
    ep = en + pr
    return (
        first * mx + second * my - sweep * rho,
        first * (mx * u + pr) + second * (my * u) - sweep * mx,
        first * (mx * v) + second * (my * v + pr) - sweep * my,
        first * (ep * u) + second * (ep * v) - sweep * en,
    )


def _radial_pairs(c0, lane, forward):
    width = c0.shape[-1]
    last = width - 1
    one_a = pltpu.roll(c0, 1, 1)
    one_b = pltpu.roll(c0, last, 1)
    two_a = pltpu.roll(c0, 2, 1)
    two_b = pltpu.roll(c0, width - 2, 1)
    m1 = jnp.where(lane == 0, c0, jnp.where(forward, one_a, one_b))
    p1 = jnp.where(lane == last, c0, jnp.where(forward, one_b, one_a))
    m2 = jnp.where(lane <= 1, m1, jnp.where(forward, two_a, two_b))
    p2 = jnp.where(lane >= last - 1, p1, jnp.where(forward, two_b, two_a))
    return m1 + p1, m2 + p2


def _volume(grid, a, npch, old):
    def comp(c, row, lo, hi):
        value = grid[c, row, lo:hi]
        if old:
            value = value - grid[c + 2, row, lo:hi]
        return value

    x_zeta = 1.0 + (comp(0, a + 3, 2, npch + 2) - comp(0, a + 1, 2, npch + 2)) * 0.5
    x_xi = (comp(0, a + 2, 3, npch + 3) - comp(0, a + 2, 1, npch + 1)) * 0.5
    y_xi = 1.0 + (comp(1, a + 2, 3, npch + 3) - comp(1, a + 2, 1, npch + 1)) * 0.5
    y_zeta = (comp(1, a + 3, 2, npch + 2) - comp(1, a + 1, 2, npch + 2)) * 0.5
    return x_zeta * y_xi - x_xi * y_zeta


def _section_body(scale, pad_hbm, grid_hbm, q0_hbm, out_hbm, af, pf, pad, grid, q0, out, sems):
    na = out.shape[1]
    npch = out.shape[2]
    width = out.shape[3]

    def row_copy(which, j):
        source, target = ((pad_hbm, pad), (grid_hbm, grid), (q0_hbm, q0), (out, out_hbm))[which]
        return pltpu.make_async_copy(
            source.at[:, pl.ds(j, 1)], target.at[:, pl.ds(j, 1)], sems.at[which, j]
        )

    for j in range(na + 4):
        row_copy(0, j).start()
        if 1 <= j <= na + 2:
            row_copy(1, j).start()
    for j in range(na):
        row_copy(2, j).start()

    def axial_row(j, carry):
        row_copy(0, j + 1).wait()
        row_copy(1, j + 1).wait()
        x_xi = (grid[0, j + 1, 3 : npch + 3] - grid[0, j + 1, 1 : npch + 1]) * 0.5
        y_xi = 1.0 + (grid[1, j + 1, 3 : npch + 3] - grid[1, j + 1, 1 : npch + 1]) * 0.5
        speed_x = grid[2, j + 1, 2 : npch + 2] / TIME_STEP
        speed_y = grid[3, j + 1, 2 : npch + 2] / TIME_STEP
        second = -x_xi
        sweep = y_xi * speed_x + second * speed_y
        q = [pad[k, j + 1, 2 : npch + 2] for k in range(4)]
        f = _flux(*q, y_xi, second, sweep)
        for k in range(4):
            af[k, j] = f[k]
        return carry

    lax.fori_loop(0, na + 2, axial_row, 0)
    lane = lax.broadcasted_iota(jnp.int32, (npch, width), 1)
    probe = pltpu.roll(lane, 1, 1)
    forward = probe == jnp.where(lane == 0, width - 1, lane - 1)

    row_copy(0, 0).wait()
    row_copy(0, na + 3).wait()

    def row(a, carry):
        row_copy(2, a).wait()
        x_zeta = 1.0 + (grid[0, a + 3, 1 : npch + 3] - grid[0, a + 1, 1 : npch + 3]) * 0.5
        y_zeta = (grid[1, a + 3, 1 : npch + 3] - grid[1, a + 1, 1 : npch + 3]) * 0.5
        speed_x = grid[2, a + 2, 1 : npch + 3] / TIME_STEP
        speed_y = grid[3, a + 2, 1 : npch + 3] / TIME_STEP
        first = -y_zeta
        sweep = first * speed_x + x_zeta * speed_y
        q = [pad[k, a + 2, 1 : npch + 3] for k in range(4)]
        f = _flux(*q, first, x_zeta, sweep)
        for k in range(4):
            pf[k] = f[k]
        volume_old = _volume(grid, a, npch, True)
        inverse_new = 1.0 / _volume(grid, a, npch, False)
        for k in range(4):
            div = (pf[k, 2 : npch + 2] - pf[k, 0:npch]) * 0.5 + (af[k, a + 2] - af[k, a]) * 0.5
            c0 = pad[k, a + 2, 2 : npch + 2]
            near_r, far_r = _radial_pairs(c0, lane, forward)
            near = (
                pad[k, a + 2, 3 : npch + 3]
                + pad[k, a + 2, 1 : npch + 1]
                + pad[k, a + 3, 2 : npch + 2]
                + pad[k, a + 1, 2 : npch + 2]
                + near_r
            )
            far = (
                pad[k, a + 2, 4 : npch + 4]
                + pad[k, a + 2, 0:npch]
                + pad[k, a + 4, 2 : npch + 2]
                + pad[k, a, 2 : npch + 2]
                + far_r
            )
            res = div + DAMPING * (far - 4.0 * near + 18.0 * c0)
            out[k, a] = (volume_old * q0[k, a] - scale * res) * inverse_new
        row_copy(3, a).start()
        return carry

    lax.fori_loop(0, na, row, 0)
    for j in range(na):
        row_copy(3, j).wait()


def section_kernel(padded, grid_pad, start, scale, interpret=False):
    _, na, npch, width = start.shape
    body = lambda *refs: _section_body(scale, *refs)
    cells = na * npch * width
    return pl.pallas_call(
        body,
        out_shape=jax.ShapeDtypeStruct(start.shape, start.dtype),
        in_specs=[pl.BlockSpec(memory_space=pl.ANY)] * 3,
        out_specs=pl.BlockSpec(memory_space=pl.ANY),
        scratch_shapes=[
            pltpu.VMEM((4, na + 2, npch, width), jnp.float32),
            pltpu.VMEM((4, npch + 2, width), jnp.float32),
            pltpu.VMEM(padded.shape, jnp.float32),
            pltpu.VMEM(grid_pad.shape, jnp.float32),
            pltpu.VMEM(start.shape, jnp.float32),
            pltpu.VMEM(start.shape, jnp.float32),
            pltpu.SemaphoreType.DMA((4, na + 4)),
        ],
        compiler_params=pltpu.CompilerParams(vmem_limit_bytes=60 * 1024 * 1024),
        cost_estimate=pl.CostEstimate(
            flops=500 * cells, transcendentals=0, bytes_accessed=4 * 14 * cells
        ),
        interpret=interpret,
    )(padded, grid_pad, start)


def per_device(flow_state, node_offset, blade_mode, phase_angles, lag_series):
    n_pitch = lax.axis_size("pitch")
    n_span = lax.axis_size("span")
    pitch_rows = flow_state.shape[2]
    axial_cols = flow_state.shape[1]
    total_pitch = pitch_rows * n_pitch
    total_axial = axial_cols * n_span
    pitch_at = lax.axis_index("pitch")
    span_at = lax.axis_index("span")
    lead_edge = total_axial // 4
    axial_index = span_at * axial_cols + jnp.arange(axial_cols, dtype=jnp.int32)
    blade_flag = (axial_index >= lead_edge) & (axial_index < total_axial - lead_edge)
    blade_mask = blade_flag.astype(jnp.float32)[:, None]
    phase_now = phase_angles[0]
    phase_lag = phase_angles[1]
    low_guess = wall_amplitude(blade_mode, phase_now, blade_mask) * unit_normal(
        node_offset[:, :, 0], node_offset[:, :, 1]
    )
    high_guess = wall_amplitude(blade_mode, phase_now + phase_lag, blade_mask) * unit_normal(
        node_offset[:, :, pitch_rows - 2], node_offset[:, :, pitch_rows - 1]
    )
    low_wall = low_guess
    high_wall = high_guess
    sent = jnp.where(pitch_at == 0, low_guess, high_guess)
    for shift in range(1, n_pitch):
        got = lax.ppermute(sent, "pitch", [(0, shift), (n_pitch - 1, shift - 1)])
        low_wall = jnp.where(pitch_at == shift, got, low_wall)
        high_wall = jnp.where(pitch_at == shift - 1, got, high_wall)
    pitch_index = pitch_at * pitch_rows + jnp.arange(pitch_rows, dtype=jnp.int32)
    blend_row = (pitch_index.astype(jnp.float32) / (total_pitch - 1))[:, None]
    shift_field = (1.0 - blend_row) * low_wall[:, :, None, :] + blend_row * high_wall[:, :, None, :]
    moved_offset = node_offset + shift_field
    grid_field = jnp.concatenate([moved_offset, shift_field], 0)
    rim_width = 2
    grid_pad = padded_2(grid_field, (("pitch", 2), ("span", 1)), rim_width, wrap=False)
    first_pad = padded_cross(flow_state, rim_width)
    low_end = pitch_at == 0
    high_end = pitch_at == n_pitch - 1
    first_end = span_at == 0
    last_end = span_at == n_span - 1
    grid_pad = fill_ends(grid_pad, 1, rim_width, first_end, last_end)
    grid_pad = fill_ends(grid_pad, 2, 2, low_end, high_end)
    corr_low = lag_shift(lag_series[1], phase_now, -phase_lag)
    corr_high = lag_shift(lag_series[0], phase_now, phase_lag)
    padded = finish_flow(
        first_pad, 2, blade_flag, corr_low, corr_high, low_end, high_end, first_end, last_end
    )
    section_one = section_kernel(padded, grid_pad, flow_state, SECTION_WEIGHTS[0] * TIME_STEP)
    second_pad = padded_cross(section_one, 2)
    padded = finish_flow(
        second_pad, 2, blade_flag, corr_low, corr_high, low_end, high_end, first_end, last_end
    )
    current = section_kernel(padded, grid_pad, flow_state, SECTION_WEIGHTS[1] * TIME_STEP)
    return (current, moved_offset)


def solution(mesh):
    placed = (
        P(None, "span", "pitch", None),
        P(None, "span", "pitch", None),
        P(None, "span", None),
        P(),
        P(None, None, None, None, "span", None),
    )
    return jax.shard_map(
        per_device,
        mesh=mesh,
        in_specs=placed,
        out_specs=(P(None, "span", "pitch", None), P(None, "span", "pitch", None)),
        check_vma=False,
    )
```

```python
import jax
import jax.numpy as jnp
from jax import lax
from jax.sharding import PartitionSpec as P
from jax.experimental import pallas as pl
from jax.experimental.pallas import tpu as pltpu

HEAT_RATIO = 1.4
TIME_STEP = 0.25
DAMPING = 0.02
SECTION_WEIGHTS = (0.5, 1.0)


def broadcast(value, axis, root):
    mine = lax.axis_index(axis) == root
    return lax.psum(jnp.where(mine, value, jnp.zeros_like(value)), axis)


def padded_2(block, sides, width):
    for axis, dim in sides:
        count = lax.axis_size(axis)
        forward = [(i, i + 1) for i in range(count - 1)]
        forward.append((count - 1, 0))
        backward = [(target, source) for source, target in forward]
        low = lax.ppermute(
            lax.slice_in_dim(block, block.shape[dim] - width, None, axis=dim), axis, forward
        )
        high = lax.ppermute(lax.slice_in_dim(block, 0, width, axis=dim), axis, backward)
        block = jnp.concatenate([low, block, high], axis=dim)
    return block


def padded_cross(block, width):
    rims = []
    for axis, dim in (("pitch", 2), ("span", 1)):
        count = lax.axis_size(axis)
        forward = [(i, (i + 1) % count) for i in range(count)]
        backward = [(target, source) for source, target in forward]
        low = lax.ppermute(
            lax.slice_in_dim(block, block.shape[dim] - width, None, axis=dim), axis, forward
        )
        high = lax.ppermute(lax.slice_in_dim(block, 0, width, axis=dim), axis, backward)
        rims.append((low, high))
    (pitch_low, pitch_high), (span_low, span_high) = rims
    middle = jnp.concatenate([pitch_low, block, pitch_high], axis=2)
    corner = jnp.zeros(span_low.shape[:2] + (width,) + span_low.shape[3:], block.dtype)
    top = jnp.concatenate([corner, span_low, corner], axis=2)
    bottom = jnp.concatenate([corner, span_high, corner], axis=2)
    return jnp.concatenate([top, middle, bottom], axis=1)


def fill_ends(padded, axis_pos, depth, at_first, at_last):
    length = padded.shape[axis_pos]
    inner_first = lax.slice_in_dim(padded, depth, depth + 1, axis=axis_pos)
    inner_second = lax.slice_in_dim(padded, depth + 1, depth + 2, axis=axis_pos)
    inner_last = lax.slice_in_dim(padded, length - depth - 1, length - depth, axis=axis_pos)
    inner_before = lax.slice_in_dim(padded, length - depth - 2, length - depth - 1, axis=axis_pos)
    step_low = inner_first - inner_second
    step_high = inner_last - inner_before
    low_side = jnp.concatenate(
        [inner_first + float(count) * step_low for count in range(depth, 0, -1)], axis=axis_pos
    )
    high_side = jnp.concatenate(
        [inner_last + float(count) * step_high for count in range(1, depth + 1)], axis=axis_pos
    )
    low_side = jnp.where(at_first, low_side, lax.slice_in_dim(padded, 0, depth, axis=axis_pos))
    high_side = jnp.where(
        at_last, high_side, lax.slice_in_dim(padded, length - depth, length, axis=axis_pos)
    )
    return jnp.concatenate(
        [low_side, lax.slice_in_dim(padded, depth, length - depth, axis=axis_pos), high_side],
        axis=axis_pos,
    )


def radial_damping(values, axis_pos):
    count = values.shape[axis_pos]
    first_row = lax.slice_in_dim(values, 0, 1, axis=axis_pos)
    last_row = lax.slice_in_dim(values, count - 1, count, axis=axis_pos)
    extended = jnp.concatenate([first_row, first_row, values, last_row, last_row], axis=axis_pos)
    return (
        lax.slice_in_dim(extended, 4, 4 + count, axis=axis_pos)
        - 4.0 * lax.slice_in_dim(extended, 3, 3 + count, axis=axis_pos)
        + 6.0 * values
        - 4.0 * lax.slice_in_dim(extended, 1, 1 + count, axis=axis_pos)
        + lax.slice_in_dim(extended, 0, count, axis=axis_pos)
    )


def unit_normal(earlier, later):
    along_x = later[0] - earlier[0]
    along_y = 1.0 + later[1] - earlier[1]
    length = jnp.sqrt(along_x * along_x + along_y * along_y)
    return jnp.stack([along_x / length, along_y / length])


def wall_amplitude(shape_mode, angle, blade_mask):
    return (shape_mode[0] * jnp.cos(angle) - shape_mode[1] * jnp.sin(angle)) * blade_mask


def lag_shift(series, phase_now, phase_move):
    series_sum = jnp.zeros(series.shape[2:], jnp.float32)
    for number in range(series.shape[0]):
        harmonic = float(number + 1)
        change_cos = jnp.cos(harmonic * (phase_now + phase_move)) - jnp.cos(harmonic * phase_now)
        change_sin = jnp.sin(harmonic * (phase_now + phase_move)) - jnp.sin(harmonic * phase_now)
        series_sum = series_sum + series[number, 0] * change_cos - series[number, 1] * change_sin
    return series_sum


def metric_terms(offset_x, offset_y):
    x_zeta = 1.0 + (offset_x[2:, 1:-1] - offset_x[:-2, 1:-1]) * 0.5
    x_xi = (offset_x[1:-1, 2:] - offset_x[1:-1, :-2]) * 0.5
    y_xi = 1.0 + (offset_y[1:-1, 2:] - offset_y[1:-1, :-2]) * 0.5
    y_zeta = (offset_y[2:, 1:-1] - offset_y[:-2, 1:-1]) * 0.5
    return (x_zeta, x_xi, y_xi, y_zeta)


def geometry(grid_pad):
    x_zeta, x_xi, y_xi, y_zeta = metric_terms(grid_pad[0], grid_pad[1])
    old_zeta, old_xi, oldy_xi, oldy_zeta = metric_terms(
        grid_pad[0] - grid_pad[2], grid_pad[1] - grid_pad[3]
    )
    volume_new = (x_zeta * y_xi - x_xi * y_zeta)[1:-1, 1:-1]
    volume_old = (old_zeta * oldy_xi - old_xi * oldy_zeta)[1:-1, 1:-1]
    speed_x = grid_pad[2][1:-1, 1:-1] / TIME_STEP
    speed_y = grid_pad[3][1:-1, 1:-1] / TIME_STEP
    first_pitch = -y_zeta
    sweep_pitch = first_pitch * speed_x + x_zeta * speed_y
    second_axial = -x_xi
    sweep_axial = y_xi * speed_x + second_axial * speed_y
    return (
        (first_pitch, x_zeta, sweep_pitch, y_xi, second_axial, sweep_axial),
        volume_old,
        volume_new,
    )


def directional(strip_cells, first_coef, second_coef, sweep_term):
    density = strip_cells[0]
    vel_x = strip_cells[1] / density
    vel_y = strip_cells[2] / density
    energy = strip_cells[3]
    pressure = (HEAT_RATIO - 1.0) * (energy - 0.5 * density * (vel_x * vel_x + vel_y * vel_y))
    flux_x = jnp.stack(
        [
            strip_cells[1],
            strip_cells[1] * vel_x + pressure,
            strip_cells[1] * vel_y,
            (energy + pressure) * vel_x,
        ]
    )
    flux_y = jnp.stack(
        [
            strip_cells[2],
            strip_cells[2] * vel_x,
            strip_cells[2] * vel_y + pressure,
            (energy + pressure) * vel_y,
        ]
    )
    return first_coef * flux_x + second_coef * flux_y - sweep_term * strip_cells


def residual(padded, geo_terms):
    first_pitch, second_pitch, sweep_pitch, first_axial, second_axial, sweep_axial = geo_terms
    pitch_flux = directional(
        padded[:, 2:-2, 1:-1], first_pitch[1:-1], second_pitch[1:-1], sweep_pitch[1:-1]
    )
    axial_flux = directional(
        padded[:, 1:-1, 2:-2], first_axial[:, 1:-1], second_axial[:, 1:-1], sweep_axial[:, 1:-1]
    )
    divergence = (pitch_flux[:, :, 2:] - pitch_flux[:, :, :-2]) * 0.5 + (
        axial_flux[:, 2:] - axial_flux[:, :-2]
    ) * 0.5
    centre = padded[:, 2:-2, 2:-2]
    fourth = (
        padded[:, 2:-2, 4:]
        - 4.0 * padded[:, 2:-2, 3:-1]
        + 6.0 * centre
        - 4.0 * padded[:, 2:-2, 1:-3]
        + padded[:, 2:-2, :-4]
        + (
            padded[:, 4:, 2:-2]
            - 4.0 * padded[:, 3:-1, 2:-2]
            + 6.0 * centre
            - 4.0 * padded[:, 1:-3, 2:-2]
            + padded[:, :-4, 2:-2]
        )
    )
    return divergence + DAMPING * fourth + DAMPING * radial_damping(centre, 3)


def flow_ghosts(
    row_zero,
    row_one,
    row_last,
    row_before,
    wrap_low0,
    wrap_low1,
    wrap_high0,
    wrap_high1,
    blade_flag,
    corr_low,
    corr_high,
):
    sign_flip = jnp.array([1.0, 1.0, -1.0, 1.0], jnp.float32).reshape(
        (4,) + (1,) * (row_zero.ndim - 1)
    )
    ghost_m2 = jnp.where(blade_flag, row_one * sign_flip, wrap_low0 + corr_low)
    ghost_m1 = jnp.where(blade_flag, row_zero * sign_flip, wrap_low1 + corr_low)
    ghost_p0 = jnp.where(blade_flag, row_last * sign_flip, wrap_high0 + corr_high)
    ghost_p1 = jnp.where(blade_flag, row_before * sign_flip, wrap_high1 + corr_high)
    return (ghost_m2, ghost_m1, ghost_p0, ghost_p1)


def finish_flow(
    padded, depth, row_flag, corr_low, corr_high, low_end, high_end, first_end, last_end
):
    middle_rows = padded[:, 2:-2]
    width = middle_rows.shape[2]
    ghost_m2, ghost_m1, ghost_p0, ghost_p1 = flow_ghosts(
        middle_rows[:, :, 2],
        middle_rows[:, :, 3],
        middle_rows[:, :, width - 3],
        middle_rows[:, :, width - 4],
        middle_rows[:, :, 0],
        middle_rows[:, :, 1],
        middle_rows[:, :, width - 2],
        middle_rows[:, :, width - 1],
        row_flag[:, None],
        corr_low,
        corr_high,
    )
    low_pair = jnp.where(low_end, jnp.stack([ghost_m2, ghost_m1], 2), middle_rows[:, :, 0:2])
    high_pair = jnp.where(
        high_end, jnp.stack([ghost_p0, ghost_p1], 2), middle_rows[:, :, width - 2 :]
    )
    middle_rows = jnp.concatenate([low_pair, middle_rows[:, :, 2 : width - 2], high_pair], 2)
    whole = jnp.concatenate([padded[:, 0:2], middle_rows, padded[:, -2:]], 1)
    top_copy = jnp.repeat(whole[:, depth : depth + 1], depth, axis=1)
    bottom_copy = jnp.repeat(whole[:, -depth - 1 : -depth], depth, axis=1)
    top_rows = jnp.where(first_end, top_copy, whole[:, :depth])
    bottom_rows = jnp.where(last_end, bottom_copy, whole[:, -depth:])
    return jnp.concatenate([top_rows, whole[:, depth:-depth], bottom_rows], 1)


def _flux(rho, mx, my, en, first, second, sweep):
    inverse = 1.0 / rho
    u = mx * inverse
    v = my * inverse
    pr = (HEAT_RATIO - 1.0) * (en - 0.5 * rho * (u * u + v * v))
    ep = en + pr
    return (
        first * mx + second * my - sweep * rho,
        first * (mx * u + pr) + second * (my * u) - sweep * mx,
        first * (mx * v) + second * (my * v + pr) - sweep * my,
        first * (ep * u) + second * (ep * v) - sweep * en,
    )


def _radial_pairs(c0, lane, forward):
    width = c0.shape[-1]
    last = width - 1
    one_a = pltpu.roll(c0, 1, 1)
    one_b = pltpu.roll(c0, last, 1)
    two_a = pltpu.roll(c0, 2, 1)
    two_b = pltpu.roll(c0, width - 2, 1)
    m1 = jnp.where(lane == 0, c0, jnp.where(forward, one_a, one_b))
    p1 = jnp.where(lane == last, c0, jnp.where(forward, one_b, one_a))
    m2 = jnp.where(lane <= 1, m1, jnp.where(forward, two_a, two_b))
    p2 = jnp.where(lane >= last - 1, p1, jnp.where(forward, two_b, two_a))
    return m1 + p1, m2 + p2


def _volume(grid, a, npch, old):
    def comp(c, row, lo, hi):
        value = grid[c, row, lo:hi]
        if old:
            value = value - grid[c + 2, row, lo:hi]
        return value

    x_zeta = 1.0 + (comp(0, a + 3, 2, npch + 2) - comp(0, a + 1, 2, npch + 2)) * 0.5
    x_xi = (comp(0, a + 2, 3, npch + 3) - comp(0, a + 2, 1, npch + 1)) * 0.5
    y_xi = 1.0 + (comp(1, a + 2, 3, npch + 3) - comp(1, a + 2, 1, npch + 1)) * 0.5
    y_zeta = (comp(1, a + 3, 2, npch + 2) - comp(1, a + 1, 2, npch + 2)) * 0.5
    return x_zeta * y_xi - x_xi * y_zeta


def _section_body(scale, pad_hbm, grid_hbm, q0_hbm, out_hbm, af, pf, pad, grid, q0, out, sems):
    na = out.shape[1]
    npch = out.shape[2]
    width = out.shape[3]

    def row_copy(which, j):
        source, target = ((pad_hbm, pad), (grid_hbm, grid), (q0_hbm, q0), (out, out_hbm))[which]
        return pltpu.make_async_copy(
            source.at[:, pl.ds(j, 1)], target.at[:, pl.ds(j, 1)], sems.at[which, j]
        )

    for j in range(na + 4):
        row_copy(0, j).start()
        if 1 <= j <= na + 2:
            row_copy(1, j).start()
    for j in range(na):
        row_copy(2, j).start()

    def axial_row(j, carry):
        row_copy(0, j + 1).wait()
        row_copy(1, j + 1).wait()
        x_xi = (grid[0, j + 1, 3 : npch + 3] - grid[0, j + 1, 1 : npch + 1]) * 0.5
        y_xi = 1.0 + (grid[1, j + 1, 3 : npch + 3] - grid[1, j + 1, 1 : npch + 1]) * 0.5
        speed_x = grid[2, j + 1, 2 : npch + 2] / TIME_STEP
        speed_y = grid[3, j + 1, 2 : npch + 2] / TIME_STEP
        second = -x_xi
        sweep = y_xi * speed_x + second * speed_y
        q = [pad[k, j + 1, 2 : npch + 2] for k in range(4)]
        f = _flux(*q, y_xi, second, sweep)
        for k in range(4):
            af[k, j] = f[k]
        return carry

    lax.fori_loop(0, na + 2, axial_row, 0)
    lane = lax.broadcasted_iota(jnp.int32, (npch, width), 1)
    probe = pltpu.roll(lane, 1, 1)
    forward = probe == jnp.where(lane == 0, width - 1, lane - 1)

    row_copy(0, 0).wait()
    row_copy(0, na + 3).wait()

    def row(a, carry):
        row_copy(2, a).wait()
        x_zeta = 1.0 + (grid[0, a + 3, 1 : npch + 3] - grid[0, a + 1, 1 : npch + 3]) * 0.5
        y_zeta = (grid[1, a + 3, 1 : npch + 3] - grid[1, a + 1, 1 : npch + 3]) * 0.5
        speed_x = grid[2, a + 2, 1 : npch + 3] / TIME_STEP
        speed_y = grid[3, a + 2, 1 : npch + 3] / TIME_STEP
        first = -y_zeta
        sweep = first * speed_x + x_zeta * speed_y
        q = [pad[k, a + 2, 1 : npch + 3] for k in range(4)]
        f = _flux(*q, first, x_zeta, sweep)
        for k in range(4):
            pf[k] = f[k]
        volume_old = _volume(grid, a, npch, True)
        inverse_new = 1.0 / _volume(grid, a, npch, False)
        for k in range(4):
            div = (pf[k, 2 : npch + 2] - pf[k, 0:npch]) * 0.5 + (af[k, a + 2] - af[k, a]) * 0.5
            c0 = pad[k, a + 2, 2 : npch + 2]
            near_r, far_r = _radial_pairs(c0, lane, forward)
            near = (
                pad[k, a + 2, 3 : npch + 3]
                + pad[k, a + 2, 1 : npch + 1]
                + pad[k, a + 3, 2 : npch + 2]
                + pad[k, a + 1, 2 : npch + 2]
                + near_r
            )
            far = (
                pad[k, a + 2, 4 : npch + 4]
                + pad[k, a + 2, 0:npch]
                + pad[k, a + 4, 2 : npch + 2]
                + pad[k, a, 2 : npch + 2]
                + far_r
            )
            res = div + DAMPING * (far - 4.0 * near + 18.0 * c0)
            out[k, a] = (volume_old * q0[k, a] - scale * res) * inverse_new
        row_copy(3, a).start()
        return carry

    lax.fori_loop(0, na, row, 0)
    for j in range(na):
        row_copy(3, j).wait()


def section_kernel(padded, grid_pad, start, scale, interpret=False):
    _, na, npch, width = start.shape
    body = lambda *refs: _section_body(scale, *refs)
    cells = na * npch * width
    return pl.pallas_call(
        body,
        out_shape=jax.ShapeDtypeStruct(start.shape, start.dtype),
        in_specs=[pl.BlockSpec(memory_space=pl.ANY)] * 3,
        out_specs=pl.BlockSpec(memory_space=pl.ANY),
        scratch_shapes=[
            pltpu.VMEM((4, na + 2, npch, width), jnp.float32),
            pltpu.VMEM((4, npch + 2, width), jnp.float32),
            pltpu.VMEM(padded.shape, jnp.float32),
            pltpu.VMEM(grid_pad.shape, jnp.float32),
            pltpu.VMEM(start.shape, jnp.float32),
            pltpu.VMEM(start.shape, jnp.float32),
            pltpu.SemaphoreType.DMA((4, na + 4)),
        ],
        compiler_params=pltpu.CompilerParams(vmem_limit_bytes=60 * 1024 * 1024),
        cost_estimate=pl.CostEstimate(
            flops=500 * cells, transcendentals=0, bytes_accessed=4 * 14 * cells
        ),
        interpret=interpret,
    )(padded, grid_pad, start)


def per_device(flow_state, node_offset, blade_mode, phase_angles, lag_series):
    n_pitch = lax.axis_size("pitch")
    n_span = lax.axis_size("span")
    pitch_rows = flow_state.shape[2]
    axial_cols = flow_state.shape[1]
    total_pitch = pitch_rows * n_pitch
    total_axial = axial_cols * n_span
    pitch_at = lax.axis_index("pitch")
    span_at = lax.axis_index("span")
    lead_edge = total_axial // 4
    axial_index = span_at * axial_cols + jnp.arange(axial_cols, dtype=jnp.int32)
    blade_flag = (axial_index >= lead_edge) & (axial_index < total_axial - lead_edge)
    blade_mask = blade_flag.astype(jnp.float32)[:, None]
    phase_now = phase_angles[0]
    phase_lag = phase_angles[1]
    low_guess = wall_amplitude(blade_mode, phase_now, blade_mask) * unit_normal(
        node_offset[:, :, 0], node_offset[:, :, 1]
    )
    high_guess = wall_amplitude(blade_mode, phase_now + phase_lag, blade_mask) * unit_normal(
        node_offset[:, :, pitch_rows - 2], node_offset[:, :, pitch_rows - 1]
    )
    low_wall = low_guess
    high_wall = high_guess
    half = n_pitch // 2
    if n_pitch % 2:
        sent = jnp.where(pitch_at == 0, low_guess, high_guess)
        for shift in range(1, n_pitch):
            got = lax.ppermute(sent, "pitch", [(0, shift), (n_pitch - 1, shift - 1)])
            low_wall = jnp.where(pitch_at == shift, got, low_wall)
            high_wall = jnp.where(pitch_at == shift - 1, got, high_wall)
    else:
        known = 1
        while known < half:
            step = min(known, half - known)
            pairs = [(i, i + known) for i in range(step)]
            pairs += [(n_pitch - 1 - i, n_pitch - 1 - i - known) for i in range(step)]
            got = lax.ppermute(
                jnp.where(pitch_at < half, low_wall, high_wall), "pitch", pairs
            )
            takes_low = (pitch_at >= known) & (pitch_at < known + step)
            takes_high = (pitch_at <= n_pitch - 1 - known) & (pitch_at > n_pitch - 1 - known - step)
            low_wall = jnp.where(takes_low, got, low_wall)
            high_wall = jnp.where(takes_high, got, high_wall)
            known += step
        pairs = [(i, (i + half) % n_pitch) for i in range(n_pitch)]
        got = lax.ppermute(jnp.where(pitch_at < half, low_wall, high_wall), "pitch", pairs)
        low_wall = jnp.where(pitch_at >= half, got, low_wall)
        high_wall = jnp.where(pitch_at < half, got, high_wall)
    pitch_index = pitch_at * pitch_rows + jnp.arange(pitch_rows, dtype=jnp.int32)
    blend_row = (pitch_index.astype(jnp.float32) / (total_pitch - 1))[:, None]
    shift_field = (1.0 - blend_row) * low_wall[:, :, None, :] + blend_row * high_wall[:, :, None, :]
    moved_offset = node_offset + shift_field
    grid_field = jnp.concatenate([moved_offset, shift_field], 0)
    rim_width = 2
    grid_pad = padded_2(grid_field, (("pitch", 2), ("span", 1)), rim_width)
    first_pad = padded_cross(flow_state, rim_width)
    low_end = pitch_at == 0
    high_end = pitch_at == n_pitch - 1
    first_end = span_at == 0
    last_end = span_at == n_span - 1
    grid_pad = fill_ends(grid_pad, 1, rim_width, first_end, last_end)
    grid_pad = fill_ends(grid_pad, 2, 2, low_end, high_end)
    corr_low = lag_shift(lag_series[1], phase_now, -phase_lag)
    corr_high = lag_shift(lag_series[0], phase_now, phase_lag)
    padded = finish_flow(
        first_pad, 2, blade_flag, corr_low, corr_high, low_end, high_end, first_end, last_end
    )
    section_one = section_kernel(padded, grid_pad, flow_state, SECTION_WEIGHTS[0] * TIME_STEP)
    second_pad = padded_cross(section_one, 2)
    padded = finish_flow(
        second_pad, 2, blade_flag, corr_low, corr_high, low_end, high_end, first_end, last_end
    )
    current = section_kernel(padded, grid_pad, flow_state, SECTION_WEIGHTS[1] * TIME_STEP)
    return (current, moved_offset)


def solution(mesh):
    placed = (
        P(None, "span", "pitch", None),
        P(None, "span", "pitch", None),
        P(None, "span", None),
        P(),
        P(None, None, None, None, "span", None),
    )
    return jax.shard_map(
        per_device,
        mesh=mesh,
        in_specs=placed,
        out_specs=(P(None, "span", "pitch", None), P(None, "span", "pitch", None)),
        check_vma=False,
    )
```

```python
import jax
import jax.numpy as jnp
from jax import lax
from jax.sharding import PartitionSpec as P
from jax.experimental import pallas as pl
from jax.experimental.pallas import tpu as pltpu

HEAT_RATIO = 1.4
TIME_STEP = 0.25
DAMPING = 0.02
SECTION_WEIGHTS = (0.5, 1.0)


def broadcast(value, axis, root):
    mine = lax.axis_index(axis) == root
    return lax.psum(jnp.where(mine, value, jnp.zeros_like(value)), axis)


def padded_2(block, sides, width):
    for axis, dim in sides:
        count = lax.axis_size(axis)
        forward = [(i, i + 1) for i in range(count - 1)]
        forward.append((count - 1, 0))
        backward = [(target, source) for source, target in forward]
        low = lax.ppermute(
            lax.slice_in_dim(block, block.shape[dim] - width, None, axis=dim), axis, forward
        )
        high = lax.ppermute(lax.slice_in_dim(block, 0, width, axis=dim), axis, backward)
        block = jnp.concatenate([low, block, high], axis=dim)
    return block


def padded_cross(block, width):
    rims = []
    for axis, dim in (("pitch", 2), ("span", 1)):
        count = lax.axis_size(axis)
        forward = [(i, (i + 1) % count) for i in range(count)]
        backward = [(target, source) for source, target in forward]
        low = lax.ppermute(
            lax.slice_in_dim(block, block.shape[dim] - width, None, axis=dim), axis, forward
        )
        high = lax.ppermute(lax.slice_in_dim(block, 0, width, axis=dim), axis, backward)
        rims.append((low, high))
    (pitch_low, pitch_high), (span_low, span_high) = rims
    middle = jnp.concatenate([pitch_low, block, pitch_high], axis=2)
    corner = jnp.zeros(span_low.shape[:2] + (width,) + span_low.shape[3:], block.dtype)
    top = jnp.concatenate([corner, span_low, corner], axis=2)
    bottom = jnp.concatenate([corner, span_high, corner], axis=2)
    return jnp.concatenate([top, middle, bottom], axis=1)


def fill_ends(padded, axis_pos, depth, at_first, at_last):
    length = padded.shape[axis_pos]
    inner_first = lax.slice_in_dim(padded, depth, depth + 1, axis=axis_pos)
    inner_second = lax.slice_in_dim(padded, depth + 1, depth + 2, axis=axis_pos)
    inner_last = lax.slice_in_dim(padded, length - depth - 1, length - depth, axis=axis_pos)
    inner_before = lax.slice_in_dim(padded, length - depth - 2, length - depth - 1, axis=axis_pos)
    step_low = inner_first - inner_second
    step_high = inner_last - inner_before
    low_side = jnp.concatenate(
        [inner_first + float(count) * step_low for count in range(depth, 0, -1)], axis=axis_pos
    )
    high_side = jnp.concatenate(
        [inner_last + float(count) * step_high for count in range(1, depth + 1)], axis=axis_pos
    )
    low_side = jnp.where(at_first, low_side, lax.slice_in_dim(padded, 0, depth, axis=axis_pos))
    high_side = jnp.where(
        at_last, high_side, lax.slice_in_dim(padded, length - depth, length, axis=axis_pos)
    )
    return jnp.concatenate(
        [low_side, lax.slice_in_dim(padded, depth, length - depth, axis=axis_pos), high_side],
        axis=axis_pos,
    )


def radial_damping(values, axis_pos):
    count = values.shape[axis_pos]
    first_row = lax.slice_in_dim(values, 0, 1, axis=axis_pos)
    last_row = lax.slice_in_dim(values, count - 1, count, axis=axis_pos)
    extended = jnp.concatenate([first_row, first_row, values, last_row, last_row], axis=axis_pos)
    return (
        lax.slice_in_dim(extended, 4, 4 + count, axis=axis_pos)
        - 4.0 * lax.slice_in_dim(extended, 3, 3 + count, axis=axis_pos)
        + 6.0 * values
        - 4.0 * lax.slice_in_dim(extended, 1, 1 + count, axis=axis_pos)
        + lax.slice_in_dim(extended, 0, count, axis=axis_pos)
    )


def unit_normal(earlier, later):
    along_x = later[0] - earlier[0]
    along_y = 1.0 + later[1] - earlier[1]
    length = jnp.sqrt(along_x * along_x + along_y * along_y)
    return jnp.stack([along_x / length, along_y / length])


def wall_amplitude(shape_mode, angle, blade_mask):
    return (shape_mode[0] * jnp.cos(angle) - shape_mode[1] * jnp.sin(angle)) * blade_mask


def lag_shift(series, phase_now, phase_move):
    series_sum = jnp.zeros(series.shape[2:], jnp.float32)
    for number in range(series.shape[0]):
        harmonic = float(number + 1)
        change_cos = jnp.cos(harmonic * (phase_now + phase_move)) - jnp.cos(harmonic * phase_now)
        change_sin = jnp.sin(harmonic * (phase_now + phase_move)) - jnp.sin(harmonic * phase_now)
        series_sum = series_sum + series[number, 0] * change_cos - series[number, 1] * change_sin
    return series_sum


def metric_terms(offset_x, offset_y):
    x_zeta = 1.0 + (offset_x[2:, 1:-1] - offset_x[:-2, 1:-1]) * 0.5
    x_xi = (offset_x[1:-1, 2:] - offset_x[1:-1, :-2]) * 0.5
    y_xi = 1.0 + (offset_y[1:-1, 2:] - offset_y[1:-1, :-2]) * 0.5
    y_zeta = (offset_y[2:, 1:-1] - offset_y[:-2, 1:-1]) * 0.5
    return (x_zeta, x_xi, y_xi, y_zeta)


def geometry(grid_pad):
    x_zeta, x_xi, y_xi, y_zeta = metric_terms(grid_pad[0], grid_pad[1])
    old_zeta, old_xi, oldy_xi, oldy_zeta = metric_terms(
        grid_pad[0] - grid_pad[2], grid_pad[1] - grid_pad[3]
    )
    volume_new = (x_zeta * y_xi - x_xi * y_zeta)[1:-1, 1:-1]
    volume_old = (old_zeta * oldy_xi - old_xi * oldy_zeta)[1:-1, 1:-1]
    speed_x = grid_pad[2][1:-1, 1:-1] / TIME_STEP
    speed_y = grid_pad[3][1:-1, 1:-1] / TIME_STEP
    first_pitch = -y_zeta
    sweep_pitch = first_pitch * speed_x + x_zeta * speed_y
    second_axial = -x_xi
    sweep_axial = y_xi * speed_x + second_axial * speed_y
    return (
        (first_pitch, x_zeta, sweep_pitch, y_xi, second_axial, sweep_axial),
        volume_old,
        volume_new,
    )


def directional(strip_cells, first_coef, second_coef, sweep_term):
    density = strip_cells[0]
    vel_x = strip_cells[1] / density
    vel_y = strip_cells[2] / density
    energy = strip_cells[3]
    pressure = (HEAT_RATIO - 1.0) * (energy - 0.5 * density * (vel_x * vel_x + vel_y * vel_y))
    flux_x = jnp.stack(
        [
            strip_cells[1],
            strip_cells[1] * vel_x + pressure,
            strip_cells[1] * vel_y,
            (energy + pressure) * vel_x,
        ]
    )
    flux_y = jnp.stack(
        [
            strip_cells[2],
            strip_cells[2] * vel_x,
            strip_cells[2] * vel_y + pressure,
            (energy + pressure) * vel_y,
        ]
    )
    return first_coef * flux_x + second_coef * flux_y - sweep_term * strip_cells


def residual(padded, geo_terms):
    first_pitch, second_pitch, sweep_pitch, first_axial, second_axial, sweep_axial = geo_terms
    pitch_flux = directional(
        padded[:, 2:-2, 1:-1], first_pitch[1:-1], second_pitch[1:-1], sweep_pitch[1:-1]
    )
    axial_flux = directional(
        padded[:, 1:-1, 2:-2], first_axial[:, 1:-1], second_axial[:, 1:-1], sweep_axial[:, 1:-1]
    )
    divergence = (pitch_flux[:, :, 2:] - pitch_flux[:, :, :-2]) * 0.5 + (
        axial_flux[:, 2:] - axial_flux[:, :-2]
    ) * 0.5
    centre = padded[:, 2:-2, 2:-2]
    fourth = (
        padded[:, 2:-2, 4:]
        - 4.0 * padded[:, 2:-2, 3:-1]
        + 6.0 * centre
        - 4.0 * padded[:, 2:-2, 1:-3]
        + padded[:, 2:-2, :-4]
        + (
            padded[:, 4:, 2:-2]
            - 4.0 * padded[:, 3:-1, 2:-2]
            + 6.0 * centre
            - 4.0 * padded[:, 1:-3, 2:-2]
            + padded[:, :-4, 2:-2]
        )
    )
    return divergence + DAMPING * fourth + DAMPING * radial_damping(centre, 3)


def flow_ghosts(
    row_zero,
    row_one,
    row_last,
    row_before,
    wrap_low0,
    wrap_low1,
    wrap_high0,
    wrap_high1,
    blade_flag,
    corr_low,
    corr_high,
):
    sign_flip = jnp.array([1.0, 1.0, -1.0, 1.0], jnp.float32).reshape(
        (4,) + (1,) * (row_zero.ndim - 1)
    )
    ghost_m2 = jnp.where(blade_flag, row_one * sign_flip, wrap_low0 + corr_low)
    ghost_m1 = jnp.where(blade_flag, row_zero * sign_flip, wrap_low1 + corr_low)
    ghost_p0 = jnp.where(blade_flag, row_last * sign_flip, wrap_high0 + corr_high)
    ghost_p1 = jnp.where(blade_flag, row_before * sign_flip, wrap_high1 + corr_high)
    return (ghost_m2, ghost_m1, ghost_p0, ghost_p1)


def finish_flow(
    padded, depth, row_flag, corr_low, corr_high, low_end, high_end, first_end, last_end
):
    middle_rows = padded[:, 2:-2]
    width = middle_rows.shape[2]
    ghost_m2, ghost_m1, ghost_p0, ghost_p1 = flow_ghosts(
        middle_rows[:, :, 2],
        middle_rows[:, :, 3],
        middle_rows[:, :, width - 3],
        middle_rows[:, :, width - 4],
        middle_rows[:, :, 0],
        middle_rows[:, :, 1],
        middle_rows[:, :, width - 2],
        middle_rows[:, :, width - 1],
        row_flag[:, None],
        corr_low,
        corr_high,
    )
    low_pair = jnp.where(low_end, jnp.stack([ghost_m2, ghost_m1], 2), middle_rows[:, :, 0:2])
    high_pair = jnp.where(
        high_end, jnp.stack([ghost_p0, ghost_p1], 2), middle_rows[:, :, width - 2 :]
    )
    middle_rows = jnp.concatenate([low_pair, middle_rows[:, :, 2 : width - 2], high_pair], 2)
    whole = jnp.concatenate([padded[:, 0:2], middle_rows, padded[:, -2:]], 1)
    top_copy = jnp.repeat(whole[:, depth : depth + 1], depth, axis=1)
    bottom_copy = jnp.repeat(whole[:, -depth - 1 : -depth], depth, axis=1)
    top_rows = jnp.where(first_end, top_copy, whole[:, :depth])
    bottom_rows = jnp.where(last_end, bottom_copy, whole[:, -depth:])
    return jnp.concatenate([top_rows, whole[:, depth:-depth], bottom_rows], 1)


def _flux(rho, mx, my, en, first, second, sweep):
    inverse = 1.0 / rho
    u = mx * inverse
    v = my * inverse
    pr = (HEAT_RATIO - 1.0) * (en - 0.5 * rho * (u * u + v * v))
    ep = en + pr
    return (
        first * mx + second * my - sweep * rho,
        first * (mx * u + pr) + second * (my * u) - sweep * mx,
        first * (mx * v) + second * (my * v + pr) - sweep * my,
        first * (ep * u) + second * (ep * v) - sweep * en,
    )


def _radial_pairs(c0, lane, forward):
    width = c0.shape[-1]
    last = width - 1
    one_a = pltpu.roll(c0, 1, 1)
    one_b = pltpu.roll(c0, last, 1)
    two_a = pltpu.roll(c0, 2, 1)
    two_b = pltpu.roll(c0, width - 2, 1)
    m1 = jnp.where(lane == 0, c0, jnp.where(forward, one_a, one_b))
    p1 = jnp.where(lane == last, c0, jnp.where(forward, one_b, one_a))
    m2 = jnp.where(lane <= 1, m1, jnp.where(forward, two_a, two_b))
    p2 = jnp.where(lane >= last - 1, p1, jnp.where(forward, two_b, two_a))
    return m1 + p1, m2 + p2


def _volume(grid, a, npch, old):
    def comp(c, row, lo, hi):
        value = grid[c, row, lo:hi]
        if old:
            value = value - grid[c + 2, row, lo:hi]
        return value

    x_zeta = 1.0 + (comp(0, a + 3, 2, npch + 2) - comp(0, a + 1, 2, npch + 2)) * 0.5
    x_xi = (comp(0, a + 2, 3, npch + 3) - comp(0, a + 2, 1, npch + 1)) * 0.5
    y_xi = 1.0 + (comp(1, a + 2, 3, npch + 3) - comp(1, a + 2, 1, npch + 1)) * 0.5
    y_zeta = (comp(1, a + 3, 2, npch + 2) - comp(1, a + 1, 2, npch + 2)) * 0.5
    return x_zeta * y_xi - x_xi * y_zeta


def _section_body(scale, pad_hbm, grid_hbm, q0_hbm, out_hbm, af, pf, pad, grid, q0, out, sems):
    na = out.shape[1]
    npch = out.shape[2]
    width = out.shape[3]

    def row_copy(which, j):
        source, target = ((pad_hbm, pad), (grid_hbm, grid), (q0_hbm, q0), (out, out_hbm))[which]
        return pltpu.make_async_copy(
            source.at[:, pl.ds(j, 1)], target.at[:, pl.ds(j, 1)], sems.at[which, j]
        )

    for j in range(na + 4):
        row_copy(0, j).start()
        if 1 <= j <= na + 2:
            row_copy(1, j).start()
    for j in range(na):
        row_copy(2, j).start()

    def axial_row(j, carry):
        row_copy(0, j + 1).wait()
        row_copy(1, j + 1).wait()
        x_xi = (grid[0, j + 1, 3 : npch + 3] - grid[0, j + 1, 1 : npch + 1]) * 0.5
        y_xi = 1.0 + (grid[1, j + 1, 3 : npch + 3] - grid[1, j + 1, 1 : npch + 1]) * 0.5
        speed_x = grid[2, j + 1, 2 : npch + 2] / TIME_STEP
        speed_y = grid[3, j + 1, 2 : npch + 2] / TIME_STEP
        second = -x_xi
        sweep = y_xi * speed_x + second * speed_y
        q = [pad[k, j + 1, 2 : npch + 2] for k in range(4)]
        f = _flux(*q, y_xi, second, sweep)
        for k in range(4):
            af[k, j] = f[k]
        return carry

    lax.fori_loop(0, na + 2, axial_row, 0)
    lane = lax.broadcasted_iota(jnp.int32, (npch, width), 1)
    probe = pltpu.roll(lane, 1, 1)
    forward = probe == jnp.where(lane == 0, width - 1, lane - 1)

    row_copy(0, 0).wait()
    row_copy(0, na + 3).wait()

    def row(a, carry):
        row_copy(2, a).wait()
        x_zeta = 1.0 + (grid[0, a + 3, 1 : npch + 3] - grid[0, a + 1, 1 : npch + 3]) * 0.5
        y_zeta = (grid[1, a + 3, 1 : npch + 3] - grid[1, a + 1, 1 : npch + 3]) * 0.5
        speed_x = grid[2, a + 2, 1 : npch + 3] / TIME_STEP
        speed_y = grid[3, a + 2, 1 : npch + 3] / TIME_STEP
        first = -y_zeta
        sweep = first * speed_x + x_zeta * speed_y
        q = [pad[k, a + 2, 1 : npch + 3] for k in range(4)]
        f = _flux(*q, first, x_zeta, sweep)
        for k in range(4):
            pf[k] = f[k]
        volume_old = _volume(grid, a, npch, True)
        inverse_new = 1.0 / _volume(grid, a, npch, False)
        for k in range(4):
            div = (pf[k, 2 : npch + 2] - pf[k, 0:npch]) * 0.5 + (af[k, a + 2] - af[k, a]) * 0.5
            c0 = pad[k, a + 2, 2 : npch + 2]
            near_r, far_r = _radial_pairs(c0, lane, forward)
            near = (
                pad[k, a + 2, 3 : npch + 3]
                + pad[k, a + 2, 1 : npch + 1]
                + pad[k, a + 3, 2 : npch + 2]
                + pad[k, a + 1, 2 : npch + 2]
                + near_r
            )
            far = (
                pad[k, a + 2, 4 : npch + 4]
                + pad[k, a + 2, 0:npch]
                + pad[k, a + 4, 2 : npch + 2]
                + pad[k, a, 2 : npch + 2]
                + far_r
            )
            res = div + DAMPING * (far - 4.0 * near + 18.0 * c0)
            out[k, a] = (volume_old * q0[k, a] - scale * res) * inverse_new
        row_copy(3, a).start()
        return carry

    lax.fori_loop(0, na, row, 0)
    for j in range(na):
        row_copy(3, j).wait()


def section_kernel(padded, grid_pad, start, scale, interpret=False):
    _, na, npch, width = start.shape
    body = lambda *refs: _section_body(scale, *refs)
    cells = na * npch * width
    return pl.pallas_call(
        body,
        out_shape=jax.ShapeDtypeStruct(start.shape, start.dtype),
        in_specs=[pl.BlockSpec(memory_space=pl.ANY)] * 3,
        out_specs=pl.BlockSpec(memory_space=pl.ANY),
        scratch_shapes=[
            pltpu.VMEM((4, na + 2, npch, width), jnp.float32),
            pltpu.VMEM((4, npch + 2, width), jnp.float32),
            pltpu.VMEM(padded.shape, jnp.float32),
            pltpu.VMEM(grid_pad.shape, jnp.float32),
            pltpu.VMEM(start.shape, jnp.float32),
            pltpu.VMEM(start.shape, jnp.float32),
            pltpu.SemaphoreType.DMA((4, na + 4)),
        ],
        compiler_params=pltpu.CompilerParams(vmem_limit_bytes=60 * 1024 * 1024),
        cost_estimate=pl.CostEstimate(
            flops=500 * cells, transcendentals=0, bytes_accessed=4 * 14 * cells
        ),
        interpret=interpret,
    )(padded, grid_pad, start)


def per_device(flow_state, node_offset, blade_mode, phase_angles, lag_series):
    n_pitch = lax.axis_size("pitch")
    n_span = lax.axis_size("span")
    pitch_rows = flow_state.shape[2]
    axial_cols = flow_state.shape[1]
    total_pitch = pitch_rows * n_pitch
    total_axial = axial_cols * n_span
    pitch_at = lax.axis_index("pitch")
    span_at = lax.axis_index("span")
    lead_edge = total_axial // 4
    axial_index = span_at * axial_cols + jnp.arange(axial_cols, dtype=jnp.int32)
    blade_flag = (axial_index >= lead_edge) & (axial_index < total_axial - lead_edge)
    blade_mask = blade_flag.astype(jnp.float32)[:, None]
    phase_now = phase_angles[0]
    phase_lag = phase_angles[1]
    low_guess = wall_amplitude(blade_mode, phase_now, blade_mask) * unit_normal(
        node_offset[:, :, 0], node_offset[:, :, 1]
    )
    high_guess = wall_amplitude(blade_mode, phase_now + phase_lag, blade_mask) * unit_normal(
        node_offset[:, :, pitch_rows - 2], node_offset[:, :, pitch_rows - 1]
    )
    node_side = padded_2(node_offset, (("pitch", 2),), 2)
    low_wall = low_guess
    high_wall = high_guess
    half = n_pitch // 2
    if n_pitch % 2:
        sent = jnp.where(pitch_at == 0, low_guess, high_guess)
        for shift in range(1, n_pitch):
            got = lax.ppermute(sent, "pitch", [(0, shift), (n_pitch - 1, shift - 1)])
            low_wall = jnp.where(pitch_at == shift, got, low_wall)
            high_wall = jnp.where(pitch_at == shift - 1, got, high_wall)
    else:
        known = 1
        while known < half:
            step = min(known, half - known)
            pairs = [(i, i + known) for i in range(step)]
            pairs += [(n_pitch - 1 - i, n_pitch - 1 - i - known) for i in range(step)]
            got = lax.ppermute(
                jnp.where(pitch_at < half, low_wall, high_wall), "pitch", pairs
            )
            takes_low = (pitch_at >= known) & (pitch_at < known + step)
            takes_high = (pitch_at <= n_pitch - 1 - known) & (pitch_at > n_pitch - 1 - known - step)
            low_wall = jnp.where(takes_low, got, low_wall)
            high_wall = jnp.where(takes_high, got, high_wall)
            known += step
        pairs = [(i, (i + half) % n_pitch) for i in range(n_pitch)]
        got = lax.ppermute(jnp.where(pitch_at < half, low_wall, high_wall), "pitch", pairs)
        low_wall = jnp.where(pitch_at >= half, got, low_wall)
        high_wall = jnp.where(pitch_at < half, got, high_wall)
    pitch_index = pitch_at * pitch_rows + jnp.arange(pitch_rows, dtype=jnp.int32)
    blend_row = (pitch_index.astype(jnp.float32) / (total_pitch - 1))[:, None]
    shift_field = (1.0 - blend_row) * low_wall[:, :, None, :] + blend_row * high_wall[:, :, None, :]
    moved_offset = node_offset + shift_field
    rim_width = 2
    pitch_wide = pitch_at * pitch_rows + jnp.arange(
        -rim_width, pitch_rows + rim_width, dtype=jnp.int32
    )
    blend_wide = (pitch_wide.astype(jnp.float32) / (total_pitch - 1))[:, None]
    shift_wide = (1.0 - blend_wide) * low_wall[:, :, None, :] + blend_wide * high_wall[:, :, None, :]
    grid_side = jnp.concatenate([node_side + shift_wide, shift_wide], 0)
    grid_pad = padded_2(grid_side, (("span", 1),), rim_width)
    first_pad = padded_cross(flow_state, rim_width)
    low_end = pitch_at == 0
    high_end = pitch_at == n_pitch - 1
    first_end = span_at == 0
    last_end = span_at == n_span - 1
    grid_pad = fill_ends(grid_pad, 1, rim_width, first_end, last_end)
    grid_pad = fill_ends(grid_pad, 2, 2, low_end, high_end)
    corr_low = lag_shift(lag_series[1], phase_now, -phase_lag)
    corr_high = lag_shift(lag_series[0], phase_now, phase_lag)
    padded = finish_flow(
        first_pad, 2, blade_flag, corr_low, corr_high, low_end, high_end, first_end, last_end
    )
    section_one = section_kernel(padded, grid_pad, flow_state, SECTION_WEIGHTS[0] * TIME_STEP)
    second_pad = padded_cross(section_one, 2)
    padded = finish_flow(
        second_pad, 2, blade_flag, corr_low, corr_high, low_end, high_end, first_end, last_end
    )
    current = section_kernel(padded, grid_pad, flow_state, SECTION_WEIGHTS[1] * TIME_STEP)
    return (current, moved_offset)


def solution(mesh):
    placed = (
        P(None, "span", "pitch", None),
        P(None, "span", "pitch", None),
        P(None, "span", None),
        P(),
        P(None, None, None, None, "span", None),
    )
    return jax.shard_map(
        per_device,
        mesh=mesh,
        in_specs=placed,
        out_specs=(P(None, "span", "pitch", None), P(None, "span", "pitch", None)),
        check_vma=False,
    )
```

```python
import jax
import jax.numpy as jnp
from jax import lax
from jax.sharding import PartitionSpec as P
from jax.experimental import pallas as pl
from jax.experimental.pallas import tpu as pltpu

HEAT_RATIO = 1.4
TIME_STEP = 0.25
DAMPING = 0.02
SECTION_WEIGHTS = (0.5, 1.0)


def broadcast(value, axis, root):
    mine = lax.axis_index(axis) == root
    return lax.psum(jnp.where(mine, value, jnp.zeros_like(value)), axis)


def padded_2(block, sides, width):
    for axis, dim in sides:
        count = lax.axis_size(axis)
        forward = [(i, i + 1) for i in range(count - 1)]
        forward.append((count - 1, 0))
        backward = [(target, source) for source, target in forward]
        low = lax.ppermute(
            lax.slice_in_dim(block, block.shape[dim] - width, None, axis=dim), axis, forward
        )
        high = lax.ppermute(lax.slice_in_dim(block, 0, width, axis=dim), axis, backward)
        block = jnp.concatenate([low, block, high], axis=dim)
    return block


def padded_cross(block, width):
    rims = []
    for axis, dim in (("pitch", 2), ("span", 1)):
        count = lax.axis_size(axis)
        forward = [(i, (i + 1) % count) for i in range(count)]
        backward = [(target, source) for source, target in forward]
        low = lax.ppermute(
            lax.slice_in_dim(block, block.shape[dim] - width, None, axis=dim), axis, forward
        )
        high = lax.ppermute(lax.slice_in_dim(block, 0, width, axis=dim), axis, backward)
        rims.append((low, high))
    (pitch_low, pitch_high), (span_low, span_high) = rims
    middle = jnp.concatenate([pitch_low, block, pitch_high], axis=2)
    corner = jnp.zeros(span_low.shape[:2] + (width,) + span_low.shape[3:], block.dtype)
    top = jnp.concatenate([corner, span_low, corner], axis=2)
    bottom = jnp.concatenate([corner, span_high, corner], axis=2)
    return jnp.concatenate([top, middle, bottom], axis=1)


def fill_ends(padded, axis_pos, depth, at_first, at_last):
    length = padded.shape[axis_pos]
    inner_first = lax.slice_in_dim(padded, depth, depth + 1, axis=axis_pos)
    inner_second = lax.slice_in_dim(padded, depth + 1, depth + 2, axis=axis_pos)
    inner_last = lax.slice_in_dim(padded, length - depth - 1, length - depth, axis=axis_pos)
    inner_before = lax.slice_in_dim(padded, length - depth - 2, length - depth - 1, axis=axis_pos)
    step_low = inner_first - inner_second
    step_high = inner_last - inner_before
    low_side = jnp.concatenate(
        [inner_first + float(count) * step_low for count in range(depth, 0, -1)], axis=axis_pos
    )
    high_side = jnp.concatenate(
        [inner_last + float(count) * step_high for count in range(1, depth + 1)], axis=axis_pos
    )
    low_side = jnp.where(at_first, low_side, lax.slice_in_dim(padded, 0, depth, axis=axis_pos))
    high_side = jnp.where(
        at_last, high_side, lax.slice_in_dim(padded, length - depth, length, axis=axis_pos)
    )
    return jnp.concatenate(
        [low_side, lax.slice_in_dim(padded, depth, length - depth, axis=axis_pos), high_side],
        axis=axis_pos,
    )


def radial_damping(values, axis_pos):
    count = values.shape[axis_pos]
    first_row = lax.slice_in_dim(values, 0, 1, axis=axis_pos)
    last_row = lax.slice_in_dim(values, count - 1, count, axis=axis_pos)
    extended = jnp.concatenate([first_row, first_row, values, last_row, last_row], axis=axis_pos)
    return (
        lax.slice_in_dim(extended, 4, 4 + count, axis=axis_pos)
        - 4.0 * lax.slice_in_dim(extended, 3, 3 + count, axis=axis_pos)
        + 6.0 * values
        - 4.0 * lax.slice_in_dim(extended, 1, 1 + count, axis=axis_pos)
        + lax.slice_in_dim(extended, 0, count, axis=axis_pos)
    )


def unit_normal(earlier, later):
    along_x = later[0] - earlier[0]
    along_y = 1.0 + later[1] - earlier[1]
    length = jnp.sqrt(along_x * along_x + along_y * along_y)
    return jnp.stack([along_x / length, along_y / length])


def wall_amplitude(shape_mode, angle, blade_mask):
    return (shape_mode[0] * jnp.cos(angle) - shape_mode[1] * jnp.sin(angle)) * blade_mask


def lag_shift(series, phase_now, phase_move):
    series_sum = jnp.zeros(series.shape[2:], jnp.float32)
    for number in range(series.shape[0]):
        harmonic = float(number + 1)
        change_cos = jnp.cos(harmonic * (phase_now + phase_move)) - jnp.cos(harmonic * phase_now)
        change_sin = jnp.sin(harmonic * (phase_now + phase_move)) - jnp.sin(harmonic * phase_now)
        series_sum = series_sum + series[number, 0] * change_cos - series[number, 1] * change_sin
    return series_sum


def metric_terms(offset_x, offset_y):
    x_zeta = 1.0 + (offset_x[2:, 1:-1] - offset_x[:-2, 1:-1]) * 0.5
    x_xi = (offset_x[1:-1, 2:] - offset_x[1:-1, :-2]) * 0.5
    y_xi = 1.0 + (offset_y[1:-1, 2:] - offset_y[1:-1, :-2]) * 0.5
    y_zeta = (offset_y[2:, 1:-1] - offset_y[:-2, 1:-1]) * 0.5
    return (x_zeta, x_xi, y_xi, y_zeta)


def geometry(grid_pad):
    x_zeta, x_xi, y_xi, y_zeta = metric_terms(grid_pad[0], grid_pad[1])
    old_zeta, old_xi, oldy_xi, oldy_zeta = metric_terms(
        grid_pad[0] - grid_pad[2], grid_pad[1] - grid_pad[3]
    )
    volume_new = (x_zeta * y_xi - x_xi * y_zeta)[1:-1, 1:-1]
    volume_old = (old_zeta * oldy_xi - old_xi * oldy_zeta)[1:-1, 1:-1]
    speed_x = grid_pad[2][1:-1, 1:-1] / TIME_STEP
    speed_y = grid_pad[3][1:-1, 1:-1] / TIME_STEP
    first_pitch = -y_zeta
    sweep_pitch = first_pitch * speed_x + x_zeta * speed_y
    second_axial = -x_xi
    sweep_axial = y_xi * speed_x + second_axial * speed_y
    return (
        (first_pitch, x_zeta, sweep_pitch, y_xi, second_axial, sweep_axial),
        volume_old,
        volume_new,
    )


def directional(strip_cells, first_coef, second_coef, sweep_term):
    density = strip_cells[0]
    vel_x = strip_cells[1] / density
    vel_y = strip_cells[2] / density
    energy = strip_cells[3]
    pressure = (HEAT_RATIO - 1.0) * (energy - 0.5 * density * (vel_x * vel_x + vel_y * vel_y))
    flux_x = jnp.stack(
        [
            strip_cells[1],
            strip_cells[1] * vel_x + pressure,
            strip_cells[1] * vel_y,
            (energy + pressure) * vel_x,
        ]
    )
    flux_y = jnp.stack(
        [
            strip_cells[2],
            strip_cells[2] * vel_x,
            strip_cells[2] * vel_y + pressure,
            (energy + pressure) * vel_y,
        ]
    )
    return first_coef * flux_x + second_coef * flux_y - sweep_term * strip_cells


def residual(padded, geo_terms):
    first_pitch, second_pitch, sweep_pitch, first_axial, second_axial, sweep_axial = geo_terms
    pitch_flux = directional(
        padded[:, 2:-2, 1:-1], first_pitch[1:-1], second_pitch[1:-1], sweep_pitch[1:-1]
    )
    axial_flux = directional(
        padded[:, 1:-1, 2:-2], first_axial[:, 1:-1], second_axial[:, 1:-1], sweep_axial[:, 1:-1]
    )
    divergence = (pitch_flux[:, :, 2:] - pitch_flux[:, :, :-2]) * 0.5 + (
        axial_flux[:, 2:] - axial_flux[:, :-2]
    ) * 0.5
    centre = padded[:, 2:-2, 2:-2]
    fourth = (
        padded[:, 2:-2, 4:]
        - 4.0 * padded[:, 2:-2, 3:-1]
        + 6.0 * centre
        - 4.0 * padded[:, 2:-2, 1:-3]
        + padded[:, 2:-2, :-4]
        + (
            padded[:, 4:, 2:-2]
            - 4.0 * padded[:, 3:-1, 2:-2]
            + 6.0 * centre
            - 4.0 * padded[:, 1:-3, 2:-2]
            + padded[:, :-4, 2:-2]
        )
    )
    return divergence + DAMPING * fourth + DAMPING * radial_damping(centre, 3)


def flow_ghosts(
    row_zero,
    row_one,
    row_last,
    row_before,
    wrap_low0,
    wrap_low1,
    wrap_high0,
    wrap_high1,
    blade_flag,
    corr_low,
    corr_high,
):
    sign_flip = jnp.array([1.0, 1.0, -1.0, 1.0], jnp.float32).reshape(
        (4,) + (1,) * (row_zero.ndim - 1)
    )
    ghost_m2 = jnp.where(blade_flag, row_one * sign_flip, wrap_low0 + corr_low)
    ghost_m1 = jnp.where(blade_flag, row_zero * sign_flip, wrap_low1 + corr_low)
    ghost_p0 = jnp.where(blade_flag, row_last * sign_flip, wrap_high0 + corr_high)
    ghost_p1 = jnp.where(blade_flag, row_before * sign_flip, wrap_high1 + corr_high)
    return (ghost_m2, ghost_m1, ghost_p0, ghost_p1)


def finish_flow(
    padded, depth, row_flag, corr_low, corr_high, low_end, high_end, first_end, last_end
):
    middle_rows = padded[:, 2:-2]
    width = middle_rows.shape[2]
    ghost_m2, ghost_m1, ghost_p0, ghost_p1 = flow_ghosts(
        middle_rows[:, :, 2],
        middle_rows[:, :, 3],
        middle_rows[:, :, width - 3],
        middle_rows[:, :, width - 4],
        middle_rows[:, :, 0],
        middle_rows[:, :, 1],
        middle_rows[:, :, width - 2],
        middle_rows[:, :, width - 1],
        row_flag[:, None],
        corr_low,
        corr_high,
    )
    low_pair = jnp.where(low_end, jnp.stack([ghost_m2, ghost_m1], 2), middle_rows[:, :, 0:2])
    high_pair = jnp.where(
        high_end, jnp.stack([ghost_p0, ghost_p1], 2), middle_rows[:, :, width - 2 :]
    )
    middle_rows = jnp.concatenate([low_pair, middle_rows[:, :, 2 : width - 2], high_pair], 2)
    whole = jnp.concatenate([padded[:, 0:2], middle_rows, padded[:, -2:]], 1)
    top_copy = jnp.repeat(whole[:, depth : depth + 1], depth, axis=1)
    bottom_copy = jnp.repeat(whole[:, -depth - 1 : -depth], depth, axis=1)
    top_rows = jnp.where(first_end, top_copy, whole[:, :depth])
    bottom_rows = jnp.where(last_end, bottom_copy, whole[:, -depth:])
    return jnp.concatenate([top_rows, whole[:, depth:-depth], bottom_rows], 1)


def _flux(rho, mx, my, en, first, second, sweep):
    inverse = 1.0 / rho
    u = mx * inverse
    v = my * inverse
    pr = (HEAT_RATIO - 1.0) * (en - 0.5 * rho * (u * u + v * v))
    ep = en + pr
    return (
        first * mx + second * my - sweep * rho,
        first * (mx * u + pr) + second * (my * u) - sweep * mx,
        first * (mx * v) + second * (my * v + pr) - sweep * my,
        first * (ep * u) + second * (ep * v) - sweep * en,
    )


def _radial_pairs(c0, lane, forward):
    width = c0.shape[-1]
    last = width - 1
    one_a = pltpu.roll(c0, 1, 1)
    one_b = pltpu.roll(c0, last, 1)
    two_a = pltpu.roll(c0, 2, 1)
    two_b = pltpu.roll(c0, width - 2, 1)
    m1 = jnp.where(lane == 0, c0, jnp.where(forward, one_a, one_b))
    p1 = jnp.where(lane == last, c0, jnp.where(forward, one_b, one_a))
    m2 = jnp.where(lane <= 1, m1, jnp.where(forward, two_a, two_b))
    p2 = jnp.where(lane >= last - 1, p1, jnp.where(forward, two_b, two_a))
    return m1 + p1, m2 + p2


def _volume(grid, a, npch, old):
    def comp(c, row, lo, hi):
        value = grid[c, row, lo:hi]
        if old:
            value = value - grid[c + 2, row, lo:hi]
        return value

    x_zeta = 1.0 + (comp(0, a + 3, 2, npch + 2) - comp(0, a + 1, 2, npch + 2)) * 0.5
    x_xi = (comp(0, a + 2, 3, npch + 3) - comp(0, a + 2, 1, npch + 1)) * 0.5
    y_xi = 1.0 + (comp(1, a + 2, 3, npch + 3) - comp(1, a + 2, 1, npch + 1)) * 0.5
    y_zeta = (comp(1, a + 3, 2, npch + 2) - comp(1, a + 1, 2, npch + 2)) * 0.5
    return x_zeta * y_xi - x_xi * y_zeta


def _section_body(scale, pad_hbm, grid_hbm, q0_hbm, out_hbm, af, pf, pad, grid, q0, out, sems):
    na = out.shape[1]
    npch = out.shape[2]
    width = out.shape[3]

    def row_copy(which, j):
        source, target = ((pad_hbm, pad), (grid_hbm, grid), (q0_hbm, q0), (out, out_hbm))[which]
        return pltpu.make_async_copy(
            source.at[:, pl.ds(j, 1)], target.at[:, pl.ds(j, 1)], sems.at[which, j]
        )

    for j in range(na + 4):
        row_copy(0, j).start()
        if 1 <= j <= na + 2:
            row_copy(1, j).start()
    for j in range(na):
        row_copy(2, j).start()

    def axial_row(j, carry):
        row_copy(0, j + 1).wait()
        row_copy(1, j + 1).wait()
        x_xi = (grid[0, j + 1, 3 : npch + 3] - grid[0, j + 1, 1 : npch + 1]) * 0.5
        y_xi = 1.0 + (grid[1, j + 1, 3 : npch + 3] - grid[1, j + 1, 1 : npch + 1]) * 0.5
        speed_x = grid[2, j + 1, 2 : npch + 2] / TIME_STEP
        speed_y = grid[3, j + 1, 2 : npch + 2] / TIME_STEP
        second = -x_xi
        sweep = y_xi * speed_x + second * speed_y
        q = [pad[k, j + 1, 2 : npch + 2] for k in range(4)]
        f = _flux(*q, y_xi, second, sweep)
        for k in range(4):
            af[k, j] = f[k]
        return carry

    lax.fori_loop(0, na + 2, axial_row, 0)
    lane = lax.broadcasted_iota(jnp.int32, (npch, width), 1)
    probe = pltpu.roll(lane, 1, 1)
    forward = probe == jnp.where(lane == 0, width - 1, lane - 1)

    row_copy(0, 0).wait()
    row_copy(0, na + 3).wait()

    def one_row(a, buffer):
        row_copy(2, a).wait()
        x_zeta = 1.0 + (grid[0, a + 3, 1 : npch + 3] - grid[0, a + 1, 1 : npch + 3]) * 0.5
        y_zeta = (grid[1, a + 3, 1 : npch + 3] - grid[1, a + 1, 1 : npch + 3]) * 0.5
        speed_x = grid[2, a + 2, 1 : npch + 3] / TIME_STEP
        speed_y = grid[3, a + 2, 1 : npch + 3] / TIME_STEP
        first = -y_zeta
        sweep = first * speed_x + x_zeta * speed_y
        q = [pad[k, a + 2, 1 : npch + 3] for k in range(4)]
        f = _flux(*q, first, x_zeta, sweep)
        for k in range(4):
            pf[buffer, k] = f[k]
        volume_old = _volume(grid, a, npch, True)
        inverse_new = 1.0 / _volume(grid, a, npch, False)
        for k in range(4):
            div = (pf[buffer, k, 2 : npch + 2] - pf[buffer, k, 0:npch]) * 0.5 + (
                af[k, a + 2] - af[k, a]
            ) * 0.5
            c0 = pad[k, a + 2, 2 : npch + 2]
            near_r, far_r = _radial_pairs(c0, lane, forward)
            near = (
                pad[k, a + 2, 3 : npch + 3]
                + pad[k, a + 2, 1 : npch + 1]
                + pad[k, a + 3, 2 : npch + 2]
                + pad[k, a + 1, 2 : npch + 2]
                + near_r
            )
            far = (
                pad[k, a + 2, 4 : npch + 4]
                + pad[k, a + 2, 0:npch]
                + pad[k, a + 4, 2 : npch + 2]
                + pad[k, a, 2 : npch + 2]
                + far_r
            )
            res = div + DAMPING * (far - 4.0 * near + 18.0 * c0)
            out[k, a] = (volume_old * q0[k, a] - scale * res) * inverse_new
        row_copy(3, a).start()

    def row_pair(pair, carry):
        one_row(2 * pair, 0)
        one_row(2 * pair + 1, 1)
        return carry

    lax.fori_loop(0, na // 2, row_pair, 0)
    if na % 2:
        one_row(na - 1, 0)
    for j in range(na):
        row_copy(3, j).wait()


def section_kernel(padded, grid_pad, start, scale, interpret=False):
    _, na, npch, width = start.shape
    body = lambda *refs: _section_body(scale, *refs)
    cells = na * npch * width
    return pl.pallas_call(
        body,
        out_shape=jax.ShapeDtypeStruct(start.shape, start.dtype),
        in_specs=[pl.BlockSpec(memory_space=pl.ANY)] * 3,
        out_specs=pl.BlockSpec(memory_space=pl.ANY),
        scratch_shapes=[
            pltpu.VMEM((4, na + 2, npch, width), jnp.float32),
            pltpu.VMEM((2, 4, npch + 2, width), jnp.float32),
            pltpu.VMEM(padded.shape, jnp.float32),
            pltpu.VMEM(grid_pad.shape, jnp.float32),
            pltpu.VMEM(start.shape, jnp.float32),
            pltpu.VMEM(start.shape, jnp.float32),
            pltpu.SemaphoreType.DMA((4, na + 4)),
        ],
        compiler_params=pltpu.CompilerParams(vmem_limit_bytes=60 * 1024 * 1024),
        cost_estimate=pl.CostEstimate(
            flops=500 * cells, transcendentals=0, bytes_accessed=4 * 14 * cells
        ),
        interpret=interpret,
    )(padded, grid_pad, start)


def per_device(flow_state, node_offset, blade_mode, phase_angles, lag_series):
    n_pitch = lax.axis_size("pitch")
    n_span = lax.axis_size("span")
    pitch_rows = flow_state.shape[2]
    axial_cols = flow_state.shape[1]
    total_pitch = pitch_rows * n_pitch
    total_axial = axial_cols * n_span
    pitch_at = lax.axis_index("pitch")
    span_at = lax.axis_index("span")
    lead_edge = total_axial // 4
    axial_index = span_at * axial_cols + jnp.arange(axial_cols, dtype=jnp.int32)
    blade_flag = (axial_index >= lead_edge) & (axial_index < total_axial - lead_edge)
    blade_mask = blade_flag.astype(jnp.float32)[:, None]
    phase_now = phase_angles[0]
    phase_lag = phase_angles[1]
    low_guess = wall_amplitude(blade_mode, phase_now, blade_mask) * unit_normal(
        node_offset[:, :, 0], node_offset[:, :, 1]
    )
    high_guess = wall_amplitude(blade_mode, phase_now + phase_lag, blade_mask) * unit_normal(
        node_offset[:, :, pitch_rows - 2], node_offset[:, :, pitch_rows - 1]
    )
    low_wall = low_guess
    high_wall = high_guess
    half = n_pitch // 2
    if n_pitch % 2:
        sent = jnp.where(pitch_at == 0, low_guess, high_guess)
        for shift in range(1, n_pitch):
            got = lax.ppermute(sent, "pitch", [(0, shift), (n_pitch - 1, shift - 1)])
            low_wall = jnp.where(pitch_at == shift, got, low_wall)
            high_wall = jnp.where(pitch_at == shift - 1, got, high_wall)
    else:
        known = 1
        while known < half:
            step = min(known, half - known)
            pairs = [(i, i + known) for i in range(step)]
            pairs += [(n_pitch - 1 - i, n_pitch - 1 - i - known) for i in range(step)]
            got = lax.ppermute(
                jnp.where(pitch_at < half, low_wall, high_wall), "pitch", pairs
            )
            takes_low = (pitch_at >= known) & (pitch_at < known + step)
            takes_high = (pitch_at <= n_pitch - 1 - known) & (pitch_at > n_pitch - 1 - known - step)
            low_wall = jnp.where(takes_low, got, low_wall)
            high_wall = jnp.where(takes_high, got, high_wall)
            known += step
        pairs = [(i, (i + half) % n_pitch) for i in range(n_pitch)]
        got = lax.ppermute(jnp.where(pitch_at < half, low_wall, high_wall), "pitch", pairs)
        low_wall = jnp.where(pitch_at >= half, got, low_wall)
        high_wall = jnp.where(pitch_at < half, got, high_wall)
    pitch_index = pitch_at * pitch_rows + jnp.arange(pitch_rows, dtype=jnp.int32)
    blend_row = (pitch_index.astype(jnp.float32) / (total_pitch - 1))[:, None]
    shift_field = (1.0 - blend_row) * low_wall[:, :, None, :] + blend_row * high_wall[:, :, None, :]
    moved_offset = node_offset + shift_field
    grid_field = jnp.concatenate([moved_offset, shift_field], 0)
    rim_width = 2
    grid_pad = padded_2(grid_field, (("pitch", 2), ("span", 1)), rim_width)
    first_pad = padded_cross(flow_state, rim_width)
    low_end = pitch_at == 0
    high_end = pitch_at == n_pitch - 1
    first_end = span_at == 0
    last_end = span_at == n_span - 1
    grid_pad = fill_ends(grid_pad, 1, rim_width, first_end, last_end)
    grid_pad = fill_ends(grid_pad, 2, 2, low_end, high_end)
    corr_low = lag_shift(lag_series[1], phase_now, -phase_lag)
    corr_high = lag_shift(lag_series[0], phase_now, phase_lag)
    padded = finish_flow(
        first_pad, 2, blade_flag, corr_low, corr_high, low_end, high_end, first_end, last_end
    )
    section_one = section_kernel(padded, grid_pad, flow_state, SECTION_WEIGHTS[0] * TIME_STEP)
    second_pad = padded_cross(section_one, 2)
    padded = finish_flow(
        second_pad, 2, blade_flag, corr_low, corr_high, low_end, high_end, first_end, last_end
    )
    current = section_kernel(padded, grid_pad, flow_state, SECTION_WEIGHTS[1] * TIME_STEP)
    return (current, moved_offset)


def solution(mesh):
    placed = (
        P(None, "span", "pitch", None),
        P(None, "span", "pitch", None),
        P(None, "span", None),
        P(),
        P(None, None, None, None, "span", None),
    )
    return jax.shard_map(
        per_device,
        mesh=mesh,
        in_specs=placed,
        out_specs=(P(None, "span", "pitch", None), P(None, "span", "pitch", None)),
        check_vma=False,
    )
```

```python
import jax
import jax.numpy as jnp
from jax import lax
from jax.sharding import PartitionSpec as P
from jax.experimental import pallas as pl
from jax.experimental.pallas import tpu as pltpu

HEAT_RATIO = 1.4
TIME_STEP = 0.25
DAMPING = 0.02
SECTION_WEIGHTS = (0.5, 1.0)


def broadcast(value, axis, root):
    mine = lax.axis_index(axis) == root
    return lax.psum(jnp.where(mine, value, jnp.zeros_like(value)), axis)


def padded_2(block, sides, width):
    for axis, dim in sides:
        count = lax.axis_size(axis)
        forward = [(i, i + 1) for i in range(count - 1)]
        forward.append((count - 1, 0))
        backward = [(target, source) for source, target in forward]
        low = lax.ppermute(
            lax.slice_in_dim(block, block.shape[dim] - width, None, axis=dim), axis, forward
        )
        high = lax.ppermute(lax.slice_in_dim(block, 0, width, axis=dim), axis, backward)
        block = jnp.concatenate([low, block, high], axis=dim)
    return block


def padded_cross(block, width):
    rims = []
    for axis, dim in (("pitch", 2), ("span", 1)):
        count = lax.axis_size(axis)
        forward = [(i, (i + 1) % count) for i in range(count)]
        backward = [(target, source) for source, target in forward]
        low = lax.ppermute(
            lax.slice_in_dim(block, block.shape[dim] - width, None, axis=dim), axis, forward
        )
        high = lax.ppermute(lax.slice_in_dim(block, 0, width, axis=dim), axis, backward)
        rims.append((low, high))
    (pitch_low, pitch_high), (span_low, span_high) = rims
    middle = jnp.concatenate([pitch_low, block, pitch_high], axis=2)
    corner = jnp.zeros(span_low.shape[:2] + (width,) + span_low.shape[3:], block.dtype)
    top = jnp.concatenate([corner, span_low, corner], axis=2)
    bottom = jnp.concatenate([corner, span_high, corner], axis=2)
    return jnp.concatenate([top, middle, bottom], axis=1)


def fill_ends(padded, axis_pos, depth, at_first, at_last):
    length = padded.shape[axis_pos]
    inner_first = lax.slice_in_dim(padded, depth, depth + 1, axis=axis_pos)
    inner_second = lax.slice_in_dim(padded, depth + 1, depth + 2, axis=axis_pos)
    inner_last = lax.slice_in_dim(padded, length - depth - 1, length - depth, axis=axis_pos)
    inner_before = lax.slice_in_dim(padded, length - depth - 2, length - depth - 1, axis=axis_pos)
    step_low = inner_first - inner_second
    step_high = inner_last - inner_before
    low_side = jnp.concatenate(
        [inner_first + float(count) * step_low for count in range(depth, 0, -1)], axis=axis_pos
    )
    high_side = jnp.concatenate(
        [inner_last + float(count) * step_high for count in range(1, depth + 1)], axis=axis_pos
    )
    low_side = jnp.where(at_first, low_side, lax.slice_in_dim(padded, 0, depth, axis=axis_pos))
    high_side = jnp.where(
        at_last, high_side, lax.slice_in_dim(padded, length - depth, length, axis=axis_pos)
    )
    return jnp.concatenate(
        [low_side, lax.slice_in_dim(padded, depth, length - depth, axis=axis_pos), high_side],
        axis=axis_pos,
    )


def radial_damping(values, axis_pos):
    count = values.shape[axis_pos]
    first_row = lax.slice_in_dim(values, 0, 1, axis=axis_pos)
    last_row = lax.slice_in_dim(values, count - 1, count, axis=axis_pos)
    extended = jnp.concatenate([first_row, first_row, values, last_row, last_row], axis=axis_pos)
    return (
        lax.slice_in_dim(extended, 4, 4 + count, axis=axis_pos)
        - 4.0 * lax.slice_in_dim(extended, 3, 3 + count, axis=axis_pos)
        + 6.0 * values
        - 4.0 * lax.slice_in_dim(extended, 1, 1 + count, axis=axis_pos)
        + lax.slice_in_dim(extended, 0, count, axis=axis_pos)
    )


def unit_normal(earlier, later):
    along_x = later[0] - earlier[0]
    along_y = 1.0 + later[1] - earlier[1]
    length = jnp.sqrt(along_x * along_x + along_y * along_y)
    return jnp.stack([along_x / length, along_y / length])


def wall_amplitude(shape_mode, angle, blade_mask):
    return (shape_mode[0] * jnp.cos(angle) - shape_mode[1] * jnp.sin(angle)) * blade_mask


def lag_shift(series, phase_now, phase_move):
    series_sum = jnp.zeros(series.shape[2:], jnp.float32)
    for number in range(series.shape[0]):
        harmonic = float(number + 1)
        change_cos = jnp.cos(harmonic * (phase_now + phase_move)) - jnp.cos(harmonic * phase_now)
        change_sin = jnp.sin(harmonic * (phase_now + phase_move)) - jnp.sin(harmonic * phase_now)
        series_sum = series_sum + series[number, 0] * change_cos - series[number, 1] * change_sin
    return series_sum


def metric_terms(offset_x, offset_y):
    x_zeta = 1.0 + (offset_x[2:, 1:-1] - offset_x[:-2, 1:-1]) * 0.5
    x_xi = (offset_x[1:-1, 2:] - offset_x[1:-1, :-2]) * 0.5
    y_xi = 1.0 + (offset_y[1:-1, 2:] - offset_y[1:-1, :-2]) * 0.5
    y_zeta = (offset_y[2:, 1:-1] - offset_y[:-2, 1:-1]) * 0.5
    return (x_zeta, x_xi, y_xi, y_zeta)


def geometry(grid_pad):
    x_zeta, x_xi, y_xi, y_zeta = metric_terms(grid_pad[0], grid_pad[1])
    old_zeta, old_xi, oldy_xi, oldy_zeta = metric_terms(
        grid_pad[0] - grid_pad[2], grid_pad[1] - grid_pad[3]
    )
    volume_new = (x_zeta * y_xi - x_xi * y_zeta)[1:-1, 1:-1]
    volume_old = (old_zeta * oldy_xi - old_xi * oldy_zeta)[1:-1, 1:-1]
    speed_x = grid_pad[2][1:-1, 1:-1] / TIME_STEP
    speed_y = grid_pad[3][1:-1, 1:-1] / TIME_STEP
    first_pitch = -y_zeta
    sweep_pitch = first_pitch * speed_x + x_zeta * speed_y
    second_axial = -x_xi
    sweep_axial = y_xi * speed_x + second_axial * speed_y
    return (
        (first_pitch, x_zeta, sweep_pitch, y_xi, second_axial, sweep_axial),
        volume_old,
        volume_new,
    )


def directional(strip_cells, first_coef, second_coef, sweep_term):
    density = strip_cells[0]
    vel_x = strip_cells[1] / density
    vel_y = strip_cells[2] / density
    energy = strip_cells[3]
    pressure = (HEAT_RATIO - 1.0) * (energy - 0.5 * density * (vel_x * vel_x + vel_y * vel_y))
    flux_x = jnp.stack(
        [
            strip_cells[1],
            strip_cells[1] * vel_x + pressure,
            strip_cells[1] * vel_y,
            (energy + pressure) * vel_x,
        ]
    )
    flux_y = jnp.stack(
        [
            strip_cells[2],
            strip_cells[2] * vel_x,
            strip_cells[2] * vel_y + pressure,
            (energy + pressure) * vel_y,
        ]
    )
    return first_coef * flux_x + second_coef * flux_y - sweep_term * strip_cells


def residual(padded, geo_terms):
    first_pitch, second_pitch, sweep_pitch, first_axial, second_axial, sweep_axial = geo_terms
    pitch_flux = directional(
        padded[:, 2:-2, 1:-1], first_pitch[1:-1], second_pitch[1:-1], sweep_pitch[1:-1]
    )
    axial_flux = directional(
        padded[:, 1:-1, 2:-2], first_axial[:, 1:-1], second_axial[:, 1:-1], sweep_axial[:, 1:-1]
    )
    divergence = (pitch_flux[:, :, 2:] - pitch_flux[:, :, :-2]) * 0.5 + (
        axial_flux[:, 2:] - axial_flux[:, :-2]
    ) * 0.5
    centre = padded[:, 2:-2, 2:-2]
    fourth = (
        padded[:, 2:-2, 4:]
        - 4.0 * padded[:, 2:-2, 3:-1]
        + 6.0 * centre
        - 4.0 * padded[:, 2:-2, 1:-3]
        + padded[:, 2:-2, :-4]
        + (
            padded[:, 4:, 2:-2]
            - 4.0 * padded[:, 3:-1, 2:-2]
            + 6.0 * centre
            - 4.0 * padded[:, 1:-3, 2:-2]
            + padded[:, :-4, 2:-2]
        )
    )
    return divergence + DAMPING * fourth + DAMPING * radial_damping(centre, 3)


def flow_ghosts(
    row_zero,
    row_one,
    row_last,
    row_before,
    wrap_low0,
    wrap_low1,
    wrap_high0,
    wrap_high1,
    blade_flag,
    corr_low,
    corr_high,
):
    sign_flip = jnp.array([1.0, 1.0, -1.0, 1.0], jnp.float32).reshape(
        (4,) + (1,) * (row_zero.ndim - 1)
    )
    ghost_m2 = jnp.where(blade_flag, row_one * sign_flip, wrap_low0 + corr_low)
    ghost_m1 = jnp.where(blade_flag, row_zero * sign_flip, wrap_low1 + corr_low)
    ghost_p0 = jnp.where(blade_flag, row_last * sign_flip, wrap_high0 + corr_high)
    ghost_p1 = jnp.where(blade_flag, row_before * sign_flip, wrap_high1 + corr_high)
    return (ghost_m2, ghost_m1, ghost_p0, ghost_p1)


def finish_flow(
    padded, depth, row_flag, corr_low, corr_high, low_end, high_end, first_end, last_end
):
    middle_rows = padded[:, 2:-2]
    width = middle_rows.shape[2]
    ghost_m2, ghost_m1, ghost_p0, ghost_p1 = flow_ghosts(
        middle_rows[:, :, 2],
        middle_rows[:, :, 3],
        middle_rows[:, :, width - 3],
        middle_rows[:, :, width - 4],
        middle_rows[:, :, 0],
        middle_rows[:, :, 1],
        middle_rows[:, :, width - 2],
        middle_rows[:, :, width - 1],
        row_flag[:, None],
        corr_low,
        corr_high,
    )
    low_pair = jnp.where(low_end, jnp.stack([ghost_m2, ghost_m1], 2), middle_rows[:, :, 0:2])
    high_pair = jnp.where(
        high_end, jnp.stack([ghost_p0, ghost_p1], 2), middle_rows[:, :, width - 2 :]
    )
    middle_rows = jnp.concatenate([low_pair, middle_rows[:, :, 2 : width - 2], high_pair], 2)
    whole = jnp.concatenate([padded[:, 0:2], middle_rows, padded[:, -2:]], 1)
    top_copy = jnp.repeat(whole[:, depth : depth + 1], depth, axis=1)
    bottom_copy = jnp.repeat(whole[:, -depth - 1 : -depth], depth, axis=1)
    top_rows = jnp.where(first_end, top_copy, whole[:, :depth])
    bottom_rows = jnp.where(last_end, bottom_copy, whole[:, -depth:])
    return jnp.concatenate([top_rows, whole[:, depth:-depth], bottom_rows], 1)


def _flux(rho, mx, my, en, first, second, sweep):
    inverse = 1.0 / rho
    u = mx * inverse
    v = my * inverse
    pr = (HEAT_RATIO - 1.0) * (en - 0.5 * rho * (u * u + v * v))
    ep = en + pr
    return (
        first * mx + second * my - sweep * rho,
        first * (mx * u + pr) + second * (my * u) - sweep * mx,
        first * (mx * v) + second * (my * v + pr) - sweep * my,
        first * (ep * u) + second * (ep * v) - sweep * en,
    )


def _radial_pairs(c0, lane, forward):
    width = c0.shape[-1]
    last = width - 1
    one_a = pltpu.roll(c0, 1, 1)
    one_b = pltpu.roll(c0, last, 1)
    two_a = pltpu.roll(c0, 2, 1)
    two_b = pltpu.roll(c0, width - 2, 1)
    m1 = jnp.where(lane == 0, c0, one_a)
    p1 = jnp.where(lane == last, c0, one_b)
    m2 = jnp.where(lane <= 1, m1, two_a)
    p2 = jnp.where(lane >= last - 1, p1, two_b)
    return m1 + p1, m2 + p2


def _volume(grid, a, npch, old):
    def comp(c, row, lo, hi):
        value = grid[c, row, lo:hi]
        if old:
            value = value - grid[c + 2, row, lo:hi]
        return value

    x_zeta = 1.0 + (comp(0, a + 3, 2, npch + 2) - comp(0, a + 1, 2, npch + 2)) * 0.5
    x_xi = (comp(0, a + 2, 3, npch + 3) - comp(0, a + 2, 1, npch + 1)) * 0.5
    y_xi = 1.0 + (comp(1, a + 2, 3, npch + 3) - comp(1, a + 2, 1, npch + 1)) * 0.5
    y_zeta = (comp(1, a + 3, 2, npch + 2) - comp(1, a + 1, 2, npch + 2)) * 0.5
    return x_zeta * y_xi - x_xi * y_zeta


def _section_body(scale, pad_hbm, grid_hbm, q0_hbm, out_hbm, af, pf, pad, grid, q0, out, sems):
    na = out.shape[1]
    npch = out.shape[2]
    width = out.shape[3]

    def row_copy(which, j):
        source, target = ((pad_hbm, pad), (grid_hbm, grid), (q0_hbm, q0), (out, out_hbm))[which]
        return pltpu.make_async_copy(
            source.at[:, pl.ds(j, 1)], target.at[:, pl.ds(j, 1)], sems.at[which, j]
        )

    for j in range(na + 4):
        row_copy(0, j).start()
        if 1 <= j <= na + 2:
            row_copy(1, j).start()
    for j in range(na):
        row_copy(2, j).start()

    def axial_row(j, carry):
        row_copy(0, j + 1).wait()
        row_copy(1, j + 1).wait()
        x_xi = (grid[0, j + 1, 3 : npch + 3] - grid[0, j + 1, 1 : npch + 1]) * 0.5
        y_xi = 1.0 + (grid[1, j + 1, 3 : npch + 3] - grid[1, j + 1, 1 : npch + 1]) * 0.5
        speed_x = grid[2, j + 1, 2 : npch + 2] / TIME_STEP
        speed_y = grid[3, j + 1, 2 : npch + 2] / TIME_STEP
        second = -x_xi
        sweep = y_xi * speed_x + second * speed_y
        q = [pad[k, j + 1, 2 : npch + 2] for k in range(4)]
        f = _flux(*q, y_xi, second, sweep)
        for k in range(4):
            af[k, j] = f[k]
        return carry

    lax.fori_loop(0, na + 2, axial_row, 0)
    lane = lax.broadcasted_iota(jnp.int32, (npch, width), 1)
    probe = pltpu.roll(lane, 1, 1)
    forward = probe == jnp.where(lane == 0, width - 1, lane - 1)

    row_copy(0, 0).wait()
    row_copy(0, na + 3).wait()

    def one_row(a, buffer):
        row_copy(2, a).wait()
        x_zeta = 1.0 + (grid[0, a + 3, 1 : npch + 3] - grid[0, a + 1, 1 : npch + 3]) * 0.5
        y_zeta = (grid[1, a + 3, 1 : npch + 3] - grid[1, a + 1, 1 : npch + 3]) * 0.5
        speed_x = grid[2, a + 2, 1 : npch + 3] / TIME_STEP
        speed_y = grid[3, a + 2, 1 : npch + 3] / TIME_STEP
        first = -y_zeta
        sweep = first * speed_x + x_zeta * speed_y
        q = [pad[k, a + 2, 1 : npch + 3] for k in range(4)]
        f = _flux(*q, first, x_zeta, sweep)
        for k in range(4):
            pf[buffer, k] = f[k]
        volume_old = _volume(grid, a, npch, True)
        inverse_new = 1.0 / _volume(grid, a, npch, False)
        for k in range(4):
            div = (pf[buffer, k, 2 : npch + 2] - pf[buffer, k, 0:npch]) * 0.5 + (
                af[k, a + 2] - af[k, a]
            ) * 0.5
            c0 = pad[k, a + 2, 2 : npch + 2]
            near_r, far_r = _radial_pairs(c0, lane, forward)
            near = (
                pad[k, a + 2, 3 : npch + 3]
                + pad[k, a + 2, 1 : npch + 1]
                + pad[k, a + 3, 2 : npch + 2]
                + pad[k, a + 1, 2 : npch + 2]
                + near_r
            )
            far = (
                pad[k, a + 2, 4 : npch + 4]
                + pad[k, a + 2, 0:npch]
                + pad[k, a + 4, 2 : npch + 2]
                + pad[k, a, 2 : npch + 2]
                + far_r
            )
            res = div + DAMPING * (far - 4.0 * near + 18.0 * c0)
            out[k, a] = (volume_old * q0[k, a] - scale * res) * inverse_new
        row_copy(3, a).start()

    def row_pair(pair, carry):
        one_row(2 * pair, 0)
        one_row(2 * pair + 1, 1)
        return carry

    lax.fori_loop(0, na // 2, row_pair, 0)
    if na % 2:
        one_row(na - 1, 0)
    for j in range(na):
        row_copy(3, j).wait()


def section_kernel(padded, grid_pad, start, scale, interpret=False):
    _, na, npch, width = start.shape
    body = lambda *refs: _section_body(scale, *refs)
    cells = na * npch * width
    return pl.pallas_call(
        body,
        out_shape=jax.ShapeDtypeStruct(start.shape, start.dtype),
        in_specs=[pl.BlockSpec(memory_space=pl.ANY)] * 3,
        out_specs=pl.BlockSpec(memory_space=pl.ANY),
        scratch_shapes=[
            pltpu.VMEM((4, na + 2, npch, width), jnp.float32),
            pltpu.VMEM((2, 4, npch + 2, width), jnp.float32),
            pltpu.VMEM(padded.shape, jnp.float32),
            pltpu.VMEM(grid_pad.shape, jnp.float32),
            pltpu.VMEM(start.shape, jnp.float32),
            pltpu.VMEM(start.shape, jnp.float32),
            pltpu.SemaphoreType.DMA((4, na + 4)),
        ],
        compiler_params=pltpu.CompilerParams(vmem_limit_bytes=60 * 1024 * 1024),
        cost_estimate=pl.CostEstimate(
            flops=500 * cells, transcendentals=0, bytes_accessed=4 * 14 * cells
        ),
        interpret=interpret,
    )(padded, grid_pad, start)


def per_device(flow_state, node_offset, blade_mode, phase_angles, lag_series):
    n_pitch = lax.axis_size("pitch")
    n_span = lax.axis_size("span")
    pitch_rows = flow_state.shape[2]
    axial_cols = flow_state.shape[1]
    total_pitch = pitch_rows * n_pitch
    total_axial = axial_cols * n_span
    pitch_at = lax.axis_index("pitch")
    span_at = lax.axis_index("span")
    lead_edge = total_axial // 4
    axial_index = span_at * axial_cols + jnp.arange(axial_cols, dtype=jnp.int32)
    blade_flag = (axial_index >= lead_edge) & (axial_index < total_axial - lead_edge)
    blade_mask = blade_flag.astype(jnp.float32)[:, None]
    phase_now = phase_angles[0]
    phase_lag = phase_angles[1]
    low_guess = wall_amplitude(blade_mode, phase_now, blade_mask) * unit_normal(
        node_offset[:, :, 0], node_offset[:, :, 1]
    )
    high_guess = wall_amplitude(blade_mode, phase_now + phase_lag, blade_mask) * unit_normal(
        node_offset[:, :, pitch_rows - 2], node_offset[:, :, pitch_rows - 1]
    )
    low_wall = low_guess
    high_wall = high_guess
    half = n_pitch // 2
    if n_pitch % 2:
        sent = jnp.where(pitch_at == 0, low_guess, high_guess)
        for shift in range(1, n_pitch):
            got = lax.ppermute(sent, "pitch", [(0, shift), (n_pitch - 1, shift - 1)])
            low_wall = jnp.where(pitch_at == shift, got, low_wall)
            high_wall = jnp.where(pitch_at == shift - 1, got, high_wall)
    else:
        known = 1
        while known < half:
            step = min(known, half - known)
            pairs = [(i, i + known) for i in range(step)]
            pairs += [(n_pitch - 1 - i, n_pitch - 1 - i - known) for i in range(step)]
            got = lax.ppermute(
                jnp.where(pitch_at < half, low_wall, high_wall), "pitch", pairs
            )
            takes_low = (pitch_at >= known) & (pitch_at < known + step)
            takes_high = (pitch_at <= n_pitch - 1 - known) & (pitch_at > n_pitch - 1 - known - step)
            low_wall = jnp.where(takes_low, got, low_wall)
            high_wall = jnp.where(takes_high, got, high_wall)
            known += step
        pairs = [(i, (i + half) % n_pitch) for i in range(n_pitch)]
        got = lax.ppermute(jnp.where(pitch_at < half, low_wall, high_wall), "pitch", pairs)
        low_wall = jnp.where(pitch_at >= half, got, low_wall)
        high_wall = jnp.where(pitch_at < half, got, high_wall)
    pitch_index = pitch_at * pitch_rows + jnp.arange(pitch_rows, dtype=jnp.int32)
    blend_row = (pitch_index.astype(jnp.float32) / (total_pitch - 1))[:, None]
    shift_field = (1.0 - blend_row) * low_wall[:, :, None, :] + blend_row * high_wall[:, :, None, :]
    moved_offset = node_offset + shift_field
    grid_field = jnp.concatenate([moved_offset, shift_field], 0)
    rim_width = 2
    grid_pad = padded_2(grid_field, (("pitch", 2), ("span", 1)), rim_width)
    first_pad = padded_cross(flow_state, rim_width)
    low_end = pitch_at == 0
    high_end = pitch_at == n_pitch - 1
    first_end = span_at == 0
    last_end = span_at == n_span - 1
    grid_pad = fill_ends(grid_pad, 1, rim_width, first_end, last_end)
    grid_pad = fill_ends(grid_pad, 2, 2, low_end, high_end)
    corr_low = lag_shift(lag_series[1], phase_now, -phase_lag)
    corr_high = lag_shift(lag_series[0], phase_now, phase_lag)
    padded = finish_flow(
        first_pad, 2, blade_flag, corr_low, corr_high, low_end, high_end, first_end, last_end
    )
    section_one = section_kernel(padded, grid_pad, flow_state, SECTION_WEIGHTS[0] * TIME_STEP)
    second_pad = padded_cross(section_one, 2)
    padded = finish_flow(
        second_pad, 2, blade_flag, corr_low, corr_high, low_end, high_end, first_end, last_end
    )
    current = section_kernel(padded, grid_pad, flow_state, SECTION_WEIGHTS[1] * TIME_STEP)
    return (current, moved_offset)


def solution(mesh):
    placed = (
        P(None, "span", "pitch", None),
        P(None, "span", "pitch", None),
        P(None, "span", None),
        P(),
        P(None, None, None, None, "span", None),
    )
    return jax.shard_map(
        per_device,
        mesh=mesh,
        in_specs=placed,
        out_specs=(P(None, "span", "pitch", None), P(None, "span", "pitch", None)),
        check_vma=False,
    )
```

```python
import jax
import jax.numpy as jnp
from jax import lax
from jax.sharding import PartitionSpec as P
from jax.experimental import pallas as pl
from jax.experimental.pallas import tpu as pltpu

HEAT_RATIO = 1.4
TIME_STEP = 0.25
DAMPING = 0.02
SECTION_WEIGHTS = (0.5, 1.0)


def broadcast(value, axis, root):
    mine = lax.axis_index(axis) == root
    return lax.psum(jnp.where(mine, value, jnp.zeros_like(value)), axis)


def padded_2(block, sides, width):
    for axis, dim in sides:
        count = lax.axis_size(axis)
        forward = [(i, i + 1) for i in range(count - 1)]
        forward.append((count - 1, 0))
        backward = [(target, source) for source, target in forward]
        low = lax.ppermute(
            lax.slice_in_dim(block, block.shape[dim] - width, None, axis=dim), axis, forward
        )
        high = lax.ppermute(lax.slice_in_dim(block, 0, width, axis=dim), axis, backward)
        block = jnp.concatenate([low, block, high], axis=dim)
    return block


def padded_cross(block, width):
    rims = []
    for axis, dim in (("pitch", 2), ("span", 1)):
        count = lax.axis_size(axis)
        forward = [(i, (i + 1) % count) for i in range(count)]
        backward = [(target, source) for source, target in forward]
        low = lax.ppermute(
            lax.slice_in_dim(block, block.shape[dim] - width, None, axis=dim), axis, forward
        )
        high = lax.ppermute(lax.slice_in_dim(block, 0, width, axis=dim), axis, backward)
        rims.append((low, high))
    (pitch_low, pitch_high), (span_low, span_high) = rims
    middle = jnp.concatenate([pitch_low, block, pitch_high], axis=2)
    corner = jnp.zeros(span_low.shape[:2] + (width,) + span_low.shape[3:], block.dtype)
    top = jnp.concatenate([corner, span_low, corner], axis=2)
    bottom = jnp.concatenate([corner, span_high, corner], axis=2)
    return jnp.concatenate([top, middle, bottom], axis=1)


def fill_ends(padded, axis_pos, depth, at_first, at_last):
    length = padded.shape[axis_pos]
    inner_first = lax.slice_in_dim(padded, depth, depth + 1, axis=axis_pos)
    inner_second = lax.slice_in_dim(padded, depth + 1, depth + 2, axis=axis_pos)
    inner_last = lax.slice_in_dim(padded, length - depth - 1, length - depth, axis=axis_pos)
    inner_before = lax.slice_in_dim(padded, length - depth - 2, length - depth - 1, axis=axis_pos)
    step_low = inner_first - inner_second
    step_high = inner_last - inner_before
    low_side = jnp.concatenate(
        [inner_first + float(count) * step_low for count in range(depth, 0, -1)], axis=axis_pos
    )
    high_side = jnp.concatenate(
        [inner_last + float(count) * step_high for count in range(1, depth + 1)], axis=axis_pos
    )
    low_side = jnp.where(at_first, low_side, lax.slice_in_dim(padded, 0, depth, axis=axis_pos))
    high_side = jnp.where(
        at_last, high_side, lax.slice_in_dim(padded, length - depth, length, axis=axis_pos)
    )
    return jnp.concatenate(
        [low_side, lax.slice_in_dim(padded, depth, length - depth, axis=axis_pos), high_side],
        axis=axis_pos,
    )


def radial_damping(values, axis_pos):
    count = values.shape[axis_pos]
    first_row = lax.slice_in_dim(values, 0, 1, axis=axis_pos)
    last_row = lax.slice_in_dim(values, count - 1, count, axis=axis_pos)
    extended = jnp.concatenate([first_row, first_row, values, last_row, last_row], axis=axis_pos)
    return (
        lax.slice_in_dim(extended, 4, 4 + count, axis=axis_pos)
        - 4.0 * lax.slice_in_dim(extended, 3, 3 + count, axis=axis_pos)
        + 6.0 * values
        - 4.0 * lax.slice_in_dim(extended, 1, 1 + count, axis=axis_pos)
        + lax.slice_in_dim(extended, 0, count, axis=axis_pos)
    )


def unit_normal(earlier, later):
    along_x = later[0] - earlier[0]
    along_y = 1.0 + later[1] - earlier[1]
    length = jnp.sqrt(along_x * along_x + along_y * along_y)
    return jnp.stack([along_x / length, along_y / length])


def wall_amplitude(shape_mode, angle, blade_mask):
    return (shape_mode[0] * jnp.cos(angle) - shape_mode[1] * jnp.sin(angle)) * blade_mask


def lag_shift(series, phase_now, phase_move):
    series_sum = jnp.zeros(series.shape[2:], jnp.float32)
    for number in range(series.shape[0]):
        harmonic = float(number + 1)
        change_cos = jnp.cos(harmonic * (phase_now + phase_move)) - jnp.cos(harmonic * phase_now)
        change_sin = jnp.sin(harmonic * (phase_now + phase_move)) - jnp.sin(harmonic * phase_now)
        series_sum = series_sum + series[number, 0] * change_cos - series[number, 1] * change_sin
    return series_sum


def metric_terms(offset_x, offset_y):
    x_zeta = 1.0 + (offset_x[2:, 1:-1] - offset_x[:-2, 1:-1]) * 0.5
    x_xi = (offset_x[1:-1, 2:] - offset_x[1:-1, :-2]) * 0.5
    y_xi = 1.0 + (offset_y[1:-1, 2:] - offset_y[1:-1, :-2]) * 0.5
    y_zeta = (offset_y[2:, 1:-1] - offset_y[:-2, 1:-1]) * 0.5
    return (x_zeta, x_xi, y_xi, y_zeta)


def geometry(grid_pad):
    x_zeta, x_xi, y_xi, y_zeta = metric_terms(grid_pad[0], grid_pad[1])
    old_zeta, old_xi, oldy_xi, oldy_zeta = metric_terms(
        grid_pad[0] - grid_pad[2], grid_pad[1] - grid_pad[3]
    )
    volume_new = (x_zeta * y_xi - x_xi * y_zeta)[1:-1, 1:-1]
    volume_old = (old_zeta * oldy_xi - old_xi * oldy_zeta)[1:-1, 1:-1]
    speed_x = grid_pad[2][1:-1, 1:-1] / TIME_STEP
    speed_y = grid_pad[3][1:-1, 1:-1] / TIME_STEP
    first_pitch = -y_zeta
    sweep_pitch = first_pitch * speed_x + x_zeta * speed_y
    second_axial = -x_xi
    sweep_axial = y_xi * speed_x + second_axial * speed_y
    return (
        (first_pitch, x_zeta, sweep_pitch, y_xi, second_axial, sweep_axial),
        volume_old,
        volume_new,
    )


def directional(strip_cells, first_coef, second_coef, sweep_term):
    density = strip_cells[0]
    vel_x = strip_cells[1] / density
    vel_y = strip_cells[2] / density
    energy = strip_cells[3]
    pressure = (HEAT_RATIO - 1.0) * (energy - 0.5 * density * (vel_x * vel_x + vel_y * vel_y))
    flux_x = jnp.stack(
        [
            strip_cells[1],
            strip_cells[1] * vel_x + pressure,
            strip_cells[1] * vel_y,
            (energy + pressure) * vel_x,
        ]
    )
    flux_y = jnp.stack(
        [
            strip_cells[2],
            strip_cells[2] * vel_x,
            strip_cells[2] * vel_y + pressure,
            (energy + pressure) * vel_y,
        ]
    )
    return first_coef * flux_x + second_coef * flux_y - sweep_term * strip_cells


def residual(padded, geo_terms):
    first_pitch, second_pitch, sweep_pitch, first_axial, second_axial, sweep_axial = geo_terms
    pitch_flux = directional(
        padded[:, 2:-2, 1:-1], first_pitch[1:-1], second_pitch[1:-1], sweep_pitch[1:-1]
    )
    axial_flux = directional(
        padded[:, 1:-1, 2:-2], first_axial[:, 1:-1], second_axial[:, 1:-1], sweep_axial[:, 1:-1]
    )
    divergence = (pitch_flux[:, :, 2:] - pitch_flux[:, :, :-2]) * 0.5 + (
        axial_flux[:, 2:] - axial_flux[:, :-2]
    ) * 0.5
    centre = padded[:, 2:-2, 2:-2]
    fourth = (
        padded[:, 2:-2, 4:]
        - 4.0 * padded[:, 2:-2, 3:-1]
        + 6.0 * centre
        - 4.0 * padded[:, 2:-2, 1:-3]
        + padded[:, 2:-2, :-4]
        + (
            padded[:, 4:, 2:-2]
            - 4.0 * padded[:, 3:-1, 2:-2]
            + 6.0 * centre
            - 4.0 * padded[:, 1:-3, 2:-2]
            + padded[:, :-4, 2:-2]
        )
    )
    return divergence + DAMPING * fourth + DAMPING * radial_damping(centre, 3)


def flow_ghosts(
    row_zero,
    row_one,
    row_last,
    row_before,
    wrap_low0,
    wrap_low1,
    wrap_high0,
    wrap_high1,
    blade_flag,
    corr_low,
    corr_high,
):
    sign_flip = jnp.array([1.0, 1.0, -1.0, 1.0], jnp.float32).reshape(
        (4,) + (1,) * (row_zero.ndim - 1)
    )
    ghost_m2 = jnp.where(blade_flag, row_one * sign_flip, wrap_low0 + corr_low)
    ghost_m1 = jnp.where(blade_flag, row_zero * sign_flip, wrap_low1 + corr_low)
    ghost_p0 = jnp.where(blade_flag, row_last * sign_flip, wrap_high0 + corr_high)
    ghost_p1 = jnp.where(blade_flag, row_before * sign_flip, wrap_high1 + corr_high)
    return (ghost_m2, ghost_m1, ghost_p0, ghost_p1)


def finish_flow(
    padded, depth, row_flag, corr_low, corr_high, low_end, high_end, first_end, last_end
):
    middle_rows = padded[:, 2:-2]
    width = middle_rows.shape[2]
    ghost_m2, ghost_m1, ghost_p0, ghost_p1 = flow_ghosts(
        middle_rows[:, :, 2],
        middle_rows[:, :, 3],
        middle_rows[:, :, width - 3],
        middle_rows[:, :, width - 4],
        middle_rows[:, :, 0],
        middle_rows[:, :, 1],
        middle_rows[:, :, width - 2],
        middle_rows[:, :, width - 1],
        row_flag[:, None],
        corr_low,
        corr_high,
    )
    low_pair = jnp.where(low_end, jnp.stack([ghost_m2, ghost_m1], 2), middle_rows[:, :, 0:2])
    high_pair = jnp.where(
        high_end, jnp.stack([ghost_p0, ghost_p1], 2), middle_rows[:, :, width - 2 :]
    )
    middle_rows = jnp.concatenate([low_pair, middle_rows[:, :, 2 : width - 2], high_pair], 2)
    whole = jnp.concatenate([padded[:, 0:2], middle_rows, padded[:, -2:]], 1)
    top_copy = jnp.repeat(whole[:, depth : depth + 1], depth, axis=1)
    bottom_copy = jnp.repeat(whole[:, -depth - 1 : -depth], depth, axis=1)
    top_rows = jnp.where(first_end, top_copy, whole[:, :depth])
    bottom_rows = jnp.where(last_end, bottom_copy, whole[:, -depth:])
    return jnp.concatenate([top_rows, whole[:, depth:-depth], bottom_rows], 1)


def _flux(rho, mx, my, en, first, second, sweep):
    inverse = 1.0 / rho
    u = mx * inverse
    v = my * inverse
    pr = (HEAT_RATIO - 1.0) * (en - 0.5 * rho * (u * u + v * v))
    ep = en + pr
    return (
        first * mx + second * my - sweep * rho,
        first * (mx * u + pr) + second * (my * u) - sweep * mx,
        first * (mx * v) + second * (my * v + pr) - sweep * my,
        first * (ep * u) + second * (ep * v) - sweep * en,
    )


def _radial_pairs(c0, lane, forward):
    width = c0.shape[-1]
    last = width - 1
    one_a = pltpu.roll(c0, 1, 1)
    one_b = pltpu.roll(c0, last, 1)
    two_a = pltpu.roll(c0, 2, 1)
    two_b = pltpu.roll(c0, width - 2, 1)
    m1 = jnp.where(lane == 0, c0, one_a)
    p1 = jnp.where(lane == last, c0, one_b)
    m2 = jnp.where(lane <= 1, m1, two_a)
    p2 = jnp.where(lane >= last - 1, p1, two_b)
    return m1 + p1, m2 + p2


def _volume(grid, a, npch, old):
    def comp(c, row, lo, hi):
        value = grid[c, row, lo:hi]
        if old:
            value = value - grid[c + 2, row, lo:hi]
        return value

    x_zeta = 1.0 + (comp(0, a + 3, 2, npch + 2) - comp(0, a + 1, 2, npch + 2)) * 0.5
    x_xi = (comp(0, a + 2, 3, npch + 3) - comp(0, a + 2, 1, npch + 1)) * 0.5
    y_xi = 1.0 + (comp(1, a + 2, 3, npch + 3) - comp(1, a + 2, 1, npch + 1)) * 0.5
    y_zeta = (comp(1, a + 3, 2, npch + 2) - comp(1, a + 1, 2, npch + 2)) * 0.5
    return x_zeta * y_xi - x_xi * y_zeta


def _section_body(scale, pad_hbm, grid_hbm, q0_hbm, out_hbm, af, pf, pad, grid, q0, out, sems):
    na = out.shape[1]
    npch = out.shape[2]
    width = out.shape[3]

    def row_copy(which, j):
        source, target = ((pad_hbm, pad), (grid_hbm, grid), (q0_hbm, q0), (out, out_hbm))[which]
        return pltpu.make_async_copy(
            source.at[:, pl.ds(j, 1)], target.at[:, pl.ds(j, 1)], sems.at[which, j]
        )

    for j in range(na + 4):
        row_copy(0, j).start()
        if 1 <= j <= na + 2:
            row_copy(1, j).start()
    for j in range(na):
        row_copy(2, j).start()

    def axial_row(j, carry):
        row_copy(0, j + 1).wait()
        row_copy(1, j + 1).wait()
        x_xi = (grid[0, j + 1, 3 : npch + 3] - grid[0, j + 1, 1 : npch + 1]) * 0.5
        y_xi = 1.0 + (grid[1, j + 1, 3 : npch + 3] - grid[1, j + 1, 1 : npch + 1]) * 0.5
        speed_x = grid[2, j + 1, 2 : npch + 2] / TIME_STEP
        speed_y = grid[3, j + 1, 2 : npch + 2] / TIME_STEP
        second = -x_xi
        sweep = y_xi * speed_x + second * speed_y
        q = [pad[k, j + 1, 2 : npch + 2] for k in range(4)]
        f = _flux(*q, y_xi, second, sweep)
        for k in range(4):
            af[k, j] = f[k]
        return carry

    lax.fori_loop(0, na + 2, axial_row, 0)
    lane = lax.broadcasted_iota(jnp.int32, (npch, width), 1)
    probe = pltpu.roll(lane, 1, 1)
    forward = probe == jnp.where(lane == 0, width - 1, lane - 1)

    row_copy(0, 0).wait()
    row_copy(0, na + 3).wait()

    def one_row(a, buffer):
        row_copy(2, a).wait()
        x_zeta = 1.0 + (grid[0, a + 3, 1 : npch + 3] - grid[0, a + 1, 1 : npch + 3]) * 0.5
        y_zeta = (grid[1, a + 3, 1 : npch + 3] - grid[1, a + 1, 1 : npch + 3]) * 0.5
        speed_x = grid[2, a + 2, 1 : npch + 3] / TIME_STEP
        speed_y = grid[3, a + 2, 1 : npch + 3] / TIME_STEP
        first = -y_zeta
        sweep = first * speed_x + x_zeta * speed_y
        q = [pad[k, a + 2, 1 : npch + 3] for k in range(4)]
        f = _flux(*q, first, x_zeta, sweep)
        for k in range(4):
            pf[buffer, k] = f[k]
        volume_old = _volume(grid, a, npch, True)
        inverse_new = 1.0 / _volume(grid, a, npch, False)
        for k in range(4):
            spread = (pf[buffer, k, 2 : npch + 2] - pf[buffer, k, 0:npch]) + (
                af[k, a + 2] - af[k, a]
            )
            c0 = pad[k, a + 2, 2 : npch + 2]
            near_r, far_r = _radial_pairs(c0, lane, forward)
            near = (
                pad[k, a + 2, 3 : npch + 3]
                + pad[k, a + 2, 1 : npch + 1]
                + pad[k, a + 3, 2 : npch + 2]
                + pad[k, a + 1, 2 : npch + 2]
                + near_r
            )
            far = (
                pad[k, a + 2, 4 : npch + 4]
                + pad[k, a + 2, 0:npch]
                + pad[k, a + 4, 2 : npch + 2]
                + pad[k, a, 2 : npch + 2]
                + far_r
            )
            res = (0.5 * scale) * spread + (DAMPING * scale) * (far - 4.0 * near + 18.0 * c0)
            out[k, a] = (volume_old * q0[k, a] - res) * inverse_new
        row_copy(3, a).start()

    def row_pair(pair, carry):
        one_row(2 * pair, 0)
        one_row(2 * pair + 1, 1)
        return carry

    lax.fori_loop(0, na // 2, row_pair, 0)
    if na % 2:
        one_row(na - 1, 0)
    for j in range(na):
        row_copy(3, j).wait()


def section_kernel(padded, grid_pad, start, scale, interpret=False):
    _, na, npch, width = start.shape
    body = lambda *refs: _section_body(scale, *refs)
    cells = na * npch * width
    return pl.pallas_call(
        body,
        out_shape=jax.ShapeDtypeStruct(start.shape, start.dtype),
        in_specs=[pl.BlockSpec(memory_space=pl.ANY)] * 3,
        out_specs=pl.BlockSpec(memory_space=pl.ANY),
        scratch_shapes=[
            pltpu.VMEM((4, na + 2, npch, width), jnp.float32),
            pltpu.VMEM((2, 4, npch + 2, width), jnp.float32),
            pltpu.VMEM(padded.shape, jnp.float32),
            pltpu.VMEM(grid_pad.shape, jnp.float32),
            pltpu.VMEM(start.shape, jnp.float32),
            pltpu.VMEM(start.shape, jnp.float32),
            pltpu.SemaphoreType.DMA((4, na + 4)),
        ],
        compiler_params=pltpu.CompilerParams(vmem_limit_bytes=60 * 1024 * 1024),
        cost_estimate=pl.CostEstimate(
            flops=500 * cells, transcendentals=0, bytes_accessed=4 * 14 * cells
        ),
        interpret=interpret,
    )(padded, grid_pad, start)


def per_device(flow_state, node_offset, blade_mode, phase_angles, lag_series):
    n_pitch = lax.axis_size("pitch")
    n_span = lax.axis_size("span")
    pitch_rows = flow_state.shape[2]
    axial_cols = flow_state.shape[1]
    total_pitch = pitch_rows * n_pitch
    total_axial = axial_cols * n_span
    pitch_at = lax.axis_index("pitch")
    span_at = lax.axis_index("span")
    lead_edge = total_axial // 4
    axial_index = span_at * axial_cols + jnp.arange(axial_cols, dtype=jnp.int32)
    blade_flag = (axial_index >= lead_edge) & (axial_index < total_axial - lead_edge)
    blade_mask = blade_flag.astype(jnp.float32)[:, None]
    phase_now = phase_angles[0]
    phase_lag = phase_angles[1]
    low_guess = wall_amplitude(blade_mode, phase_now, blade_mask) * unit_normal(
        node_offset[:, :, 0], node_offset[:, :, 1]
    )
    high_guess = wall_amplitude(blade_mode, phase_now + phase_lag, blade_mask) * unit_normal(
        node_offset[:, :, pitch_rows - 2], node_offset[:, :, pitch_rows - 1]
    )
    low_wall = low_guess
    high_wall = high_guess
    half = n_pitch // 2
    if n_pitch % 2:
        sent = jnp.where(pitch_at == 0, low_guess, high_guess)
        for shift in range(1, n_pitch):
            got = lax.ppermute(sent, "pitch", [(0, shift), (n_pitch - 1, shift - 1)])
            low_wall = jnp.where(pitch_at == shift, got, low_wall)
            high_wall = jnp.where(pitch_at == shift - 1, got, high_wall)
    else:
        known = 1
        while known < half:
            step = min(known, half - known)
            pairs = [(i, i + known) for i in range(step)]
            pairs += [(n_pitch - 1 - i, n_pitch - 1 - i - known) for i in range(step)]
            got = lax.ppermute(
                jnp.where(pitch_at < half, low_wall, high_wall), "pitch", pairs
            )
            takes_low = (pitch_at >= known) & (pitch_at < known + step)
            takes_high = (pitch_at <= n_pitch - 1 - known) & (pitch_at > n_pitch - 1 - known - step)
            low_wall = jnp.where(takes_low, got, low_wall)
            high_wall = jnp.where(takes_high, got, high_wall)
            known += step
        pairs = [(i, (i + half) % n_pitch) for i in range(n_pitch)]
        got = lax.ppermute(jnp.where(pitch_at < half, low_wall, high_wall), "pitch", pairs)
        low_wall = jnp.where(pitch_at >= half, got, low_wall)
        high_wall = jnp.where(pitch_at < half, got, high_wall)
    pitch_index = pitch_at * pitch_rows + jnp.arange(pitch_rows, dtype=jnp.int32)
    blend_row = (pitch_index.astype(jnp.float32) / (total_pitch - 1))[:, None]
    shift_field = (1.0 - blend_row) * low_wall[:, :, None, :] + blend_row * high_wall[:, :, None, :]
    moved_offset = node_offset + shift_field
    grid_field = jnp.concatenate([moved_offset, shift_field], 0)
    rim_width = 2
    grid_pad = padded_2(grid_field, (("pitch", 2), ("span", 1)), rim_width)
    first_pad = padded_cross(flow_state, rim_width)
    low_end = pitch_at == 0
    high_end = pitch_at == n_pitch - 1
    first_end = span_at == 0
    last_end = span_at == n_span - 1
    grid_pad = fill_ends(grid_pad, 1, rim_width, first_end, last_end)
    grid_pad = fill_ends(grid_pad, 2, 2, low_end, high_end)
    corr_low = lag_shift(lag_series[1], phase_now, -phase_lag)
    corr_high = lag_shift(lag_series[0], phase_now, phase_lag)
    padded = finish_flow(
        first_pad, 2, blade_flag, corr_low, corr_high, low_end, high_end, first_end, last_end
    )
    section_one = section_kernel(padded, grid_pad, flow_state, SECTION_WEIGHTS[0] * TIME_STEP)
    second_pad = padded_cross(section_one, 2)
    padded = finish_flow(
        second_pad, 2, blade_flag, corr_low, corr_high, low_end, high_end, first_end, last_end
    )
    current = section_kernel(padded, grid_pad, flow_state, SECTION_WEIGHTS[1] * TIME_STEP)
    return (current, moved_offset)


def solution(mesh):
    placed = (
        P(None, "span", "pitch", None),
        P(None, "span", "pitch", None),
        P(None, "span", None),
        P(),
        P(None, None, None, None, "span", None),
    )
    return jax.shard_map(
        per_device,
        mesh=mesh,
        in_specs=placed,
        out_specs=(P(None, "span", "pitch", None), P(None, "span", "pitch", None)),
        check_vma=False,
    )
```

```python
import jax
import jax.numpy as jnp
from jax import lax
from jax.sharding import PartitionSpec as P
from jax.experimental import pallas as pl
from jax.experimental.pallas import tpu as pltpu

HEAT_RATIO = 1.4
TIME_STEP = 0.25
DAMPING = 0.02
SECTION_WEIGHTS = (0.5, 1.0)


def broadcast(value, axis, root):
    mine = lax.axis_index(axis) == root
    return lax.psum(jnp.where(mine, value, jnp.zeros_like(value)), axis)


def padded_2(block, sides, width):
    for axis, dim in sides:
        count = lax.axis_size(axis)
        forward = [(i, i + 1) for i in range(count - 1)]
        forward.append((count - 1, 0))
        backward = [(target, source) for source, target in forward]
        low = lax.ppermute(
            lax.slice_in_dim(block, block.shape[dim] - width, None, axis=dim), axis, forward
        )
        high = lax.ppermute(lax.slice_in_dim(block, 0, width, axis=dim), axis, backward)
        block = jnp.concatenate([low, block, high], axis=dim)
    return block


def padded_cross(block, width):
    rims = []
    for axis, dim in (("pitch", 2), ("span", 1)):
        count = lax.axis_size(axis)
        forward = [(i, (i + 1) % count) for i in range(count)]
        backward = [(target, source) for source, target in forward]
        low = lax.ppermute(
            lax.slice_in_dim(block, block.shape[dim] - width, None, axis=dim), axis, forward
        )
        high = lax.ppermute(lax.slice_in_dim(block, 0, width, axis=dim), axis, backward)
        rims.append((low, high))
    (pitch_low, pitch_high), (span_low, span_high) = rims
    middle = jnp.concatenate([pitch_low, block, pitch_high], axis=2)
    corner = jnp.zeros(span_low.shape[:2] + (width,) + span_low.shape[3:], block.dtype)
    top = jnp.concatenate([corner, span_low, corner], axis=2)
    bottom = jnp.concatenate([corner, span_high, corner], axis=2)
    return jnp.concatenate([top, middle, bottom], axis=1)


def fill_ends(padded, axis_pos, depth, at_first, at_last):
    length = padded.shape[axis_pos]
    inner_first = lax.slice_in_dim(padded, depth, depth + 1, axis=axis_pos)
    inner_second = lax.slice_in_dim(padded, depth + 1, depth + 2, axis=axis_pos)
    inner_last = lax.slice_in_dim(padded, length - depth - 1, length - depth, axis=axis_pos)
    inner_before = lax.slice_in_dim(padded, length - depth - 2, length - depth - 1, axis=axis_pos)
    step_low = inner_first - inner_second
    step_high = inner_last - inner_before
    low_side = jnp.concatenate(
        [inner_first + float(count) * step_low for count in range(depth, 0, -1)], axis=axis_pos
    )
    high_side = jnp.concatenate(
        [inner_last + float(count) * step_high for count in range(1, depth + 1)], axis=axis_pos
    )
    low_side = jnp.where(at_first, low_side, lax.slice_in_dim(padded, 0, depth, axis=axis_pos))
    high_side = jnp.where(
        at_last, high_side, lax.slice_in_dim(padded, length - depth, length, axis=axis_pos)
    )
    return jnp.concatenate(
        [low_side, lax.slice_in_dim(padded, depth, length - depth, axis=axis_pos), high_side],
        axis=axis_pos,
    )


def radial_damping(values, axis_pos):
    count = values.shape[axis_pos]
    first_row = lax.slice_in_dim(values, 0, 1, axis=axis_pos)
    last_row = lax.slice_in_dim(values, count - 1, count, axis=axis_pos)
    extended = jnp.concatenate([first_row, first_row, values, last_row, last_row], axis=axis_pos)
    return (
        lax.slice_in_dim(extended, 4, 4 + count, axis=axis_pos)
        - 4.0 * lax.slice_in_dim(extended, 3, 3 + count, axis=axis_pos)
        + 6.0 * values
        - 4.0 * lax.slice_in_dim(extended, 1, 1 + count, axis=axis_pos)
        + lax.slice_in_dim(extended, 0, count, axis=axis_pos)
    )


def unit_normal(earlier, later):
    along_x = later[0] - earlier[0]
    along_y = 1.0 + later[1] - earlier[1]
    length = jnp.sqrt(along_x * along_x + along_y * along_y)
    return jnp.stack([along_x / length, along_y / length])


def wall_amplitude(shape_mode, angle, blade_mask):
    return (shape_mode[0] * jnp.cos(angle) - shape_mode[1] * jnp.sin(angle)) * blade_mask


def lag_shift(series, phase_now, phase_move):
    series_sum = jnp.zeros(series.shape[2:], jnp.float32)
    for number in range(series.shape[0]):
        harmonic = float(number + 1)
        change_cos = jnp.cos(harmonic * (phase_now + phase_move)) - jnp.cos(harmonic * phase_now)
        change_sin = jnp.sin(harmonic * (phase_now + phase_move)) - jnp.sin(harmonic * phase_now)
        series_sum = series_sum + series[number, 0] * change_cos - series[number, 1] * change_sin
    return series_sum


def metric_terms(offset_x, offset_y):
    x_zeta = 1.0 + (offset_x[2:, 1:-1] - offset_x[:-2, 1:-1]) * 0.5
    x_xi = (offset_x[1:-1, 2:] - offset_x[1:-1, :-2]) * 0.5
    y_xi = 1.0 + (offset_y[1:-1, 2:] - offset_y[1:-1, :-2]) * 0.5
    y_zeta = (offset_y[2:, 1:-1] - offset_y[:-2, 1:-1]) * 0.5
    return (x_zeta, x_xi, y_xi, y_zeta)


def geometry(grid_pad):
    x_zeta, x_xi, y_xi, y_zeta = metric_terms(grid_pad[0], grid_pad[1])
    old_zeta, old_xi, oldy_xi, oldy_zeta = metric_terms(
        grid_pad[0] - grid_pad[2], grid_pad[1] - grid_pad[3]
    )
    volume_new = (x_zeta * y_xi - x_xi * y_zeta)[1:-1, 1:-1]
    volume_old = (old_zeta * oldy_xi - old_xi * oldy_zeta)[1:-1, 1:-1]
    speed_x = grid_pad[2][1:-1, 1:-1] / TIME_STEP
    speed_y = grid_pad[3][1:-1, 1:-1] / TIME_STEP
    first_pitch = -y_zeta
    sweep_pitch = first_pitch * speed_x + x_zeta * speed_y
    second_axial = -x_xi
    sweep_axial = y_xi * speed_x + second_axial * speed_y
    return (
        (first_pitch, x_zeta, sweep_pitch, y_xi, second_axial, sweep_axial),
        volume_old,
        volume_new,
    )


def directional(strip_cells, first_coef, second_coef, sweep_term):
    density = strip_cells[0]
    vel_x = strip_cells[1] / density
    vel_y = strip_cells[2] / density
    energy = strip_cells[3]
    pressure = (HEAT_RATIO - 1.0) * (energy - 0.5 * density * (vel_x * vel_x + vel_y * vel_y))
    flux_x = jnp.stack(
        [
            strip_cells[1],
            strip_cells[1] * vel_x + pressure,
            strip_cells[1] * vel_y,
            (energy + pressure) * vel_x,
        ]
    )
    flux_y = jnp.stack(
        [
            strip_cells[2],
            strip_cells[2] * vel_x,
            strip_cells[2] * vel_y + pressure,
            (energy + pressure) * vel_y,
        ]
    )
    return first_coef * flux_x + second_coef * flux_y - sweep_term * strip_cells


def residual(padded, geo_terms):
    first_pitch, second_pitch, sweep_pitch, first_axial, second_axial, sweep_axial = geo_terms
    pitch_flux = directional(
        padded[:, 2:-2, 1:-1], first_pitch[1:-1], second_pitch[1:-1], sweep_pitch[1:-1]
    )
    axial_flux = directional(
        padded[:, 1:-1, 2:-2], first_axial[:, 1:-1], second_axial[:, 1:-1], sweep_axial[:, 1:-1]
    )
    divergence = (pitch_flux[:, :, 2:] - pitch_flux[:, :, :-2]) * 0.5 + (
        axial_flux[:, 2:] - axial_flux[:, :-2]
    ) * 0.5
    centre = padded[:, 2:-2, 2:-2]
    fourth = (
        padded[:, 2:-2, 4:]
        - 4.0 * padded[:, 2:-2, 3:-1]
        + 6.0 * centre
        - 4.0 * padded[:, 2:-2, 1:-3]
        + padded[:, 2:-2, :-4]
        + (
            padded[:, 4:, 2:-2]
            - 4.0 * padded[:, 3:-1, 2:-2]
            + 6.0 * centre
            - 4.0 * padded[:, 1:-3, 2:-2]
            + padded[:, :-4, 2:-2]
        )
    )
    return divergence + DAMPING * fourth + DAMPING * radial_damping(centre, 3)


def flow_ghosts(
    row_zero,
    row_one,
    row_last,
    row_before,
    wrap_low0,
    wrap_low1,
    wrap_high0,
    wrap_high1,
    blade_flag,
    corr_low,
    corr_high,
):
    sign_flip = jnp.array([1.0, 1.0, -1.0, 1.0], jnp.float32).reshape(
        (4,) + (1,) * (row_zero.ndim - 1)
    )
    ghost_m2 = jnp.where(blade_flag, row_one * sign_flip, wrap_low0 + corr_low)
    ghost_m1 = jnp.where(blade_flag, row_zero * sign_flip, wrap_low1 + corr_low)
    ghost_p0 = jnp.where(blade_flag, row_last * sign_flip, wrap_high0 + corr_high)
    ghost_p1 = jnp.where(blade_flag, row_before * sign_flip, wrap_high1 + corr_high)
    return (ghost_m2, ghost_m1, ghost_p0, ghost_p1)


def finish_flow(
    padded, depth, row_flag, corr_low, corr_high, low_end, high_end, first_end, last_end
):
    middle_rows = padded[:, 2:-2]
    width = middle_rows.shape[2]
    ghost_m2, ghost_m1, ghost_p0, ghost_p1 = flow_ghosts(
        middle_rows[:, :, 2],
        middle_rows[:, :, 3],
        middle_rows[:, :, width - 3],
        middle_rows[:, :, width - 4],
        middle_rows[:, :, 0],
        middle_rows[:, :, 1],
        middle_rows[:, :, width - 2],
        middle_rows[:, :, width - 1],
        row_flag[:, None],
        corr_low,
        corr_high,
    )
    low_pair = jnp.where(low_end, jnp.stack([ghost_m2, ghost_m1], 2), middle_rows[:, :, 0:2])
    high_pair = jnp.where(
        high_end, jnp.stack([ghost_p0, ghost_p1], 2), middle_rows[:, :, width - 2 :]
    )
    middle_rows = jnp.concatenate([low_pair, middle_rows[:, :, 2 : width - 2], high_pair], 2)
    whole = jnp.concatenate([padded[:, 0:2], middle_rows, padded[:, -2:]], 1)
    top_copy = jnp.repeat(whole[:, depth : depth + 1], depth, axis=1)
    bottom_copy = jnp.repeat(whole[:, -depth - 1 : -depth], depth, axis=1)
    top_rows = jnp.where(first_end, top_copy, whole[:, :depth])
    bottom_rows = jnp.where(last_end, bottom_copy, whole[:, -depth:])
    return jnp.concatenate([top_rows, whole[:, depth:-depth], bottom_rows], 1)


def _flux(rho, mx, my, en, first, second, sweep):
    inverse = 1.0 / rho
    u = mx * inverse
    v = my * inverse
    mxu = mx * u
    myv = my * v
    pr = (HEAT_RATIO - 1.0) * (en - 0.5 * (mxu + myv))
    ep = en + pr
    return (
        first * mx + second * my - sweep * rho,
        first * (mxu + pr) + second * (my * u) - sweep * mx,
        first * (mx * v) + second * (myv + pr) - sweep * my,
        first * (ep * u) + second * (ep * v) - sweep * en,
    )


def _radial_pairs(c0, lane, forward):
    width = c0.shape[-1]
    last = width - 1
    one_a = pltpu.roll(c0, 1, 1)
    one_b = pltpu.roll(c0, last, 1)
    two_a = pltpu.roll(c0, 2, 1)
    two_b = pltpu.roll(c0, width - 2, 1)
    m1 = jnp.where(lane == 0, c0, one_a)
    p1 = jnp.where(lane == last, c0, one_b)
    m2 = jnp.where(lane <= 1, m1, two_a)
    p2 = jnp.where(lane >= last - 1, p1, two_b)
    return m1 + p1, m2 + p2


def _volume(grid, a, npch, old):
    def comp(c, row, lo, hi):
        value = grid[c, row, lo:hi]
        if old:
            value = value - grid[c + 2, row, lo:hi]
        return value

    x_zeta = 1.0 + (comp(0, a + 3, 2, npch + 2) - comp(0, a + 1, 2, npch + 2)) * 0.5
    x_xi = (comp(0, a + 2, 3, npch + 3) - comp(0, a + 2, 1, npch + 1)) * 0.5
    y_xi = 1.0 + (comp(1, a + 2, 3, npch + 3) - comp(1, a + 2, 1, npch + 1)) * 0.5
    y_zeta = (comp(1, a + 3, 2, npch + 2) - comp(1, a + 1, 2, npch + 2)) * 0.5
    return x_zeta * y_xi - x_xi * y_zeta


def _section_body(scale, pad_hbm, grid_hbm, q0_hbm, out_hbm, af, pf, pad, grid, q0, out, sems):
    na = out.shape[1]
    npch = out.shape[2]
    width = out.shape[3]

    def row_copy(which, j):
        source, target = ((pad_hbm, pad), (grid_hbm, grid), (q0_hbm, q0), (out, out_hbm))[which]
        return pltpu.make_async_copy(
            source.at[:, pl.ds(j, 1)], target.at[:, pl.ds(j, 1)], sems.at[which, j]
        )

    for j in range(na + 4):
        row_copy(0, j).start()
        if 1 <= j <= na + 2:
            row_copy(1, j).start()
    for j in range(na):
        row_copy(2, j).start()

    def axial_row(j, carry):
        row_copy(0, j + 1).wait()
        row_copy(1, j + 1).wait()
        x_xi = (grid[0, j + 1, 3 : npch + 3] - grid[0, j + 1, 1 : npch + 1]) * 0.5
        y_xi = 1.0 + (grid[1, j + 1, 3 : npch + 3] - grid[1, j + 1, 1 : npch + 1]) * 0.5
        speed_x = grid[2, j + 1, 2 : npch + 2] / TIME_STEP
        speed_y = grid[3, j + 1, 2 : npch + 2] / TIME_STEP
        second = -x_xi
        sweep = y_xi * speed_x + second * speed_y
        q = [pad[k, j + 1, 2 : npch + 2] for k in range(4)]
        f = _flux(*q, y_xi, second, sweep)
        for k in range(4):
            af[k, j] = f[k]
        return carry

    lax.fori_loop(0, na + 2, axial_row, 0)
    lane = lax.broadcasted_iota(jnp.int32, (npch, width), 1)
    probe = pltpu.roll(lane, 1, 1)
    forward = probe == jnp.where(lane == 0, width - 1, lane - 1)

    row_copy(0, 0).wait()
    row_copy(0, na + 3).wait()

    def one_row(a, buffer):
        row_copy(2, a).wait()
        x_zeta = 1.0 + (grid[0, a + 3, 1 : npch + 3] - grid[0, a + 1, 1 : npch + 3]) * 0.5
        y_zeta = (grid[1, a + 3, 1 : npch + 3] - grid[1, a + 1, 1 : npch + 3]) * 0.5
        speed_x = grid[2, a + 2, 1 : npch + 3] / TIME_STEP
        speed_y = grid[3, a + 2, 1 : npch + 3] / TIME_STEP
        first = -y_zeta
        sweep = first * speed_x + x_zeta * speed_y
        q = [pad[k, a + 2, 1 : npch + 3] for k in range(4)]
        f = _flux(*q, first, x_zeta, sweep)
        for k in range(4):
            pf[buffer, k] = f[k]
        volume_old = _volume(grid, a, npch, True)
        inverse_new = 1.0 / _volume(grid, a, npch, False)
        for k in range(4):
            spread = (pf[buffer, k, 2 : npch + 2] - pf[buffer, k, 0:npch]) + (
                af[k, a + 2] - af[k, a]
            )
            c0 = pad[k, a + 2, 2 : npch + 2]
            near_r, far_r = _radial_pairs(c0, lane, forward)
            near = (
                pad[k, a + 2, 3 : npch + 3]
                + pad[k, a + 2, 1 : npch + 1]
                + pad[k, a + 3, 2 : npch + 2]
                + pad[k, a + 1, 2 : npch + 2]
                + near_r
            )
            far = (
                pad[k, a + 2, 4 : npch + 4]
                + pad[k, a + 2, 0:npch]
                + pad[k, a + 4, 2 : npch + 2]
                + pad[k, a, 2 : npch + 2]
                + far_r
            )
            res = (0.5 * scale) * spread + (DAMPING * scale) * (far - 4.0 * near + 18.0 * c0)
            out[k, a] = (volume_old * q0[k, a] - res) * inverse_new
        row_copy(3, a).start()

    def row_pair(pair, carry):
        one_row(2 * pair, 0)
        one_row(2 * pair + 1, 1)
        return carry

    lax.fori_loop(0, na // 2, row_pair, 0)
    if na % 2:
        one_row(na - 1, 0)
    for j in range(na):
        row_copy(3, j).wait()


def section_kernel(padded, grid_pad, start, scale, interpret=False):
    _, na, npch, width = start.shape
    body = lambda *refs: _section_body(scale, *refs)
    cells = na * npch * width
    return pl.pallas_call(
        body,
        out_shape=jax.ShapeDtypeStruct(start.shape, start.dtype),
        in_specs=[pl.BlockSpec(memory_space=pl.ANY)] * 3,
        out_specs=pl.BlockSpec(memory_space=pl.ANY),
        scratch_shapes=[
            pltpu.VMEM((4, na + 2, npch, width), jnp.float32),
            pltpu.VMEM((2, 4, npch + 2, width), jnp.float32),
            pltpu.VMEM(padded.shape, jnp.float32),
            pltpu.VMEM(grid_pad.shape, jnp.float32),
            pltpu.VMEM(start.shape, jnp.float32),
            pltpu.VMEM(start.shape, jnp.float32),
            pltpu.SemaphoreType.DMA((4, na + 4)),
        ],
        compiler_params=pltpu.CompilerParams(vmem_limit_bytes=60 * 1024 * 1024),
        cost_estimate=pl.CostEstimate(
            flops=500 * cells, transcendentals=0, bytes_accessed=4 * 14 * cells
        ),
        interpret=interpret,
    )(padded, grid_pad, start)


def per_device(flow_state, node_offset, blade_mode, phase_angles, lag_series):
    n_pitch = lax.axis_size("pitch")
    n_span = lax.axis_size("span")
    pitch_rows = flow_state.shape[2]
    axial_cols = flow_state.shape[1]
    total_pitch = pitch_rows * n_pitch
    total_axial = axial_cols * n_span
    pitch_at = lax.axis_index("pitch")
    span_at = lax.axis_index("span")
    lead_edge = total_axial // 4
    axial_index = span_at * axial_cols + jnp.arange(axial_cols, dtype=jnp.int32)
    blade_flag = (axial_index >= lead_edge) & (axial_index < total_axial - lead_edge)
    blade_mask = blade_flag.astype(jnp.float32)[:, None]
    phase_now = phase_angles[0]
    phase_lag = phase_angles[1]
    low_guess = wall_amplitude(blade_mode, phase_now, blade_mask) * unit_normal(
        node_offset[:, :, 0], node_offset[:, :, 1]
    )
    high_guess = wall_amplitude(blade_mode, phase_now + phase_lag, blade_mask) * unit_normal(
        node_offset[:, :, pitch_rows - 2], node_offset[:, :, pitch_rows - 1]
    )
    low_wall = low_guess
    high_wall = high_guess
    half = n_pitch // 2
    if n_pitch % 2:
        sent = jnp.where(pitch_at == 0, low_guess, high_guess)
        for shift in range(1, n_pitch):
            got = lax.ppermute(sent, "pitch", [(0, shift), (n_pitch - 1, shift - 1)])
            low_wall = jnp.where(pitch_at == shift, got, low_wall)
            high_wall = jnp.where(pitch_at == shift - 1, got, high_wall)
    else:
        known = 1
        while known < half:
            step = min(known, half - known)
            pairs = [(i, i + known) for i in range(step)]
            pairs += [(n_pitch - 1 - i, n_pitch - 1 - i - known) for i in range(step)]
            got = lax.ppermute(
                jnp.where(pitch_at < half, low_wall, high_wall), "pitch", pairs
            )
            takes_low = (pitch_at >= known) & (pitch_at < known + step)
            takes_high = (pitch_at <= n_pitch - 1 - known) & (pitch_at > n_pitch - 1 - known - step)
            low_wall = jnp.where(takes_low, got, low_wall)
            high_wall = jnp.where(takes_high, got, high_wall)
            known += step
        pairs = [(i, (i + half) % n_pitch) for i in range(n_pitch)]
        got = lax.ppermute(jnp.where(pitch_at < half, low_wall, high_wall), "pitch", pairs)
        low_wall = jnp.where(pitch_at >= half, got, low_wall)
        high_wall = jnp.where(pitch_at < half, got, high_wall)
    pitch_index = pitch_at * pitch_rows + jnp.arange(pitch_rows, dtype=jnp.int32)
    blend_row = (pitch_index.astype(jnp.float32) / (total_pitch - 1))[:, None]
    shift_field = (1.0 - blend_row) * low_wall[:, :, None, :] + blend_row * high_wall[:, :, None, :]
    moved_offset = node_offset + shift_field
    grid_field = jnp.concatenate([moved_offset, shift_field], 0)
    rim_width = 2
    grid_pad = padded_2(grid_field, (("pitch", 2), ("span", 1)), rim_width)
    first_pad = padded_cross(flow_state, rim_width)
    low_end = pitch_at == 0
    high_end = pitch_at == n_pitch - 1
    first_end = span_at == 0
    last_end = span_at == n_span - 1
    grid_pad = fill_ends(grid_pad, 1, rim_width, first_end, last_end)
    grid_pad = fill_ends(grid_pad, 2, 2, low_end, high_end)
    corr_low = lag_shift(lag_series[1], phase_now, -phase_lag)
    corr_high = lag_shift(lag_series[0], phase_now, phase_lag)
    padded = finish_flow(
        first_pad, 2, blade_flag, corr_low, corr_high, low_end, high_end, first_end, last_end
    )
    section_one = section_kernel(padded, grid_pad, flow_state, SECTION_WEIGHTS[0] * TIME_STEP)
    second_pad = padded_cross(section_one, 2)
    padded = finish_flow(
        second_pad, 2, blade_flag, corr_low, corr_high, low_end, high_end, first_end, last_end
    )
    current = section_kernel(padded, grid_pad, flow_state, SECTION_WEIGHTS[1] * TIME_STEP)
    return (current, moved_offset)


def solution(mesh):
    placed = (
        P(None, "span", "pitch", None),
        P(None, "span", "pitch", None),
        P(None, "span", None),
        P(),
        P(None, None, None, None, "span", None),
    )
    return jax.shard_map(
        per_device,
        mesh=mesh,
        in_specs=placed,
        out_specs=(P(None, "span", "pitch", None), P(None, "span", "pitch", None)),
        check_vma=False,
    )
```
